256 devices in a mesh: gx: 16 (over x, y), gy: 16 (over z, core).
Axes of the slice: x: 4, y: 4, z: 8, core: 2. Of those that a mesh axis runs over, the one named last changes fastest.
Arguments:
- inv_factors: float32 [64, 64, 4096], P('gx', 'gy'), as said below
- couplings: float32 [64, 64, 2, 4096], P('gx', 'gy'), may hold values from -1.5 to 1.5
- stencil: int32 [64, 64, 2], P('gx', 'gy'), may hold values from 0 to 1
- coarse: int32 [64, 64], P('gx', 'gy'), may hold values from 0 to 1, as said below
Outputs:
- strength: float32 [64, 64, 2], P('gx', 'gy')
- restriction: bfloat16 [3072, 14, 4096], P(('gx', 'gy'))
The draws below stay inside these ranges and needn't reach their ends.
Inputs may be any that keep to these rules, and one draw needn't show every extreme that they name: Each block of inv_factors is lower triangular with diagonal entries between 0.5 and 1. Each tile of 4 x 4 elements has at most 12 coarse elements, and some tile has exactly 12.
All inputs are finite; a program needn't handle non-finite values.
Results may differ from the reference program's by a relative error of at most 0.001.
Values sent between devices are 32-bit elements; how exact they have to be, the bound alone decides.
No kernel may reach another device: no remote copies, remote signals or barrier semaphores. Data moves between devices by JAX's collectives and lax.ppermute only.
A program may use at most 64 MiB of HBM per device.

```python
import math
import jax
import jax.numpy as jnp
from jax import lax

B = 64
EX = 4
EY = 4
CAP = 12
NX = 64
NY = 64
N_GX = 16
N_GY = 16


def draw_inv_factors(key, part):
    key_diagonal, key_off = jax.random.split(key)
    full_shape = (NX, NY, B, B)
    diagonal = jnp.exp(jax.random.uniform(key_diagonal, (NX, NY, B), jnp.float32, -0.6931, 0.0))
    diagonal = jnp.clip(diagonal, 0.5, 1.0)
    off_part = jax.random.uniform(key_off, full_shape, jnp.float32, -1.0, 1.0) * (0.6 / B ** 0.5)
    identity = jnp.eye(B, dtype=jnp.float32)
    lower = jnp.tril(jnp.ones((B, B), jnp.float32), -1)
    blocks = off_part * lower + diagonal[:, :, :, None] * identity
    return blocks.reshape(NX, NY, B * B)


def draw_coarse(key, part):
    tiles_x = NX // EX
    tiles_y = NY // EY
    tile_count = tiles_x * tiles_y
    cell_count = EX * EY
    key_heavy, key_forced, key_light, key_scores = jax.random.split(key, 4)
    heavy_tile = jax.random.randint(key_heavy, (tile_count,), 0, 8) == 0
    forced = jax.random.randint(key_forced, (), 0, tile_count)
    light_count = jax.random.randint(key_light, (tile_count,), cell_count // 8, 3 * cell_count // 8 + 1)
    counts = jnp.where(heavy_tile | (jnp.arange(tile_count) == forced), CAP, light_count)
    scores = jax.random.randint(key_scores, (tile_count, cell_count), 0, 2 ** 20) * cell_count + jnp.arange(cell_count)[None, :]
    slot_rank = jnp.argsort(jnp.argsort(scores, axis=1, stable=True), axis=1, stable=True)
    coarse_flags = (slot_rank < counts[:, None]).astype(jnp.int32)
    return coarse_flags.reshape(tiles_x, tiles_y, EX, EY).transpose(0, 2, 1, 3).reshape(NX, NY)


def touch_ends(values, own_key, least, top_value):
    longest = values.shape.index(max(values.shape))
    spots = []
    for shift in (0, 1):
        where = [jax.random.randint(jax.random.fold_in(own_key, axis), (), 0, length) for axis, length in enumerate(values.shape)]
        where[longest] = (where[longest] + shift) % values.shape[longest]
        spots.append(tuple(where))
    return values.at[spots[0]].set(least).at[spots[1]].set(top_value)


def block_scale(stream_key, shape, cuts, least, largest):
    loudness, own = 1.0, jax.random.fold_in(stream_key, 6)
    for dim, blocks in cuts:
        draws = jnp.exp(jax.random.uniform(jax.random.fold_in(own, dim), (blocks,), jnp.float32, least / len(cuts), largest / len(cuts)))
        loudness = loudness * jnp.repeat(draws, shape[dim] // blocks).reshape([-1 if axis == dim else 1 for axis in range(len(shape))])
    return loudness


def gaussian(own_key, dims, scale, limit, shards=(), kind=jnp.bfloat16):
    values = scale * jax.random.normal(own_key, dims, jnp.float32)
    if shards:
        values = values * block_scale(own_key, dims, shards, -0.22, 0.18)
    return jnp.clip(values, -limit, limit).astype(kind)


def setup_inputs(seed: int = 0) -> dict:
    keys = jax.random.split(jax.random.key(seed), 5)
    return {
        "inv_factors": draw_inv_factors(jax.random.fold_in(keys[4], 71), 0),
        "couplings": gaussian(keys[1], (NX, NY, 2, B * B), 0.25, 1.5, ((0, 16), (1, 16)), jnp.float32),
        "stencil": touch_ends(jax.random.randint(keys[2], (NX, NY, 2), 0, 2), jax.random.fold_in(keys[2], 1), 0, 1).astype(jnp.int32),
        "coarse": draw_coarse(jax.random.fold_in(keys[4], 71), 0),
    }


def unfold(blocks):
    block_order = math.isqrt(blocks.shape[-1])
    return blocks.reshape(blocks.shape[:-1] + (block_order, block_order))

def fold(matrices):
    return matrices.reshape(matrices.shape[:-2] + (matrices.shape[-2] * matrices.shape[-1],))

def product(left_block, right_block):
    return fold(jnp.einsum('...ij,...jk->...ik', unfold(left_block), unfold(right_block), precision=lax.Precision.HIGHEST))

def transposed(blocks):
    return fold(jnp.swapaxes(unfold(blocks), -1, -2))

def crop_cycle(values, margin):
    return values[margin:values.shape[0] - margin, margin:values.shape[1] - margin]

def upwind_pick(values, upwind_side):
    trailing = (1,) * (values.ndim - 2)
    sign_x = upwind_side[:, :, 0].reshape(upwind_side.shape[:2] + trailing)
    sign_y = upwind_side[:, :, 1].reshape(upwind_side.shape[:2] + trailing)
    upwind_x = jnp.where(sign_x == 1, values[2:, 1:-1], values[:-2, 1:-1])
    upwind_y = jnp.where(sign_y == 1, values[1:-1, 2:], values[1:-1, :-2])
    return (upwind_x, upwind_y)

def near_paths(fine_inverse, coupling, upwind_side):
    upwind_x, upwind_y = upwind_pick(fine_inverse, crop_cycle(upwind_side, 1))
    middle = crop_cycle(fine_inverse, 1)
    local_coupling = crop_cycle(coupling, 1)
    step_x = product(-local_coupling[:, :, 0], upwind_x)
    step_y = product(-local_coupling[:, :, 1], upwind_y)
    return jnp.stack([middle, product(middle, step_x), product(middle, step_y)], axis=2)

def far_paths(fine_inverse, coupling, upwind_side, near):
    upwind_x, upwind_y = upwind_pick(near, crop_cycle(upwind_side, 2))
    middle = crop_cycle(fine_inverse, 2)
    local_coupling = crop_cycle(coupling, 2)
    lead_x = product(middle, -local_coupling[:, :, 0])[:, :, None]
    lead_y = product(middle, -local_coupling[:, :, 1])[:, :, None]
    return jnp.concatenate([middle[:, :, None], product(lead_x, upwind_x), product(lead_y, upwind_y)], axis=2)

def strength_of(factor_cycle, coupling, upwind_side):
    upwind_x, upwind_y = upwind_pick(factor_cycle, upwind_side)
    own_block = crop_cycle(factor_cycle, 1)
    result = []
    for direction, upwind_factor in ((0, upwind_x), (1, upwind_y)):
        scaled = product(product(own_block, coupling[:, :, direction]), transposed(upwind_factor))
        result.append(lax.optimization_barrier(jnp.mean(scaled * scaled, axis=-1)))
    return jnp.stack(result, axis=-1)

def restriction_rows(paths_cycle, coupling, upwind_side, coarse, capacity):
    upwind_x, upwind_y = upwind_pick(paths_cycle, upwind_side)
    cell_count = coarse.shape[0] * coarse.shape[1]
    flat_coarse = coarse.reshape(cell_count).astype(jnp.int32)
    slot_rank = jnp.cumsum(flat_coarse, dtype=jnp.int32) - flat_coarse
    chosen = ((slot_rank[None, :] == jnp.arange(capacity, dtype=jnp.int32)[:, None]) & (flat_coarse[None, :] == 1)).astype(jnp.int32)
    source = lax.optimization_barrier(jnp.sum(chosen * jnp.arange(cell_count, dtype=jnp.int32)[None, :], axis=1, dtype=jnp.int32))
    filled = lax.optimization_barrier(jnp.sum(chosen, axis=1, dtype=jnp.int32))
    rows_x = jnp.take(upwind_x.reshape((cell_count,) + upwind_x.shape[2:]), source, axis=0)
    rows_y = jnp.take(upwind_y.reshape((cell_count,) + upwind_y.shape[2:]), source, axis=0)
    coupling_rows = jnp.take(coupling.reshape((cell_count,) + coupling.shape[2:]), source, axis=0)
    restrict = jnp.concatenate([product(-coupling_rows[:, 0:1], rows_x), product(-coupling_rows[:, 1:2], rows_y)], axis=1)
    return (restrict * filled[:, None, None].astype(restrict.dtype)).astype(jnp.bfloat16)

def reference(inv_factors, couplings, stencil, coarse):
    cycle_depth = 3
    float_type = inv_factors.dtype
    pad_spec = ((cycle_depth, cycle_depth), (cycle_depth, cycle_depth))
    padded_factor = jnp.pad(inv_factors, pad_spec + ((0, 0),))
    padded_coupling = jnp.pad(couplings, pad_spec + ((0, 0), (0, 0)))
    padded_stencil = jnp.pad(stencil, pad_spec + ((0, 0),))
    padded_coarse = jnp.pad(coarse, pad_spec)
    identity_flat = jnp.eye(B, dtype=float_type).reshape(B * B)
    span_x = EX + 2 * cycle_depth
    span_y = EY + 2 * cycle_depth

    def one_tile(tile_index):
        start_x = (tile_index // N_GY * EX).astype(jnp.int32)
        start_y = (tile_index % N_GY * EY).astype(jnp.int32)
        zero_index = jnp.zeros((), jnp.int32)
        factor_inverse = lax.dynamic_slice(padded_factor, (start_x, start_y, zero_index), (span_x, span_y, B * B))
        coupling = lax.dynamic_slice(padded_coupling, (start_x, start_y, zero_index, zero_index), (span_x, span_y, 2, B * B))
        upwind_side = lax.dynamic_slice(padded_stencil, (start_x, start_y, zero_index), (span_x, span_y, 2))
        coarse_cycle = lax.dynamic_slice(padded_coarse, (start_x, start_y), (span_x, span_y))
        coord_x = start_x - cycle_depth + jnp.arange(span_x, dtype=jnp.int32)
        coord_y = start_y - cycle_depth + jnp.arange(span_y, dtype=jnp.int32)
        inside = ((coord_x >= 0) & (coord_x < NX))[:, None] & ((coord_y >= 0) & (coord_y < NY))[None, :]
        factor_inverse = jnp.where(inside[:, :, None], factor_inverse, identity_flat)
        target_x = coord_x[:, None] + 2 * upwind_side[:, :, 0] - 1
        target_y = coord_y[None, :] + 2 * upwind_side[:, :, 1] - 1
        reach = jnp.stack([(target_x >= 0) & (target_x < NX), (target_y >= 0) & (target_y < NY)], axis=-1)
        coupling = coupling * reach[:, :, :, None].astype(float_type)
        fine_inverse = (1 - coarse_cycle).astype(float_type)[:, :, None] * product(transposed(factor_inverse), factor_inverse)
        near = near_paths(fine_inverse, coupling, upwind_side)
        far = far_paths(fine_inverse, coupling, upwind_side, near)
        own_side = crop_cycle(upwind_side, cycle_depth)
        own_coupling = crop_cycle(coupling, cycle_depth)
        own_coarse = crop_cycle(coarse_cycle, cycle_depth)
        strong = strength_of(crop_cycle(factor_inverse, cycle_depth - 1), own_coupling, own_side)
        restrict = restriction_rows(far, own_coupling, own_side, own_coarse, CAP)
        return (strong, restrict)
    strong, restrict = lax.map(one_tile, jnp.arange(N_GX * N_GY, dtype=jnp.int32))
    strength = strong.reshape(N_GX, N_GY, EX, EY, 2).transpose(0, 2, 1, 3, 4).reshape(NX, NY, 2)
    return (strength, restrict.reshape(N_GX * N_GY * CAP, 14, B * B))
```

```python
import math

import jax
import jax.numpy as jnp
from jax import lax
from jax.sharding import PartitionSpec as P

CAP = 12


def extended(cells, sides, width):
    for axis, dim in sides:
        count = lax.axis_size(axis)
        ends = count - 1
        head = lax.slice_in_dim(cells, 0, width, axis=dim)
        tail = lax.slice_in_dim(cells, cells.shape[dim] - width, cells.shape[dim], axis=dim)
        cells = jnp.concatenate(
            [
                lax.ppermute(tail, axis, [(i, (i + 1) % count) for i in range(ends)]),
                cells,
                lax.ppermute(head, axis, [((i + 1) % count, i) for i in range(ends)]),
            ],
            axis=dim,
        )
    return cells


def matmul(left_block, right_block):
    return jnp.einsum(
        "...ij,...jk->...ik", left_block, right_block, precision=lax.Precision.HIGH
    )


def left_gram(left_block, right_block):
    return jnp.einsum(
        "...ji,...jk->...ik", left_block, right_block, precision=lax.Precision.HIGH
    )


def right_gram(left_block, right_block):
    return jnp.einsum(
        "...ij,...kj->...ik", left_block, right_block, precision=lax.Precision.HIGH
    )


def crop_cycle(values, margin):
    return values[margin : values.shape[0] - margin, margin : values.shape[1] - margin]


def upwind_pick(values, upwind_side):
    trailing = (1,) * (values.ndim - 2)
    sign_x = upwind_side[:, :, 0].reshape(upwind_side.shape[:2] + trailing)
    sign_y = upwind_side[:, :, 1].reshape(upwind_side.shape[:2] + trailing)
    upwind_x = jnp.where(sign_x == 1, values[2:, 1:-1], values[:-2, 1:-1])
    upwind_y = jnp.where(sign_y == 1, values[1:-1, 2:], values[1:-1, :-2])
    return (upwind_x, upwind_y)


def near_paths(fine_inverse, minus_coupling, upwind_side):
    upwind_x, upwind_y = upwind_pick(fine_inverse, crop_cycle(upwind_side, 1))
    middle = crop_cycle(fine_inverse, 1)
    local_coupling = crop_cycle(minus_coupling, 1)
    step_x = matmul(local_coupling[:, :, 0], upwind_x)
    step_y = matmul(local_coupling[:, :, 1], upwind_y)
    return jnp.stack([middle, matmul(middle, step_x), matmul(middle, step_y)], axis=2)


def far_paths(fine_inverse, minus_coupling, upwind_side, near):
    upwind_x, upwind_y = upwind_pick(near, crop_cycle(upwind_side, 2))
    middle = crop_cycle(fine_inverse, 2)
    local_coupling = crop_cycle(minus_coupling, 2)
    lead_x = matmul(middle, local_coupling[:, :, 0])[:, :, None]
    lead_y = matmul(middle, local_coupling[:, :, 1])[:, :, None]
    return jnp.concatenate(
        [middle[:, :, None], matmul(lead_x, upwind_x), matmul(lead_y, upwind_y)], axis=2
    )


def strength_of(factor_cycle, minus_coupling, upwind_side):
    upwind_x, upwind_y = upwind_pick(factor_cycle, upwind_side)
    own_block = crop_cycle(factor_cycle, 1)
    result = []
    for direction, upwind_factor in ((0, upwind_x), (1, upwind_y)):
        scaled = right_gram(matmul(own_block, minus_coupling[:, :, direction]), upwind_factor)
        result.append(jnp.mean(scaled * scaled, axis=(-2, -1)))
    return jnp.stack(result, axis=-1)


def restriction_rows(paths_cycle, minus_coupling, upwind_side, coarse, capacity):
    upwind_x, upwind_y = upwind_pick(paths_cycle, upwind_side)
    cell_count = coarse.shape[0] * coarse.shape[1]
    flat_coarse = coarse.reshape(cell_count)
    slot_rank = jnp.cumsum(flat_coarse, dtype=jnp.int32) - flat_coarse
    chosen = (
        (slot_rank[None, :] == jnp.arange(capacity, dtype=jnp.int32)[:, None])
        & (flat_coarse[None, :] == 1)
    ).astype(jnp.int32)
    source = jnp.sum(
        chosen * jnp.arange(cell_count, dtype=jnp.int32)[None, :], axis=1, dtype=jnp.int32
    )
    filled = jnp.sum(chosen, axis=1, dtype=jnp.int32)
    rows_x = jnp.take(upwind_x.reshape((cell_count,) + upwind_x.shape[2:]), source, axis=0)
    rows_y = jnp.take(upwind_y.reshape((cell_count,) + upwind_y.shape[2:]), source, axis=0)
    coupling_rows = jnp.take(
        minus_coupling.reshape((cell_count,) + minus_coupling.shape[2:]), source, axis=0
    )
    restrict = jnp.concatenate(
        [matmul(coupling_rows[:, 0:1], rows_x), matmul(coupling_rows[:, 1:2], rows_y)], axis=1
    )
    restrict = (restrict * filled[:, None, None, None].astype(restrict.dtype)).astype(jnp.bfloat16)
    return restrict.reshape(restrict.shape[:2] + (restrict.shape[2] * restrict.shape[3],))


def on_device(inv_factors, couplings, stencil, coarse):
    rows_x, rows_y, flat_size = inv_factors.shape
    order = math.isqrt(flat_size)
    total_x = rows_x * lax.axis_size("gx")
    total_y = rows_y * lax.axis_size("gy")
    coord_x = lax.axis_index("gx") * rows_x + jnp.arange(rows_x, dtype=jnp.int32)
    coord_y = lax.axis_index("gy") * rows_y + jnp.arange(rows_y, dtype=jnp.int32)
    target_x = coord_x[:, None] + 2 * stencil[:, :, 0] - 1
    target_y = coord_y[None, :] + 2 * stencil[:, :, 1] - 1
    reach = jnp.stack(
        [(target_x >= 0) & (target_x < total_x), (target_y >= 0) & (target_y < total_y)], axis=-1
    )
    signed_mask = -reach.astype(jnp.float32)
    minus_own = (couplings * signed_mask[:, :, :, None]).reshape(rows_x, rows_y, 2, order, order)
    factor_own = inv_factors.reshape(rows_x, rows_y, order, order)
    stencil_codes = stencil[:, :, 0] + 2 * stencil[:, :, 1] + 4 * coarse
    cycle_depth = 2
    fine_own = (1 - coarse).astype(jnp.float32)[:, :, None, None] * left_gram(
        factor_own, factor_own
    )
    packed = jnp.concatenate([factor_own[:, :, None], fine_own[:, :, None], minus_own], axis=2)
    cycle_blocks = extended(packed, (("gx", 0), ("gy", 1)), cycle_depth)
    code_cycle = extended(stencil_codes, (("gx", 0), ("gy", 1)), cycle_depth)
    upwind_side = jnp.stack([code_cycle % 2, code_cycle // 2 % 2], axis=-1)
    factor_cycle = cycle_blocks[:, :, 0]
    fine_inverse = cycle_blocks[:, :, 1]
    coupling_cycle = cycle_blocks[:, :, 2:4]
    near = near_paths(fine_inverse, coupling_cycle, upwind_side)
    far = far_paths(fine_inverse, coupling_cycle, upwind_side, near)
    paths_cycle = extended(far, (("gx", 0), ("gy", 1)), 1)
    strong = strength_of(crop_cycle(factor_cycle, cycle_depth - 1), minus_own, stencil)
    restrict = restriction_rows(paths_cycle, minus_own, stencil, coarse, CAP)
    return (strong, restrict)


def solution(mesh):
    placed = (P("gx", "gy", None), P("gx", "gy", None, None), P("gx", "gy", None), P("gx", "gy"))
    return jax.shard_map(
        on_device,
        mesh=mesh,
        in_specs=placed,
        out_specs=(P("gx", "gy", None), P(("gx", "gy"), None, None)),
        check_vma=False,
    )
```

```python
import math

import jax
import jax.numpy as jnp
from jax import lax
from jax.sharding import PartitionSpec as P

CAP = 12
PREC = lax.Precision.HIGH


def matmul(left_block, right_block):
    return jnp.einsum("...ij,...jk->...ik", left_block, right_block, precision=PREC)


def left_gram(left_block, right_block):
    return jnp.einsum("...ji,...jk->...ik", left_block, right_block, precision=PREC)


def right_gram(left_block, right_block):
    return jnp.einsum("...ij,...kj->...ik", left_block, right_block, precision=PREC)


def crop_cycle(values, margin):
    return values[margin : values.shape[0] - margin, margin : values.shape[1] - margin]


def upwind_pick(values, upwind_side):
    trailing = (1,) * (values.ndim - 2)
    sign_x = upwind_side[:, :, 0].reshape(upwind_side.shape[:2] + trailing)
    sign_y = upwind_side[:, :, 1].reshape(upwind_side.shape[:2] + trailing)
    upwind_x = jnp.where(sign_x == 1, values[2:, 1:-1], values[:-2, 1:-1])
    upwind_y = jnp.where(sign_y == 1, values[1:-1, 2:], values[1:-1, :-2])
    return (upwind_x, upwind_y)


def shift_pairs(count, step):
    return [(i, i + step) for i in range(count) if 0 <= i + step < count]


def corner_pairs(n_x, n_y, step_x, step_y):
    pairs = []
    for a in range(n_x):
        for b in range(n_y):
            if 0 <= a + step_x < n_x and 0 <= b + step_y < n_y:
                pairs.append((a * n_y + b, (a + step_x) * n_y + (b + step_y)))
    return pairs


def code_row(codes, flat):
    values = codes.reshape(1, -1).astype(jnp.float32)
    return jnp.pad(values, ((0, 0), (0, flat - values.shape[1])))


def face_buffer(fine, lead, factor, side, rows, cols):
    flat = fine.shape[-1]
    parts = [
        fine[rows[3], cols[3]].reshape(-1, flat),
        lead[rows[2], cols[2]].reshape(-1, flat),
        factor[rows[1], cols[1]].reshape(-1, flat),
        code_row(side[rows[2], cols[2]], flat),
    ]
    return jnp.concatenate(parts, axis=0)


def on_device(inv_factors, couplings, stencil, coarse):
    nx, ny, flat = inv_factors.shape
    order = math.isqrt(flat)
    n_gx = lax.axis_size("gx")
    n_gy = lax.axis_size("gy")
    total_x = nx * n_gx
    total_y = ny * n_gy
    coord_x = lax.axis_index("gx") * nx + jnp.arange(nx, dtype=jnp.int32)
    coord_y = lax.axis_index("gy") * ny + jnp.arange(ny, dtype=jnp.int32)
    target_x = coord_x[:, None] + 2 * stencil[:, :, 0] - 1
    target_y = coord_y[None, :] + 2 * stencil[:, :, 1] - 1
    reach = jnp.stack(
        [(target_x >= 0) & (target_x < total_x), (target_y >= 0) & (target_y < total_y)], axis=-1
    )
    minus_own = (couplings * (-reach.astype(jnp.float32))[:, :, :, None]).reshape(
        nx, ny, 2, order, order
    )
    factor_own = inv_factors.reshape(nx, ny, order, order)
    fine_own = (1 - coarse).astype(jnp.float32)[:, :, None, None] * left_gram(
        factor_own, factor_own
    )
    lead_own = matmul(fine_own[:, :, None], minus_own)
    fine_flat = fine_own.reshape(nx, ny, flat)
    lead_flat = lead_own.reshape(nx, ny, 2, flat)
    all_cols = {d: slice(None) for d in (1, 2, 3)}
    lo = {d: slice(0, d) for d in (1, 2, 3)}
    hi_x = {d: slice(nx - d, nx) for d in (1, 2, 3)}
    hi_y = {d: slice(ny - d, ny) for d in (1, 2, 3)}
    sizes = (3 * ny, 2 * ny * 2, ny)
    sizes_y = (3 * nx, 2 * nx * 2, nx)

    def send(buffer, axis, pairs):
        return lax.ppermute(buffer, axis, pairs)

    from_xlo = send(face_buffer(fine_flat, lead_flat, inv_factors, stencil, hi_x, all_cols),
                    "gx", shift_pairs(n_gx, 1))
    from_xhi = send(face_buffer(fine_flat, lead_flat, inv_factors, stencil, lo, all_cols),
                    "gx", shift_pairs(n_gx, -1))
    from_ylo = send(face_buffer(fine_flat, lead_flat, inv_factors, stencil, all_cols, hi_y),
                    "gy", shift_pairs(n_gy, 1))
    from_yhi = send(face_buffer(fine_flat, lead_flat, inv_factors, stencil, all_cols, lo),
                    "gy", shift_pairs(n_gy, -1))

    def corner_buffer(rows2, cols2, row1, col1):
        return jnp.concatenate(
            [
                fine_flat[rows2, cols2].reshape(-1, flat),
                lead_flat[row1, col1].reshape(-1, flat),
                code_row(stencil[row1, col1], flat),
            ],
            axis=0,
        )

    corners = {}
    for sx in (1, -1):
        for sy in (1, -1):
            rows2 = slice(nx - 2, nx) if sx == 1 else slice(0, 2)
            cols2 = slice(ny - 2, ny) if sy == 1 else slice(0, 2)
            row1 = nx - 1 if sx == 1 else 0
            col1 = ny - 1 if sy == 1 else 0
            corners[(sx, sy)] = send(
                corner_buffer(rows2, cols2, row1, col1), ("gx", "gy"),
                corner_pairs(n_gx, n_gy, sx, sy),
            )

    def unpack_face(buffer, strip_rows, strip_cols, along_x):
        count = strip_cols if along_x else strip_rows
        n_p, n_w = 3 * count, 2 * count * 2
        p_part = buffer[0:n_p]
        w_part = buffer[n_p : n_p + n_w]
        g_part = buffer[n_p + n_w : n_p + n_w + count]
        codes = buffer[n_p + n_w + count, 0 : 2 * count * 2].astype(jnp.int32)
        if along_x:
            return (p_part.reshape(3, count, flat), w_part.reshape(2, count, 2, flat),
                    g_part.reshape(1, count, flat), codes.reshape(2, count, 2))
        return (p_part.reshape(count, 3, flat), w_part.reshape(count, 2, 2, flat),
                g_part.reshape(count, 1, flat), codes.reshape(count, 2, 2))

    pxl, wxl, gxl, cxl = unpack_face(from_xlo, nx, ny, True)
    pxh, wxh, gxh, cxh = unpack_face(from_xhi, nx, ny, True)
    pyl, wyl, gyl, cyl = unpack_face(from_ylo, nx, ny, False)
    pyh, wyh, gyh, cyh = unpack_face(from_yhi, nx, ny, False)

    def unpack_corner(buffer):
        return (buffer[0:4].reshape(2, 2, flat), buffer[4:6].reshape(2, flat),
                buffer[6, 0:2].astype(jnp.int32))

    c_ll = unpack_corner(corners[(1, 1)])
    c_lh = unpack_corner(corners[(1, -1)])
    c_hl = unpack_corner(corners[(-1, 1)])
    c_hh = unpack_corner(corners[(-1, -1)])

    fine_cycle = jnp.zeros((nx + 6, ny + 6, flat), jnp.float32)
    fine_cycle = fine_cycle.at[3 : 3 + nx, 3 : 3 + ny].set(fine_flat)
    fine_cycle = fine_cycle.at[0:3, 3 : 3 + ny].set(pxl)
    fine_cycle = fine_cycle.at[3 + nx : 6 + nx, 3 : 3 + ny].set(pxh)
    fine_cycle = fine_cycle.at[3 : 3 + nx, 0:3].set(pyl)
    fine_cycle = fine_cycle.at[3 : 3 + nx, 3 + ny : 6 + ny].set(pyh)
    fine_cycle = fine_cycle.at[1:3, 1:3].set(c_ll[0])
    fine_cycle = fine_cycle.at[1:3, 3 + ny : 5 + ny].set(c_lh[0])
    fine_cycle = fine_cycle.at[3 + nx : 5 + nx, 1:3].set(c_hl[0])
    fine_cycle = fine_cycle.at[3 + nx : 5 + nx, 3 + ny : 5 + ny].set(c_hh[0])

    lead_cycle = jnp.zeros((nx + 4, ny + 4, 2, flat), jnp.float32)
    lead_cycle = lead_cycle.at[2 : 2 + nx, 2 : 2 + ny].set(lead_flat)
    lead_cycle = lead_cycle.at[0:2, 2 : 2 + ny].set(wxl)
    lead_cycle = lead_cycle.at[2 + nx : 4 + nx, 2 : 2 + ny].set(wxh)
    lead_cycle = lead_cycle.at[2 : 2 + nx, 0:2].set(wyl)
    lead_cycle = lead_cycle.at[2 : 2 + nx, 2 + ny : 4 + ny].set(wyh)
    lead_cycle = lead_cycle.at[1, 1].set(c_ll[1])
    lead_cycle = lead_cycle.at[1, 2 + ny].set(c_lh[1])
    lead_cycle = lead_cycle.at[2 + nx, 1].set(c_hl[1])
    lead_cycle = lead_cycle.at[2 + nx, 2 + ny].set(c_hh[1])

    side_cycle = jnp.zeros((nx + 4, ny + 4, 2), jnp.int32)
    side_cycle = side_cycle.at[2 : 2 + nx, 2 : 2 + ny].set(stencil)
    side_cycle = side_cycle.at[0:2, 2 : 2 + ny].set(cxl)
    side_cycle = side_cycle.at[2 + nx : 4 + nx, 2 : 2 + ny].set(cxh)
    side_cycle = side_cycle.at[2 : 2 + nx, 0:2].set(cyl)
    side_cycle = side_cycle.at[2 : 2 + nx, 2 + ny : 4 + ny].set(cyh)
    side_cycle = side_cycle.at[1, 1].set(c_ll[2])
    side_cycle = side_cycle.at[1, 2 + ny].set(c_lh[2])
    side_cycle = side_cycle.at[2 + nx, 1].set(c_hl[2])
    side_cycle = side_cycle.at[2 + nx, 2 + ny].set(c_hh[2])

    factor_cycle = jnp.zeros((nx + 2, ny + 2, flat), jnp.float32)
    factor_cycle = factor_cycle.at[1 : 1 + nx, 1 : 1 + ny].set(inv_factors)
    factor_cycle = factor_cycle.at[0:1, 1 : 1 + ny].set(gxl)
    factor_cycle = factor_cycle.at[1 + nx : 2 + nx, 1 : 1 + ny].set(gxh)
    factor_cycle = factor_cycle.at[1 : 1 + nx, 0:1].set(gyl)
    factor_cycle = factor_cycle.at[1 : 1 + nx, 1 + ny : 2 + ny].set(gyh)

    fine_m = fine_cycle.reshape(nx + 6, ny + 6, order, order)
    lead_m = lead_cycle.reshape(nx + 4, ny + 4, 2, order, order)

    up_x, up_y = upwind_pick(fine_m, side_cycle)
    near = jnp.stack(
        [crop_cycle(fine_m, 1), matmul(lead_m[:, :, 0], up_x), matmul(lead_m[:, :, 1], up_y)],
        axis=2,
    )
    near_x, near_y = upwind_pick(near, crop_cycle(side_cycle, 1))
    lead_6 = crop_cycle(lead_m, 1)
    far = jnp.concatenate(
        [
            crop_cycle(fine_m, 2)[:, :, None],
            matmul(lead_6[:, :, 0:1], near_x),
            matmul(lead_6[:, :, 1:2], near_y),
        ],
        axis=2,
    )

    factor_m = factor_cycle.reshape(nx + 2, ny + 2, order, order)
    gup_x, gup_y = upwind_pick(factor_m, stencil)
    scaled_left = matmul(factor_own[:, :, None], minus_own)
    strong = []
    for direction, gup in ((0, gup_x), (1, gup_y)):
        scaled = right_gram(scaled_left[:, :, direction], gup)
        strong.append(jnp.mean(scaled * scaled, axis=(-2, -1)))
    strong = jnp.stack(strong, axis=-1)

    cell_count = nx * ny
    flat_coarse = coarse.reshape(cell_count)
    slot_rank = jnp.cumsum(flat_coarse, dtype=jnp.int32) - flat_coarse
    chosen = (
        (slot_rank[None, :] == jnp.arange(CAP, dtype=jnp.int32)[:, None])
        & (flat_coarse[None, :] == 1)
    ).astype(jnp.int32)
    source = jnp.sum(
        chosen * jnp.arange(cell_count, dtype=jnp.int32)[None, :], axis=1, dtype=jnp.int32
    )
    filled = jnp.sum(chosen, axis=1, dtype=jnp.int32)
    span = ny + 2
    own_i = jnp.arange(nx, dtype=jnp.int32)[:, None] + 1
    own_j = jnp.arange(ny, dtype=jnp.int32)[None, :] + 1
    up_index = jnp.stack(
        [(own_i + 2 * stencil[:, :, 0] - 1) * span + own_j,
         own_i * span + own_j + 2 * stencil[:, :, 1] - 1],
        axis=-1,
    ).reshape(cell_count, 2)
    picked = jnp.take(up_index, source, axis=0, mode="clip").reshape(CAP * 2)
    far_rows = jnp.take(far.reshape((nx + 2) * (ny + 2), 7, order, order), picked, axis=0,
                        mode="clip").reshape(CAP, 2, 7, order, order)
    coupling_rows = jnp.take(minus_own.reshape(cell_count, 2, order, order), source, axis=0,
                             mode="clip")
    restrict = matmul(coupling_rows[:, :, None], far_rows)
    restrict = (restrict * filled[:, None, None, None, None].astype(restrict.dtype)).astype(
        jnp.bfloat16
    )
    return (strong, restrict.reshape(CAP, 14, flat))


def solution(mesh):
    placed = (P("gx", "gy", None), P("gx", "gy", None, None), P("gx", "gy", None), P("gx", "gy"))
    return jax.shard_map(
        on_device,
        mesh=mesh,
        in_specs=placed,
        out_specs=(P("gx", "gy", None), P(("gx", "gy"), None, None)),
        check_vma=False,
    )
```

```python
import math

import jax
import jax.numpy as jnp
from jax import lax
from jax.sharding import PartitionSpec as P

CAP = 12
PREC = lax.Precision.HIGH


def matmul(left_block, right_block):
    return jnp.einsum("...ij,...jk->...ik", left_block, right_block, precision=PREC)


def left_gram(left_block, right_block):
    return jnp.einsum("...ji,...jk->...ik", left_block, right_block, precision=PREC)


def right_gram(left_block, right_block):
    return jnp.einsum("...ij,...kj->...ik", left_block, right_block, precision=PREC)


def crop_cycle(values, margin):
    return values[margin : values.shape[0] - margin, margin : values.shape[1] - margin]


def upwind_pick(values, upwind_side):
    trailing = (1,) * (values.ndim - 2)
    sign_x = upwind_side[:, :, 0].reshape(upwind_side.shape[:2] + trailing)
    sign_y = upwind_side[:, :, 1].reshape(upwind_side.shape[:2] + trailing)
    upwind_x = jnp.where(sign_x == 1, values[2:, 1:-1], values[:-2, 1:-1])
    upwind_y = jnp.where(sign_y == 1, values[1:-1, 2:], values[1:-1, :-2])
    return (upwind_x, upwind_y)


def shift_pairs(count, step):
    return [(i, i + step) for i in range(count) if 0 <= i + step < count]


def corner_pairs(n_x, n_y, step_x, step_y):
    pairs = []
    for a in range(n_x):
        for b in range(n_y):
            if 0 <= a + step_x < n_x and 0 <= b + step_y < n_y:
                pairs.append((a * n_y + b, (a + step_x) * n_y + (b + step_y)))
    return pairs


def code_block(codes, order):
    values = codes.reshape(1, -1).astype(jnp.float32)
    return jnp.pad(values, ((0, order - 1), (0, order - values.shape[1])))[None]


def row_band(pieces):
    return jnp.concatenate(pieces, axis=1)


def padded(values, before_x, before_y):
    widths = [(1, 0) if before_x else (0, 1), (1, 0) if before_y else (0, 1)]
    widths += [(0, 0)] * (values.ndim - 2)
    return jnp.pad(values, widths)


def on_device(inv_factors, couplings, stencil, coarse):
    nx, ny, flat = inv_factors.shape
    order = math.isqrt(flat)
    blk = (order, order)
    n_gx = lax.axis_size("gx")
    n_gy = lax.axis_size("gy")
    total_x = nx * n_gx
    total_y = ny * n_gy
    coord_x = lax.axis_index("gx") * nx + jnp.arange(nx, dtype=jnp.int32)
    coord_y = lax.axis_index("gy") * ny + jnp.arange(ny, dtype=jnp.int32)
    target_x = coord_x[:, None] + 2 * stencil[:, :, 0] - 1
    target_y = coord_y[None, :] + 2 * stencil[:, :, 1] - 1
    reach = jnp.stack(
        [(target_x >= 0) & (target_x < total_x), (target_y >= 0) & (target_y < total_y)], axis=-1
    )
    minus_own = (couplings * (-reach.astype(jnp.float32))[:, :, :, None]).reshape(
        (nx, ny, 2) + blk
    )
    factor_own = inv_factors.reshape((nx, ny) + blk)
    fine_own = (1 - coarse).astype(jnp.float32)[:, :, None, None] * left_gram(
        factor_own, factor_own
    )
    lead_own = matmul(fine_own[:, :, None], minus_own)

    def face(rows, cols):
        return jnp.concatenate(
            [
                fine_own[rows[3], cols[3]].reshape((-1,) + blk),
                lead_own[rows[2], cols[2]].reshape((-1,) + blk),
                factor_own[rows[1], cols[1]].reshape((-1,) + blk),
                code_block(stencil[rows[2], cols[2]], order),
            ],
            axis=0,
        )

    every = {d: slice(None) for d in (1, 2, 3)}
    low = {d: slice(0, d) for d in (1, 2, 3)}
    high_x = {d: slice(nx - d, nx) for d in (1, 2, 3)}
    high_y = {d: slice(ny - d, ny) for d in (1, 2, 3)}
    from_xlo = lax.ppermute(face(high_x, every), "gx", shift_pairs(n_gx, 1))
    from_xhi = lax.ppermute(face(low, every), "gx", shift_pairs(n_gx, -1))
    from_ylo = lax.ppermute(face(every, high_y), "gy", shift_pairs(n_gy, 1))
    from_yhi = lax.ppermute(face(every, low), "gy", shift_pairs(n_gy, -1))

    corners = {}
    for sx in (1, -1):
        for sy in (1, -1):
            rows2 = slice(nx - 2, nx) if sx == 1 else slice(0, 2)
            cols2 = slice(ny - 2, ny) if sy == 1 else slice(0, 2)
            row1 = nx - 1 if sx == 1 else 0
            col1 = ny - 1 if sy == 1 else 0
            buffer = jnp.concatenate(
                [
                    fine_own[rows2, cols2].reshape((-1,) + blk),
                    lead_own[row1, col1],
                    code_block(stencil[row1, col1], order),
                ],
                axis=0,
            )
            corners[(sx, sy)] = lax.ppermute(
                buffer, ("gx", "gy"), corner_pairs(n_gx, n_gy, sx, sy)
            )

    def unpack_face(buffer, count, along_x):
        n_p, n_w = 3 * count, 2 * count * 2
        p_part = buffer[0:n_p]
        w_part = buffer[n_p : n_p + n_w]
        g_part = buffer[n_p + n_w : n_p + n_w + count]
        codes = buffer[n_p + n_w + count, 0, 0 : 2 * count * 2].astype(jnp.int32)
        if along_x:
            return (p_part.reshape((3, count) + blk), w_part.reshape((2, count, 2) + blk),
                    g_part.reshape((1, count) + blk), codes.reshape(2, count, 2))
        return (p_part.reshape((count, 3) + blk), w_part.reshape((count, 2, 2) + blk),
                g_part.reshape((count, 1) + blk), codes.reshape(count, 2, 2))

    pxl, wxl, gxl, cxl = unpack_face(from_xlo, ny, True)
    pxh, wxh, gxh, cxh = unpack_face(from_xhi, ny, True)
    pyl, wyl, gyl, cyl = unpack_face(from_ylo, nx, False)
    pyh, wyh, gyh, cyh = unpack_face(from_yhi, nx, False)

    def unpack_corner(buffer):
        return (buffer[0:4].reshape((2, 2) + blk), buffer[4:6].reshape((1, 1, 2) + blk),
                buffer[6, 0, 0:2].astype(jnp.int32).reshape(1, 1, 2))

    c_ll = unpack_corner(corners[(1, 1)])
    c_lh = unpack_corner(corners[(1, -1)])
    c_hl = unpack_corner(corners[(-1, 1)])
    c_hh = unpack_corner(corners[(-1, -1)])

    def cycle(k, lo_x, own, hi_x, lo_y, hi_y):
        return jnp.concatenate(
            [
                row_band([padded(c_ll[k], True, True), lo_x, padded(c_lh[k], True, False)]),
                row_band([lo_y, own, hi_y]),
                row_band([padded(c_hl[k], False, True), hi_x, padded(c_hh[k], False, False)]),
            ],
            axis=0,
        )

    fine_cycle = cycle(0, pxl, fine_own, pxh, pyl, pyh)
    lead_cycle = cycle(1, wxl, lead_own, wxh, wyl, wyh)
    side_cycle = cycle(2, cxl, stencil, cxh, cyl, cyh)
    corner_zero = jnp.zeros((1, 1) + blk, jnp.float32)
    factor_cycle = jnp.concatenate(
        [
            row_band([corner_zero, gxl, corner_zero]),
            row_band([gyl, factor_own, gyh]),
            row_band([corner_zero, gxh, corner_zero]),
        ],
        axis=0,
    )

    up_x, up_y = upwind_pick(fine_cycle, side_cycle)
    near = jnp.stack(
        [crop_cycle(fine_cycle, 1), matmul(lead_cycle[:, :, 0], up_x),
         matmul(lead_cycle[:, :, 1], up_y)],
        axis=2,
    )
    near_x, near_y = upwind_pick(near, crop_cycle(side_cycle, 1))
    lead_6 = crop_cycle(lead_cycle, 1)
    far = jnp.concatenate(
        [
            crop_cycle(fine_cycle, 2)[:, :, None],
            matmul(lead_6[:, :, 0:1], near_x),
            matmul(lead_6[:, :, 1:2], near_y),
        ],
        axis=2,
    )

    gup_x, gup_y = upwind_pick(factor_cycle, stencil)
    scaled_left = matmul(factor_own[:, :, None], minus_own)
    strong = []
    for direction, gup in ((0, gup_x), (1, gup_y)):
        scaled = right_gram(scaled_left[:, :, direction], gup)
        strong.append(jnp.mean(scaled * scaled, axis=(-2, -1)))
    strong = jnp.stack(strong, axis=-1)

    cell_count = nx * ny
    flat_coarse = coarse.reshape(cell_count)
    slot_rank = jnp.cumsum(flat_coarse, dtype=jnp.int32) - flat_coarse
    chosen = (
        (slot_rank[None, :] == jnp.arange(CAP, dtype=jnp.int32)[:, None])
        & (flat_coarse[None, :] == 1)
    ).astype(jnp.int32)
    source = jnp.sum(
        chosen * jnp.arange(cell_count, dtype=jnp.int32)[None, :], axis=1, dtype=jnp.int32
    )
    filled = jnp.sum(chosen, axis=1, dtype=jnp.int32)
    span = ny + 2
    own_i = jnp.arange(nx, dtype=jnp.int32)[:, None] + 1
    own_j = jnp.arange(ny, dtype=jnp.int32)[None, :] + 1
    up_index = jnp.stack(
        [(own_i + 2 * stencil[:, :, 0] - 1) * span + own_j,
         own_i * span + own_j + 2 * stencil[:, :, 1] - 1],
        axis=-1,
    ).reshape(cell_count, 2)
    picked = jnp.take(up_index, source, axis=0, mode="clip").reshape(CAP * 2)
    far_rows = jnp.take(far.reshape(((nx + 2) * (ny + 2), 7) + blk), picked, axis=0,
                        mode="clip").reshape((CAP, 2, 7) + blk)
    coupling_rows = jnp.take(minus_own.reshape((cell_count, 2) + blk), source, axis=0,
                             mode="clip")
    restrict = matmul(coupling_rows[:, :, None], far_rows)
    restrict = (restrict * filled[:, None, None, None, None].astype(restrict.dtype)).astype(
        jnp.bfloat16
    )
    return (strong, restrict.reshape(CAP, 14, flat))


def solution(mesh):
    placed = (P("gx", "gy", None), P("gx", "gy", None, None), P("gx", "gy", None), P("gx", "gy"))
    return jax.shard_map(
        on_device,
        mesh=mesh,
        in_specs=placed,
        out_specs=(P("gx", "gy", None), P(("gx", "gy"), None, None)),
        check_vma=False,
    )
```

```python
import math

import jax
import jax.numpy as jnp
from jax import lax
from jax.experimental import pallas as pl
from jax.experimental.pallas import tpu as pltpu
from jax.sharding import PartitionSpec as P

CAP = 12
PREC = lax.Precision.HIGH


def matmul(left_block, right_block):
    return jnp.einsum("...ij,...jk->...ik", left_block, right_block, precision=PREC)


def left_gram(left_block, right_block):
    return jnp.einsum("...ji,...jk->...ik", left_block, right_block, precision=PREC)


def right_gram(left_block, right_block):
    return jnp.einsum("...ij,...kj->...ik", left_block, right_block, precision=PREC)


def crop_cycle(values, margin):
    return values[margin : values.shape[0] - margin, margin : values.shape[1] - margin]


def upwind_pick(values, upwind_side):
    trailing = (1,) * (values.ndim - 2)
    sign_x = upwind_side[:, :, 0].reshape(upwind_side.shape[:2] + trailing)
    sign_y = upwind_side[:, :, 1].reshape(upwind_side.shape[:2] + trailing)
    upwind_x = jnp.where(sign_x == 1, values[2:, 1:-1], values[:-2, 1:-1])
    upwind_y = jnp.where(sign_y == 1, values[1:-1, 2:], values[1:-1, :-2])
    return (upwind_x, upwind_y)


def shift_pairs(count, step):
    return [(i, i + step) for i in range(count) if 0 <= i + step < count]


def corner_pairs(n_x, n_y, step_x, step_y):
    pairs = []
    for a in range(n_x):
        for b in range(n_y):
            if 0 <= a + step_x < n_x and 0 <= b + step_y < n_y:
                pairs.append((a * n_y + b, (a + step_x) * n_y + (b + step_y)))
    return pairs


def code_block(codes, order):
    values = codes.reshape(1, -1).astype(jnp.float32)
    return jnp.pad(values, ((0, order - 1), (0, order - values.shape[1])))[None]


def row_band(pieces):
    return jnp.concatenate(pieces, axis=1)


def padded(values, before_x, before_y):
    widths = [(1, 0) if before_x else (0, 1), (1, 0) if before_y else (0, 1)]
    widths += [(0, 0)] * (values.ndim - 2)
    return jnp.pad(values, widths)


def split(value):
    high = value.astype(jnp.bfloat16)
    low = (value - high.astype(jnp.float32)).astype(jnp.bfloat16)
    return high, low


def dot3(left, right, right_t=False):
    dims = (((1,), (1,)), ((), ())) if right_t else (((1,), (0,)), ((), ()))

    def one(a, b):
        return lax.dot_general(a, b, dims, preferred_element_type=jnp.float32)

    return one(left[0], right[0]) + one(left[0], right[1]) + one(left[1], right[0])


def local_kernel(side_ref, slot_ref, fine_ref, lead_ref, factor_ref, minus_ref,
                 xlo_ref, xhi_ref, ylo_ref, yhi_ref, cll_ref, clh_ref, chl_ref, chh_ref,
                 strong_ref, restrict_ref, pg, wg, gg, yg, zg):
    nx, ny = fine_ref.shape[0], fine_ref.shape[1]
    blk = fine_ref.shape[2:]
    zero = jnp.zeros(blk, jnp.float32)
    wide_x, wide_y = nx + 4, ny + 4
    pg_src, wg_src, gg_src = {}, {}, {}
    for i in range(nx):
        for j in range(ny):
            pg_src[(3 + i, 3 + j)] = (fine_ref, (i, j))
            gg_src[(1 + i, 1 + j)] = (factor_ref, (i, j))
            for e in range(2):
                wg_src[(2 + i, 2 + j, e)] = (lead_ref, (i, j, e))
    for c in range(ny):
        for r in range(3):
            pg_src[(r, 3 + c)] = (xlo_ref, (r * ny + c,))
            pg_src[(nx + 3 + r, 3 + c)] = (xhi_ref, (r * ny + c,))
        for r in range(2):
            for e in range(2):
                wg_src[(r, 2 + c, e)] = (xlo_ref, (3 * ny + (r * ny + c) * 2 + e,))
                wg_src[(nx + 2 + r, 2 + c, e)] = (xhi_ref, (3 * ny + (r * ny + c) * 2 + e,))
        gg_src[(0, 1 + c)] = (xlo_ref, (7 * ny + c,))
        gg_src[(nx + 1, 1 + c)] = (xhi_ref, (7 * ny + c,))
    for i in range(nx):
        for r in range(3):
            pg_src[(3 + i, r)] = (ylo_ref, (i * 3 + r,))
            pg_src[(3 + i, ny + 3 + r)] = (yhi_ref, (i * 3 + r,))
        for r in range(2):
            for e in range(2):
                wg_src[(2 + i, r, e)] = (ylo_ref, (3 * nx + (i * 2 + r) * 2 + e,))
                wg_src[(2 + i, ny + 2 + r, e)] = (yhi_ref, (3 * nx + (i * 2 + r) * 2 + e,))
        gg_src[(1 + i, 0)] = (ylo_ref, (7 * nx + i,))
        gg_src[(1 + i, ny + 1)] = (yhi_ref, (7 * nx + i,))
    for ref, px, py, wx, wy in ((cll_ref, 1, 1, 1, 1), (clh_ref, 1, ny + 3, 1, ny + 2),
                                (chl_ref, nx + 3, 1, nx + 2, 1),
                                (chh_ref, nx + 3, ny + 3, nx + 2, ny + 2)):
        for a in range(2):
            for b in range(2):
                pg_src[(px + a, py + b)] = (ref, (a * 2 + b,))
        for e in range(2):
            wg_src[(wx, wy, e)] = (ref, (4 + e,))
    for i in range(nx + 6):
        for j in range(ny + 6):
            ref, at = pg_src.get((i, j), (None, None))
            pg[i, j] = zero if ref is None else ref[at]
    for i in range(wide_x):
        for j in range(wide_y):
            for e in range(2):
                ref, at = wg_src.get((i, j, e), (None, None))
                wg[i, j, e] = zero if ref is None else ref[at]
    for i in range(nx + 2):
        for j in range(ny + 2):
            ref, at = gg_src.get((i, j), (None, None))
            gg[i, j] = zero if ref is None else ref[at]

    def side(i, j, d):
        return side_ref[(i * wide_y + j) * 2 + d]

    def near_step(p, carry):
        i = p // wide_y
        j = p % wide_y
        sx = side(i, j, 0)
        sy = side(i, j, 1)
        yg[i, j, 0] = dot3(split(wg[i, j, 0]), split(pg[i + 2 * sx, j + 1]))
        yg[i, j, 1] = dot3(split(wg[i, j, 1]), split(pg[i + 1, j + 2 * sy]))
        return carry

    lax.fori_loop(0, wide_x * wide_y, near_step, 0)

    def far_step(p, carry):
        i = p // (ny + 2)
        j = p % (ny + 2)
        zg[i, j, 0] = pg[i + 2, j + 2]
        for e in range(2):
            s = side(i + 1, j + 1, e)
            ui = i + 2 * s if e == 0 else i + 1
            uj = j + 1 if e == 0 else j + 2 * s
            lead = split(wg[i + 1, j + 1, e])
            zg[i, j, 1 + 3 * e] = dot3(lead, split(pg[ui + 1, uj + 1]))
            zg[i, j, 2 + 3 * e] = dot3(lead, split(yg[ui, uj, 0]))
            zg[i, j, 3 + 3 * e] = dot3(lead, split(yg[ui, uj, 1]))
        return carry

    lax.fori_loop(0, (nx + 2) * (ny + 2), far_step, 0)

    def strong_step(p, carry):
        i = p // ny
        j = p % ny
        factor = split(factor_ref[i, j])
        for d in range(2):
            s = side(i + 2, j + 2, d)
            up = gg[i + 2 * s, j + 1] if d == 0 else gg[i + 1, j + 2 * s]
            scaled = dot3(split(dot3(factor, split(minus_ref[i, j, d]))), split(up), True)
            total = jnp.sum(scaled * scaled, axis=(0, 1), keepdims=True)
            strong_ref[p * 2 + d] = jnp.broadcast_to(total * (1.0 / scaled.size), (1, 128))
        return carry

    lax.fori_loop(0, nx * ny, strong_step, 0)

    def slot_step(s, carry):
        cell = slot_ref[s * 4]
        weight = slot_ref[s * 4 + 3].astype(jnp.float32)
        ci = cell // ny
        cj = cell % ny
        for d in range(2):
            n = slot_ref[s * 4 + 1 + d]
            ni = n // (ny + 2)
            nj = n % (ny + 2)
            coupling = split(minus_ref[ci, cj, d])
            for w in range(7):
                row = dot3(coupling, split(zg[ni, nj, w]))
                restrict_ref[s, d * 7 + w] = (row * weight).astype(restrict_ref.dtype)
        return carry

    lax.fori_loop(0, restrict_ref.shape[0], slot_step, 0)


def local_compute(side_flat, slot_table, fine_own, lead_own, factor_own, minus_own, buffers):
    nx, ny = fine_own.shape[:2]
    blk = fine_own.shape[2:]
    vmem = pl.BlockSpec(memory_space=pltpu.VMEM)
    smem = pl.BlockSpec(memory_space=pltpu.SMEM)
    f32 = jnp.float32
    strong, restrict = pl.pallas_call(
        local_kernel,
        out_shape=(jax.ShapeDtypeStruct((nx * ny * 2, 1, 128), f32),
                   jax.ShapeDtypeStruct((CAP, 14) + blk, jnp.bfloat16)),
        in_specs=[smem, smem] + [vmem] * (4 + len(buffers)),
        out_specs=(vmem, vmem),
        scratch_shapes=[
            pltpu.VMEM((nx + 6, ny + 6) + blk, f32),
            pltpu.VMEM((nx + 4, ny + 4, 2) + blk, f32),
            pltpu.VMEM((nx + 2, ny + 2) + blk, f32),
            pltpu.VMEM((nx + 4, ny + 4, 2) + blk, f32),
            pltpu.VMEM((nx + 2, ny + 2, 7) + blk, f32),
        ],
        compiler_params=pltpu.CompilerParams(vmem_limit_bytes=60 * 1024 * 1024),
    )(side_flat, slot_table, fine_own, lead_own, factor_own, minus_own, *buffers)
    return strong[:, 0, 0].reshape(nx, ny, 2), restrict


def on_device(inv_factors, couplings, stencil, coarse):
    nx, ny, flat = inv_factors.shape
    order = math.isqrt(flat)
    blk = (order, order)
    n_gx = lax.axis_size("gx")
    n_gy = lax.axis_size("gy")
    total_x = nx * n_gx
    total_y = ny * n_gy
    coord_x = lax.axis_index("gx") * nx + jnp.arange(nx, dtype=jnp.int32)
    coord_y = lax.axis_index("gy") * ny + jnp.arange(ny, dtype=jnp.int32)
    target_x = coord_x[:, None] + 2 * stencil[:, :, 0] - 1
    target_y = coord_y[None, :] + 2 * stencil[:, :, 1] - 1
    reach = jnp.stack(
        [(target_x >= 0) & (target_x < total_x), (target_y >= 0) & (target_y < total_y)], axis=-1
    )
    minus_own = (couplings * (-reach.astype(jnp.float32))[:, :, :, None]).reshape(
        (nx, ny, 2) + blk
    )
    factor_own = inv_factors.reshape((nx, ny) + blk)
    fine_own = (1 - coarse).astype(jnp.float32)[:, :, None, None] * left_gram(
        factor_own, factor_own
    )
    lead_own = matmul(fine_own[:, :, None], minus_own)

    def face(rows, cols):
        return jnp.concatenate(
            [
                fine_own[rows[3], cols[3]].reshape((-1,) + blk),
                lead_own[rows[2], cols[2]].reshape((-1,) + blk),
                factor_own[rows[1], cols[1]].reshape((-1,) + blk),
                code_block(stencil[rows[2], cols[2]], order),
            ],
            axis=0,
        )

    every = {d: slice(None) for d in (1, 2, 3)}
    low = {d: slice(0, d) for d in (1, 2, 3)}
    high_x = {d: slice(nx - d, nx) for d in (1, 2, 3)}
    high_y = {d: slice(ny - d, ny) for d in (1, 2, 3)}
    from_xlo = lax.ppermute(face(high_x, every), "gx", shift_pairs(n_gx, 1))
    from_xhi = lax.ppermute(face(low, every), "gx", shift_pairs(n_gx, -1))
    from_ylo = lax.ppermute(face(every, high_y), "gy", shift_pairs(n_gy, 1))
    from_yhi = lax.ppermute(face(every, low), "gy", shift_pairs(n_gy, -1))

    corners = {}
    for sx in (1, -1):
        for sy in (1, -1):
            rows2 = slice(nx - 2, nx) if sx == 1 else slice(0, 2)
            cols2 = slice(ny - 2, ny) if sy == 1 else slice(0, 2)
            row1 = nx - 1 if sx == 1 else 0
            col1 = ny - 1 if sy == 1 else 0
            buffer = jnp.concatenate(
                [
                    fine_own[rows2, cols2].reshape((-1,) + blk),
                    lead_own[row1, col1],
                    code_block(stencil[row1, col1], order),
                ],
                axis=0,
            )
            corners[(sx, sy)] = lax.ppermute(
                buffer, ("gx", "gy"), corner_pairs(n_gx, n_gy, sx, sy)
            )

    def unpack_face(buffer, count, along_x):
        n_p, n_w = 3 * count, 2 * count * 2
        p_part = buffer[0:n_p]
        w_part = buffer[n_p : n_p + n_w]
        g_part = buffer[n_p + n_w : n_p + n_w + count]
        codes = buffer[n_p + n_w + count, 0, 0 : 2 * count * 2].astype(jnp.int32)
        if along_x:
            return (p_part.reshape((3, count) + blk), w_part.reshape((2, count, 2) + blk),
                    g_part.reshape((1, count) + blk), codes.reshape(2, count, 2))
        return (p_part.reshape((count, 3) + blk), w_part.reshape((count, 2, 2) + blk),
                g_part.reshape((count, 1) + blk), codes.reshape(count, 2, 2))

    pxl, wxl, gxl, cxl = unpack_face(from_xlo, ny, True)
    pxh, wxh, gxh, cxh = unpack_face(from_xhi, ny, True)
    pyl, wyl, gyl, cyl = unpack_face(from_ylo, nx, False)
    pyh, wyh, gyh, cyh = unpack_face(from_yhi, nx, False)

    def unpack_corner(buffer):
        return (buffer[0:4].reshape((2, 2) + blk), buffer[4:6].reshape((1, 1, 2) + blk),
                buffer[6, 0, 0:2].astype(jnp.int32).reshape(1, 1, 2))

    c_ll = unpack_corner(corners[(1, 1)])
    c_lh = unpack_corner(corners[(1, -1)])
    c_hl = unpack_corner(corners[(-1, 1)])
    c_hh = unpack_corner(corners[(-1, -1)])

    def cycle(k, lo_x, own, hi_x, lo_y, hi_y):
        return jnp.concatenate(
            [
                row_band([padded(c_ll[k], True, True), lo_x, padded(c_lh[k], True, False)]),
                row_band([lo_y, own, hi_y]),
                row_band([padded(c_hl[k], False, True), hi_x, padded(c_hh[k], False, False)]),
            ],
            axis=0,
        )

    side_cycle = cycle(2, cxl, stencil, cxh, cyl, cyh)

    cell_count = nx * ny
    flat_coarse = coarse.reshape(cell_count)
    slot_rank = jnp.cumsum(flat_coarse, dtype=jnp.int32) - flat_coarse
    chosen = (
        (slot_rank[None, :] == jnp.arange(CAP, dtype=jnp.int32)[:, None])
        & (flat_coarse[None, :] == 1)
    ).astype(jnp.int32)
    source = jnp.sum(
        chosen * jnp.arange(cell_count, dtype=jnp.int32)[None, :], axis=1, dtype=jnp.int32
    )
    filled = jnp.sum(chosen, axis=1, dtype=jnp.int32)
    span = ny + 2
    own_i = jnp.arange(nx, dtype=jnp.int32)[:, None] + 1
    own_j = jnp.arange(ny, dtype=jnp.int32)[None, :] + 1
    up_index = jnp.stack(
        [(own_i + 2 * stencil[:, :, 0] - 1) * span + own_j,
         own_i * span + own_j + 2 * stencil[:, :, 1] - 1],
        axis=-1,
    ).reshape(cell_count, 2)
    picked = jnp.take(up_index, source, axis=0, mode="clip")
    slot_table = jnp.concatenate([source[:, None], picked, filled[:, None]], axis=1).reshape(-1)
    buffers = (from_xlo, from_xhi, from_ylo, from_yhi, corners[(1, 1)], corners[(1, -1)],
               corners[(-1, 1)], corners[(-1, -1)])
    strong, restrict = local_compute(side_cycle.reshape(-1), slot_table, fine_own, lead_own,
                                     factor_own, minus_own, buffers)
    return (strong, restrict.reshape(CAP, 14, flat))


def solution(mesh):
    placed = (P("gx", "gy", None), P("gx", "gy", None, None), P("gx", "gy", None), P("gx", "gy"))
    return jax.shard_map(
        on_device,
        mesh=mesh,
        in_specs=placed,
        out_specs=(P("gx", "gy", None), P(("gx", "gy"), None, None)),
        check_vma=False,
    )
```

```python
import math

import jax
import jax.numpy as jnp
from jax import lax
from jax.experimental import pallas as pl
from jax.experimental.pallas import tpu as pltpu
from jax.sharding import PartitionSpec as P

CAP = 12
PREC = lax.Precision.HIGH


def matmul(left_block, right_block):
    return jnp.einsum("...ij,...jk->...ik", left_block, right_block, precision=PREC)


def left_gram(left_block, right_block):
    return jnp.einsum("...ji,...jk->...ik", left_block, right_block, precision=PREC)


def right_gram(left_block, right_block):
    return jnp.einsum("...ij,...kj->...ik", left_block, right_block, precision=PREC)


def crop_cycle(values, margin):
    return values[margin : values.shape[0] - margin, margin : values.shape[1] - margin]


def upwind_pick(values, upwind_side):
    trailing = (1,) * (values.ndim - 2)
    sign_x = upwind_side[:, :, 0].reshape(upwind_side.shape[:2] + trailing)
    sign_y = upwind_side[:, :, 1].reshape(upwind_side.shape[:2] + trailing)
    upwind_x = jnp.where(sign_x == 1, values[2:, 1:-1], values[:-2, 1:-1])
    upwind_y = jnp.where(sign_y == 1, values[1:-1, 2:], values[1:-1, :-2])
    return (upwind_x, upwind_y)


def shift_pairs(count, step):
    return [(i, i + step) for i in range(count) if 0 <= i + step < count]


def corner_pairs(n_x, n_y, step_x, step_y):
    pairs = []
    for a in range(n_x):
        for b in range(n_y):
            if 0 <= a + step_x < n_x and 0 <= b + step_y < n_y:
                pairs.append((a * n_y + b, (a + step_x) * n_y + (b + step_y)))
    return pairs


def code_block(codes, order):
    values = codes.reshape(1, -1).astype(jnp.float32)
    return jnp.pad(values, ((0, order - 1), (0, order - values.shape[1])))[None]


def row_band(pieces):
    return jnp.concatenate(pieces, axis=1)


def padded(values, before_x, before_y):
    widths = [(1, 0) if before_x else (0, 1), (1, 0) if before_y else (0, 1)]
    widths += [(0, 0)] * (values.ndim - 2)
    return jnp.pad(values, widths)


def split(value):
    high = value.astype(jnp.bfloat16)
    low = (value - high.astype(jnp.float32)).astype(jnp.bfloat16)
    return high, low


def dot3(left, right, right_t=False):
    dims = (((1,), (1,)), ((), ())) if right_t else (((1,), (0,)), ((), ()))

    def one(a, b):
        return lax.dot_general(a, b, dims, preferred_element_type=jnp.float32)

    return one(left[0], right[0]) + one(left[0], right[1]) + one(left[1], right[0])


def local_kernel(side_ref, slot_ref, fine_ref, lead_ref, factor_ref, minus_ref,
                 xlo_ref, xhi_ref, ylo_ref, yhi_ref, cll_ref, clh_ref, chl_ref, chh_ref,
                 strong_ref, restrict_ref, pg, wg, gg, yg, zg):
    nx, ny = fine_ref.shape[0], fine_ref.shape[1]
    blk = fine_ref.shape[2:]
    zero = jnp.zeros(blk, jnp.float32)
    wide_x, wide_y = nx + 4, ny + 4
    pg_src, wg_src, gg_src = {}, {}, {}
    for i in range(nx):
        for j in range(ny):
            pg_src[(3 + i, 3 + j)] = (fine_ref, (i, j))
            gg_src[(1 + i, 1 + j)] = (factor_ref, (i, j))
            for e in range(2):
                wg_src[(2 + i, 2 + j, e)] = (lead_ref, (i, j, e))
    for c in range(ny):
        for r in range(3):
            pg_src[(r, 3 + c)] = (xlo_ref, (r * ny + c,))
            pg_src[(nx + 3 + r, 3 + c)] = (xhi_ref, (r * ny + c,))
        for r in range(2):
            for e in range(2):
                wg_src[(r, 2 + c, e)] = (xlo_ref, (3 * ny + (r * ny + c) * 2 + e,))
                wg_src[(nx + 2 + r, 2 + c, e)] = (xhi_ref, (3 * ny + (r * ny + c) * 2 + e,))
        gg_src[(0, 1 + c)] = (xlo_ref, (7 * ny + c,))
        gg_src[(nx + 1, 1 + c)] = (xhi_ref, (7 * ny + c,))
    for i in range(nx):
        for r in range(3):
            pg_src[(3 + i, r)] = (ylo_ref, (i * 3 + r,))
            pg_src[(3 + i, ny + 3 + r)] = (yhi_ref, (i * 3 + r,))
        for r in range(2):
            for e in range(2):
                wg_src[(2 + i, r, e)] = (ylo_ref, (3 * nx + (i * 2 + r) * 2 + e,))
                wg_src[(2 + i, ny + 2 + r, e)] = (yhi_ref, (3 * nx + (i * 2 + r) * 2 + e,))
        gg_src[(1 + i, 0)] = (ylo_ref, (7 * nx + i,))
        gg_src[(1 + i, ny + 1)] = (yhi_ref, (7 * nx + i,))
    for ref, px, py, wx, wy in ((cll_ref, 1, 1, 1, 1), (clh_ref, 1, ny + 3, 1, ny + 2),
                                (chl_ref, nx + 3, 1, nx + 2, 1),
                                (chh_ref, nx + 3, ny + 3, nx + 2, ny + 2)):
        for a in range(2):
            for b in range(2):
                pg_src[(px + a, py + b)] = (ref, (a * 2 + b,))
        for e in range(2):
            wg_src[(wx, wy, e)] = (ref, (4 + e,))
    for i in range(nx + 6):
        for j in range(ny + 6):
            ref, at = pg_src.get((i, j), (None, None))
            pg[i, j] = zero if ref is None else ref[at]
    for i in range(wide_x):
        for j in range(wide_y):
            for e in range(2):
                ref, at = wg_src.get((i, j, e), (None, None))
                wg[i, j, e] = zero if ref is None else ref[at]
    for i in range(nx + 2):
        for j in range(ny + 2):
            ref, at = gg_src.get((i, j), (None, None))
            gg[i, j] = zero if ref is None else ref[at]

    def side(i, j, d):
        return side_ref[(i * wide_y + j) * 2 + d]

    def near_step(p, carry):
        i = p // wide_y
        j = p % wide_y
        sx = side(i, j, 0)
        sy = side(i, j, 1)
        yg[i, j, 0] = dot3(split(wg[i, j, 0]), split(pg[i + 2 * sx, j + 1]))
        yg[i, j, 1] = dot3(split(wg[i, j, 1]), split(pg[i + 1, j + 2 * sy]))
        return carry

    lax.fori_loop(0, wide_x * wide_y, near_step, 0, unroll=4)

    def far_step(p, carry):
        i = p // (ny + 2)
        j = p % (ny + 2)
        zg[i, j, 0] = pg[i + 2, j + 2]
        for e in range(2):
            s = side(i + 1, j + 1, e)
            ui = i + 2 * s if e == 0 else i + 1
            uj = j + 1 if e == 0 else j + 2 * s
            lead = split(wg[i + 1, j + 1, e])
            zg[i, j, 1 + 3 * e] = dot3(lead, split(pg[ui + 1, uj + 1]))
            zg[i, j, 2 + 3 * e] = dot3(lead, split(yg[ui, uj, 0]))
            zg[i, j, 3 + 3 * e] = dot3(lead, split(yg[ui, uj, 1]))
        return carry

    lax.fori_loop(0, (nx + 2) * (ny + 2), far_step, 0, unroll=4)

    def strong_step(p, carry):
        i = p // ny
        j = p % ny
        factor = split(factor_ref[i, j])
        for d in range(2):
            s = side(i + 2, j + 2, d)
            up = gg[i + 2 * s, j + 1] if d == 0 else gg[i + 1, j + 2 * s]
            scaled = dot3(split(dot3(factor, split(minus_ref[i, j, d]))), split(up), True)
            total = jnp.sum(scaled * scaled, axis=(0, 1), keepdims=True)
            strong_ref[p * 2 + d] = jnp.broadcast_to(total * (1.0 / scaled.size), (1, 128))
        return carry

    lax.fori_loop(0, nx * ny, strong_step, 0, unroll=4)

    def slot_step(s, carry):
        cell = slot_ref[s * 4]
        weight = slot_ref[s * 4 + 3].astype(jnp.float32)
        ci = cell // ny
        cj = cell % ny
        for d in range(2):
            n = slot_ref[s * 4 + 1 + d]
            ni = n // (ny + 2)
            nj = n % (ny + 2)
            coupling = split(minus_ref[ci, cj, d])
            for w in range(7):
                row = dot3(coupling, split(zg[ni, nj, w]))
                restrict_ref[s, d * 7 + w] = (row * weight).astype(restrict_ref.dtype)
        return carry

    lax.fori_loop(0, restrict_ref.shape[0], slot_step, 0, unroll=4)


def local_compute(side_flat, slot_table, fine_own, lead_own, factor_own, minus_own, buffers):
    nx, ny = fine_own.shape[:2]
    blk = fine_own.shape[2:]
    vmem = pl.BlockSpec(memory_space=pltpu.VMEM)
    smem = pl.BlockSpec(memory_space=pltpu.SMEM)
    f32 = jnp.float32
    strong, restrict = pl.pallas_call(
        local_kernel,
        out_shape=(jax.ShapeDtypeStruct((nx * ny * 2, 1, 128), f32),
                   jax.ShapeDtypeStruct((CAP, 14) + blk, jnp.bfloat16)),
        in_specs=[smem, smem] + [vmem] * (4 + len(buffers)),
        out_specs=(vmem, vmem),
        scratch_shapes=[
            pltpu.VMEM((nx + 6, ny + 6) + blk, f32),
            pltpu.VMEM((nx + 4, ny + 4, 2) + blk, f32),
            pltpu.VMEM((nx + 2, ny + 2) + blk, f32),
            pltpu.VMEM((nx + 4, ny + 4, 2) + blk, f32),
            pltpu.VMEM((nx + 2, ny + 2, 7) + blk, f32),
        ],
        compiler_params=pltpu.CompilerParams(vmem_limit_bytes=60 * 1024 * 1024),
    )(side_flat, slot_table, fine_own, lead_own, factor_own, minus_own, *buffers)
    return strong[:, 0, 0].reshape(nx, ny, 2), restrict


def on_device(inv_factors, couplings, stencil, coarse):
    nx, ny, flat = inv_factors.shape
    order = math.isqrt(flat)
    blk = (order, order)
    n_gx = lax.axis_size("gx")
    n_gy = lax.axis_size("gy")
    total_x = nx * n_gx
    total_y = ny * n_gy
    coord_x = lax.axis_index("gx") * nx + jnp.arange(nx, dtype=jnp.int32)
    coord_y = lax.axis_index("gy") * ny + jnp.arange(ny, dtype=jnp.int32)
    target_x = coord_x[:, None] + 2 * stencil[:, :, 0] - 1
    target_y = coord_y[None, :] + 2 * stencil[:, :, 1] - 1
    reach = jnp.stack(
        [(target_x >= 0) & (target_x < total_x), (target_y >= 0) & (target_y < total_y)], axis=-1
    )
    minus_own = (couplings * (-reach.astype(jnp.float32))[:, :, :, None]).reshape(
        (nx, ny, 2) + blk
    )
    factor_own = inv_factors.reshape((nx, ny) + blk)
    fine_own = (1 - coarse).astype(jnp.float32)[:, :, None, None] * left_gram(
        factor_own, factor_own
    )
    lead_own = matmul(fine_own[:, :, None], minus_own)

    def face(rows, cols):
        return jnp.concatenate(
            [
                fine_own[rows[3], cols[3]].reshape((-1,) + blk),
                lead_own[rows[2], cols[2]].reshape((-1,) + blk),
                factor_own[rows[1], cols[1]].reshape((-1,) + blk),
                code_block(stencil[rows[2], cols[2]], order),
            ],
            axis=0,
        )

    every = {d: slice(None) for d in (1, 2, 3)}
    low = {d: slice(0, d) for d in (1, 2, 3)}
    high_x = {d: slice(nx - d, nx) for d in (1, 2, 3)}
    high_y = {d: slice(ny - d, ny) for d in (1, 2, 3)}
    from_xlo = lax.ppermute(face(high_x, every), "gx", shift_pairs(n_gx, 1))
    from_xhi = lax.ppermute(face(low, every), "gx", shift_pairs(n_gx, -1))
    from_ylo = lax.ppermute(face(every, high_y), "gy", shift_pairs(n_gy, 1))
    from_yhi = lax.ppermute(face(every, low), "gy", shift_pairs(n_gy, -1))

    corners = {}
    for sx in (1, -1):
        for sy in (1, -1):
            rows2 = slice(nx - 2, nx) if sx == 1 else slice(0, 2)
            cols2 = slice(ny - 2, ny) if sy == 1 else slice(0, 2)
            row1 = nx - 1 if sx == 1 else 0
            col1 = ny - 1 if sy == 1 else 0
            buffer = jnp.concatenate(
                [
                    fine_own[rows2, cols2].reshape((-1,) + blk),
                    lead_own[row1, col1],
                    code_block(stencil[row1, col1], order),
                ],
                axis=0,
            )
            corners[(sx, sy)] = lax.ppermute(
                buffer, ("gx", "gy"), corner_pairs(n_gx, n_gy, sx, sy)
            )

    def unpack_face(buffer, count, along_x):
        n_p, n_w = 3 * count, 2 * count * 2
        p_part = buffer[0:n_p]
        w_part = buffer[n_p : n_p + n_w]
        g_part = buffer[n_p + n_w : n_p + n_w + count]
        codes = buffer[n_p + n_w + count, 0, 0 : 2 * count * 2].astype(jnp.int32)
        if along_x:
            return (p_part.reshape((3, count) + blk), w_part.reshape((2, count, 2) + blk),
                    g_part.reshape((1, count) + blk), codes.reshape(2, count, 2))
        return (p_part.reshape((count, 3) + blk), w_part.reshape((count, 2, 2) + blk),
                g_part.reshape((count, 1) + blk), codes.reshape(count, 2, 2))

    pxl, wxl, gxl, cxl = unpack_face(from_xlo, ny, True)
    pxh, wxh, gxh, cxh = unpack_face(from_xhi, ny, True)
    pyl, wyl, gyl, cyl = unpack_face(from_ylo, nx, False)
    pyh, wyh, gyh, cyh = unpack_face(from_yhi, nx, False)

    def unpack_corner(buffer):
        return (buffer[0:4].reshape((2, 2) + blk), buffer[4:6].reshape((1, 1, 2) + blk),
                buffer[6, 0, 0:2].astype(jnp.int32).reshape(1, 1, 2))

    c_ll = unpack_corner(corners[(1, 1)])
    c_lh = unpack_corner(corners[(1, -1)])
    c_hl = unpack_corner(corners[(-1, 1)])
    c_hh = unpack_corner(corners[(-1, -1)])

    def cycle(k, lo_x, own, hi_x, lo_y, hi_y):
        return jnp.concatenate(
            [
                row_band([padded(c_ll[k], True, True), lo_x, padded(c_lh[k], True, False)]),
                row_band([lo_y, own, hi_y]),
                row_band([padded(c_hl[k], False, True), hi_x, padded(c_hh[k], False, False)]),
            ],
            axis=0,
        )

    side_cycle = cycle(2, cxl, stencil, cxh, cyl, cyh)

    cell_count = nx * ny
    flat_coarse = coarse.reshape(cell_count)
    slot_rank = jnp.cumsum(flat_coarse, dtype=jnp.int32) - flat_coarse
    chosen = (
        (slot_rank[None, :] == jnp.arange(CAP, dtype=jnp.int32)[:, None])
        & (flat_coarse[None, :] == 1)
    ).astype(jnp.int32)
    source = jnp.sum(
        chosen * jnp.arange(cell_count, dtype=jnp.int32)[None, :], axis=1, dtype=jnp.int32
    )
    filled = jnp.sum(chosen, axis=1, dtype=jnp.int32)
    span = ny + 2
    own_i = jnp.arange(nx, dtype=jnp.int32)[:, None] + 1
    own_j = jnp.arange(ny, dtype=jnp.int32)[None, :] + 1
    up_index = jnp.stack(
        [(own_i + 2 * stencil[:, :, 0] - 1) * span + own_j,
         own_i * span + own_j + 2 * stencil[:, :, 1] - 1],
        axis=-1,
    ).reshape(cell_count, 2)
    picked = jnp.take(up_index, source, axis=0, mode="clip")
    slot_table = jnp.concatenate([source[:, None], picked, filled[:, None]], axis=1).reshape(-1)
    buffers = (from_xlo, from_xhi, from_ylo, from_yhi, corners[(1, 1)], corners[(1, -1)],
               corners[(-1, 1)], corners[(-1, -1)])
    strong, restrict = local_compute(side_cycle.reshape(-1), slot_table, fine_own, lead_own,
                                     factor_own, minus_own, buffers)
    return (strong, restrict.reshape(CAP, 14, flat))


def solution(mesh):
    placed = (P("gx", "gy", None), P("gx", "gy", None, None), P("gx", "gy", None), P("gx", "gy"))
    return jax.shard_map(
        on_device,
        mesh=mesh,
        in_specs=placed,
        out_specs=(P("gx", "gy", None), P(("gx", "gy"), None, None)),
        check_vma=False,
    )
```

```python
import math

import jax
import jax.numpy as jnp
from jax import lax
from jax.experimental import pallas as pl
from jax.experimental.pallas import tpu as pltpu
from jax.sharding import PartitionSpec as P

CAP = 12
PREC = lax.Precision.HIGH


def matmul(left_block, right_block):
    return jnp.einsum("...ij,...jk->...ik", left_block, right_block, precision=PREC)


def left_gram(left_block, right_block):
    return jnp.einsum("...ji,...jk->...ik", left_block, right_block, precision=PREC)


def right_gram(left_block, right_block):
    return jnp.einsum("...ij,...kj->...ik", left_block, right_block, precision=PREC)


def crop_cycle(values, margin):
    return values[margin : values.shape[0] - margin, margin : values.shape[1] - margin]


def upwind_pick(values, upwind_side):
    trailing = (1,) * (values.ndim - 2)
    sign_x = upwind_side[:, :, 0].reshape(upwind_side.shape[:2] + trailing)
    sign_y = upwind_side[:, :, 1].reshape(upwind_side.shape[:2] + trailing)
    upwind_x = jnp.where(sign_x == 1, values[2:, 1:-1], values[:-2, 1:-1])
    upwind_y = jnp.where(sign_y == 1, values[1:-1, 2:], values[1:-1, :-2])
    return (upwind_x, upwind_y)


def shift_pairs(count, step):
    return [(i, i + step) for i in range(count) if 0 <= i + step < count]


def corner_pairs(n_x, n_y, step_x, step_y):
    pairs = []
    for a in range(n_x):
        for b in range(n_y):
            if 0 <= a + step_x < n_x and 0 <= b + step_y < n_y:
                pairs.append((a * n_y + b, (a + step_x) * n_y + (b + step_y)))
    return pairs


def code_block(codes, order):
    values = codes.reshape(1, -1).astype(jnp.float32)
    return jnp.pad(values, ((0, order - 1), (0, order - values.shape[1])))[None]


def row_band(pieces):
    return jnp.concatenate(pieces, axis=1)


def padded(values, before_x, before_y):
    widths = [(1, 0) if before_x else (0, 1), (1, 0) if before_y else (0, 1)]
    widths += [(0, 0)] * (values.ndim - 2)
    return jnp.pad(values, widths)


def split(value):
    high = value.astype(jnp.bfloat16)
    low = (value - high.astype(jnp.float32)).astype(jnp.bfloat16)
    return high, low


def dot3(left, right, right_t=False):
    dims = (((1,), (1,)), ((), ())) if right_t else (((1,), (0,)), ((), ()))

    def one(a, b):
        return lax.dot_general(a, b, dims, preferred_element_type=jnp.float32)

    return one(left[0], right[0]) + one(left[0], right[1]) + one(left[1], right[0])


def local_kernel(side_ref, slot_ref, fine_ref, lead_ref, factor_ref, minus_ref,
                 xlo_ref, xhi_ref, ylo_ref, yhi_ref, cll_ref, clh_ref, chl_ref, chh_ref,
                 strong_ref, restrict_ref, pg, wg, gg, yg, zg):
    nx, ny = fine_ref.shape[0], fine_ref.shape[1]
    blk = fine_ref.shape[2:]
    zero = jnp.zeros(blk, jnp.float32)
    wide_x, wide_y = nx + 4, ny + 4
    pg_src, wg_src, gg_src = {}, {}, {}
    for i in range(nx):
        for j in range(ny):
            pg_src[(3 + i, 3 + j)] = (fine_ref, (i, j))
            gg_src[(1 + i, 1 + j)] = (factor_ref, (i, j))
            for e in range(2):
                wg_src[(2 + i, 2 + j, e)] = (lead_ref, (i, j, e))
    for c in range(ny):
        for r in range(3):
            pg_src[(r, 3 + c)] = (xlo_ref, (r * ny + c,))
            pg_src[(nx + 3 + r, 3 + c)] = (xhi_ref, (r * ny + c,))
        for r in range(2):
            for e in range(2):
                wg_src[(r, 2 + c, e)] = (xlo_ref, (3 * ny + (r * ny + c) * 2 + e,))
                wg_src[(nx + 2 + r, 2 + c, e)] = (xhi_ref, (3 * ny + (r * ny + c) * 2 + e,))
        gg_src[(0, 1 + c)] = (xlo_ref, (7 * ny + c,))
        gg_src[(nx + 1, 1 + c)] = (xhi_ref, (7 * ny + c,))
    for i in range(nx):
        for r in range(3):
            pg_src[(3 + i, r)] = (ylo_ref, (i * 3 + r,))
            pg_src[(3 + i, ny + 3 + r)] = (yhi_ref, (i * 3 + r,))
        for r in range(2):
            for e in range(2):
                wg_src[(2 + i, r, e)] = (ylo_ref, (3 * nx + (i * 2 + r) * 2 + e,))
                wg_src[(2 + i, ny + 2 + r, e)] = (yhi_ref, (3 * nx + (i * 2 + r) * 2 + e,))
        gg_src[(1 + i, 0)] = (ylo_ref, (7 * nx + i,))
        gg_src[(1 + i, ny + 1)] = (yhi_ref, (7 * nx + i,))
    for ref, px, py, wx, wy in ((cll_ref, 1, 1, 1, 1), (clh_ref, 1, ny + 3, 1, ny + 2),
                                (chl_ref, nx + 3, 1, nx + 2, 1),
                                (chh_ref, nx + 3, ny + 3, nx + 2, ny + 2)):
        for a in range(2):
            for b in range(2):
                pg_src[(px + a, py + b)] = (ref, (a * 2 + b,))
        for e in range(2):
            wg_src[(wx, wy, e)] = (ref, (4 + e,))
    for i in range(nx + 6):
        for j in range(ny + 6):
            ref, at = pg_src.get((i, j), (None, None))
            pg[i, j] = zero if ref is None else ref[at]
    for i in range(wide_x):
        for j in range(wide_y):
            for e in range(2):
                ref, at = wg_src.get((i, j, e), (None, None))
                wg[i, j, e] = zero if ref is None else ref[at]
    for i in range(nx + 2):
        for j in range(ny + 2):
            ref, at = gg_src.get((i, j), (None, None))
            gg[i, j] = zero if ref is None else ref[at]

    def side(i, j, d):
        return side_ref[(i * wide_y + j) * 2 + d]

    def near_step(p, carry):
        i = p // wide_y
        j = p % wide_y
        sx = side(i, j, 0)
        sy = side(i, j, 1)
        yg[i, j, 0] = dot3(split(wg[i, j, 0]), split(pg[i + 2 * sx, j + 1]))
        yg[i, j, 1] = dot3(split(wg[i, j, 1]), split(pg[i + 1, j + 2 * sy]))
        return carry

    lax.fori_loop(0, wide_x * wide_y, near_step, 0, unroll=8)

    def far_step(p, carry):
        i = p // (ny + 2)
        j = p % (ny + 2)
        zg[i, j, 0] = pg[i + 2, j + 2]
        for e in range(2):
            s = side(i + 1, j + 1, e)
            ui = i + 2 * s if e == 0 else i + 1
            uj = j + 1 if e == 0 else j + 2 * s
            lead = split(wg[i + 1, j + 1, e])
            zg[i, j, 1 + 3 * e] = dot3(lead, split(pg[ui + 1, uj + 1]))
            zg[i, j, 2 + 3 * e] = dot3(lead, split(yg[ui, uj, 0]))
            zg[i, j, 3 + 3 * e] = dot3(lead, split(yg[ui, uj, 1]))
        return carry

    lax.fori_loop(0, (nx + 2) * (ny + 2), far_step, 0, unroll=8)

    def strong_step(p, carry):
        i = p // ny
        j = p % ny
        factor = split(factor_ref[i, j])
        for d in range(2):
            s = side(i + 2, j + 2, d)
            up = gg[i + 2 * s, j + 1] if d == 0 else gg[i + 1, j + 2 * s]
            scaled = dot3(split(dot3(factor, split(minus_ref[i, j, d]))), split(up), True)
            total = jnp.sum(scaled * scaled, axis=(0, 1), keepdims=True)
            strong_ref[p * 2 + d] = jnp.broadcast_to(total * (1.0 / scaled.size), (1, 128))
        return carry

    lax.fori_loop(0, nx * ny, strong_step, 0, unroll=8)

    def slot_step(s, carry):
        cell = slot_ref[s * 4]
        weight = slot_ref[s * 4 + 3].astype(jnp.float32)
        ci = cell // ny
        cj = cell % ny
        for d in range(2):
            n = slot_ref[s * 4 + 1 + d]
            ni = n // (ny + 2)
            nj = n % (ny + 2)
            coupling = split(minus_ref[ci, cj, d])
            for w in range(7):
                row = dot3(coupling, split(zg[ni, nj, w]))
                restrict_ref[s, d * 7 + w] = (row * weight).astype(restrict_ref.dtype)
        return carry

    lax.fori_loop(0, restrict_ref.shape[0], slot_step, 0, unroll=8)


def local_compute(side_flat, slot_table, fine_own, lead_own, factor_own, minus_own, buffers):
    nx, ny = fine_own.shape[:2]
    blk = fine_own.shape[2:]
    vmem = pl.BlockSpec(memory_space=pltpu.VMEM)
    smem = pl.BlockSpec(memory_space=pltpu.SMEM)
    f32 = jnp.float32
    strong, restrict = pl.pallas_call(
        local_kernel,
        out_shape=(jax.ShapeDtypeStruct((nx * ny * 2, 1, 128), f32),
                   jax.ShapeDtypeStruct((CAP, 14) + blk, jnp.bfloat16)),
        in_specs=[smem, smem] + [vmem] * (4 + len(buffers)),
        out_specs=(vmem, vmem),
        scratch_shapes=[
            pltpu.VMEM((nx + 6, ny + 6) + blk, f32),
            pltpu.VMEM((nx + 4, ny + 4, 2) + blk, f32),
            pltpu.VMEM((nx + 2, ny + 2) + blk, f32),
            pltpu.VMEM((nx + 4, ny + 4, 2) + blk, f32),
            pltpu.VMEM((nx + 2, ny + 2, 7) + blk, f32),
        ],
        compiler_params=pltpu.CompilerParams(vmem_limit_bytes=60 * 1024 * 1024),
    )(side_flat, slot_table, fine_own, lead_own, factor_own, minus_own, *buffers)
    return strong[:, 0, 0].reshape(nx, ny, 2), restrict


def on_device(inv_factors, couplings, stencil, coarse):
    nx, ny, flat = inv_factors.shape
    order = math.isqrt(flat)
    blk = (order, order)
    n_gx = lax.axis_size("gx")
    n_gy = lax.axis_size("gy")
    total_x = nx * n_gx
    total_y = ny * n_gy
    coord_x = lax.axis_index("gx") * nx + jnp.arange(nx, dtype=jnp.int32)
    coord_y = lax.axis_index("gy") * ny + jnp.arange(ny, dtype=jnp.int32)
    target_x = coord_x[:, None] + 2 * stencil[:, :, 0] - 1
    target_y = coord_y[None, :] + 2 * stencil[:, :, 1] - 1
    reach = jnp.stack(
        [(target_x >= 0) & (target_x < total_x), (target_y >= 0) & (target_y < total_y)], axis=-1
    )
    minus_own = (couplings * (-reach.astype(jnp.float32))[:, :, :, None]).reshape(
        (nx, ny, 2) + blk
    )
    factor_own = inv_factors.reshape((nx, ny) + blk)
    fine_own = (1 - coarse).astype(jnp.float32)[:, :, None, None] * left_gram(
        factor_own, factor_own
    )
    lead_own = matmul(fine_own[:, :, None], minus_own)

    def face(rows, cols):
        return jnp.concatenate(
            [
                fine_own[rows[3], cols[3]].reshape((-1,) + blk),
                lead_own[rows[2], cols[2]].reshape((-1,) + blk),
                factor_own[rows[1], cols[1]].reshape((-1,) + blk),
                code_block(stencil[rows[2], cols[2]], order),
            ],
            axis=0,
        )

    every = {d: slice(None) for d in (1, 2, 3)}
    low = {d: slice(0, d) for d in (1, 2, 3)}
    high_x = {d: slice(nx - d, nx) for d in (1, 2, 3)}
    high_y = {d: slice(ny - d, ny) for d in (1, 2, 3)}
    def send_flat(buffer, axis, pairs):
        arrived = lax.ppermute(buffer.reshape(buffer.shape[0], flat), axis, pairs)
        return arrived.reshape(buffer.shape)

    from_xlo = send_flat(face(high_x, every), "gx", shift_pairs(n_gx, 1))
    from_xhi = send_flat(face(low, every), "gx", shift_pairs(n_gx, -1))
    from_ylo = send_flat(face(every, high_y), "gy", shift_pairs(n_gy, 1))
    from_yhi = send_flat(face(every, low), "gy", shift_pairs(n_gy, -1))

    corners = {}
    for sx in (1, -1):
        for sy in (1, -1):
            rows2 = slice(nx - 2, nx) if sx == 1 else slice(0, 2)
            cols2 = slice(ny - 2, ny) if sy == 1 else slice(0, 2)
            row1 = nx - 1 if sx == 1 else 0
            col1 = ny - 1 if sy == 1 else 0
            buffer = jnp.concatenate(
                [
                    fine_own[rows2, cols2].reshape((-1,) + blk),
                    lead_own[row1, col1],
                    code_block(stencil[row1, col1], order),
                ],
                axis=0,
            )
            corners[(sx, sy)] = lax.ppermute(
                buffer, ("gx", "gy"), corner_pairs(n_gx, n_gy, sx, sy)
            )

    def unpack_face(buffer, count, along_x):
        n_p, n_w = 3 * count, 2 * count * 2
        p_part = buffer[0:n_p]
        w_part = buffer[n_p : n_p + n_w]
        g_part = buffer[n_p + n_w : n_p + n_w + count]
        codes = buffer[n_p + n_w + count, 0, 0 : 2 * count * 2].astype(jnp.int32)
        if along_x:
            return (p_part.reshape((3, count) + blk), w_part.reshape((2, count, 2) + blk),
                    g_part.reshape((1, count) + blk), codes.reshape(2, count, 2))
        return (p_part.reshape((count, 3) + blk), w_part.reshape((count, 2, 2) + blk),
                g_part.reshape((count, 1) + blk), codes.reshape(count, 2, 2))

    pxl, wxl, gxl, cxl = unpack_face(from_xlo, ny, True)
    pxh, wxh, gxh, cxh = unpack_face(from_xhi, ny, True)
    pyl, wyl, gyl, cyl = unpack_face(from_ylo, nx, False)
    pyh, wyh, gyh, cyh = unpack_face(from_yhi, nx, False)

    def unpack_corner(buffer):
        return (buffer[0:4].reshape((2, 2) + blk), buffer[4:6].reshape((1, 1, 2) + blk),
                buffer[6, 0, 0:2].astype(jnp.int32).reshape(1, 1, 2))

    c_ll = unpack_corner(corners[(1, 1)])
    c_lh = unpack_corner(corners[(1, -1)])
    c_hl = unpack_corner(corners[(-1, 1)])
    c_hh = unpack_corner(corners[(-1, -1)])

    def cycle(k, lo_x, own, hi_x, lo_y, hi_y):
        return jnp.concatenate(
            [
                row_band([padded(c_ll[k], True, True), lo_x, padded(c_lh[k], True, False)]),
                row_band([lo_y, own, hi_y]),
                row_band([padded(c_hl[k], False, True), hi_x, padded(c_hh[k], False, False)]),
            ],
            axis=0,
        )

    side_cycle = cycle(2, cxl, stencil, cxh, cyl, cyh)

    cell_count = nx * ny
    flat_coarse = coarse.reshape(cell_count)
    slot_rank = jnp.cumsum(flat_coarse, dtype=jnp.int32) - flat_coarse
    chosen = (
        (slot_rank[None, :] == jnp.arange(CAP, dtype=jnp.int32)[:, None])
        & (flat_coarse[None, :] == 1)
    ).astype(jnp.int32)
    source = jnp.sum(
        chosen * jnp.arange(cell_count, dtype=jnp.int32)[None, :], axis=1, dtype=jnp.int32
    )
    filled = jnp.sum(chosen, axis=1, dtype=jnp.int32)
    span = ny + 2
    own_i = jnp.arange(nx, dtype=jnp.int32)[:, None] + 1
    own_j = jnp.arange(ny, dtype=jnp.int32)[None, :] + 1
    up_index = jnp.stack(
        [(own_i + 2 * stencil[:, :, 0] - 1) * span + own_j,
         own_i * span + own_j + 2 * stencil[:, :, 1] - 1],
        axis=-1,
    ).reshape(cell_count, 2)
    picked = jnp.take(up_index, source, axis=0, mode="clip")
    slot_table = jnp.concatenate([source[:, None], picked, filled[:, None]], axis=1).reshape(-1)
    buffers = (from_xlo, from_xhi, from_ylo, from_yhi, corners[(1, 1)], corners[(1, -1)],
               corners[(-1, 1)], corners[(-1, -1)])
    strong, restrict = local_compute(side_cycle.reshape(-1), slot_table, fine_own, lead_own,
                                     factor_own, minus_own, buffers)
    return (strong, restrict.reshape(CAP, 14, flat))


def solution(mesh):
    placed = (P("gx", "gy", None), P("gx", "gy", None, None), P("gx", "gy", None), P("gx", "gy"))
    return jax.shard_map(
        on_device,
        mesh=mesh,
        in_specs=placed,
        out_specs=(P("gx", "gy", None), P(("gx", "gy"), None, None)),
        check_vma=False,
    )
```

```python
import math

import jax
import jax.numpy as jnp
from jax import lax
from jax.experimental import pallas as pl
from jax.experimental.pallas import tpu as pltpu
from jax.sharding import PartitionSpec as P

CAP = 12
PREC = lax.Precision.HIGH


def matmul(left_block, right_block):
    return jnp.einsum("...ij,...jk->...ik", left_block, right_block, precision=PREC)


def left_gram(left_block, right_block):
    return jnp.einsum("...ji,...jk->...ik", left_block, right_block, precision=PREC)


def right_gram(left_block, right_block):
    return jnp.einsum("...ij,...kj->...ik", left_block, right_block, precision=PREC)


def crop_cycle(values, margin):
    return values[margin : values.shape[0] - margin, margin : values.shape[1] - margin]


def upwind_pick(values, upwind_side):
    trailing = (1,) * (values.ndim - 2)
    sign_x = upwind_side[:, :, 0].reshape(upwind_side.shape[:2] + trailing)
    sign_y = upwind_side[:, :, 1].reshape(upwind_side.shape[:2] + trailing)
    upwind_x = jnp.where(sign_x == 1, values[2:, 1:-1], values[:-2, 1:-1])
    upwind_y = jnp.where(sign_y == 1, values[1:-1, 2:], values[1:-1, :-2])
    return (upwind_x, upwind_y)


def shift_pairs(count, step):
    return [(i, i + step) for i in range(count) if 0 <= i + step < count]


def corner_pairs(n_x, n_y, step_x, step_y):
    pairs = []
    for a in range(n_x):
        for b in range(n_y):
            if 0 <= a + step_x < n_x and 0 <= b + step_y < n_y:
                pairs.append((a * n_y + b, (a + step_x) * n_y + (b + step_y)))
    return pairs


def code_block(codes, order):
    values = codes.reshape(1, -1).astype(jnp.float32)
    return jnp.pad(values, ((0, order - 1), (0, order - values.shape[1])))[None]


def row_band(pieces):
    return jnp.concatenate(pieces, axis=1)


def padded(values, before_x, before_y):
    widths = [(1, 0) if before_x else (0, 1), (1, 0) if before_y else (0, 1)]
    widths += [(0, 0)] * (values.ndim - 2)
    return jnp.pad(values, widths)


def split(value):
    high = value.astype(jnp.bfloat16)
    low = (value - high.astype(jnp.float32)).astype(jnp.bfloat16)
    return high, low


def dot3(left, right, right_t=False):
    dims = (((1,), (1,)), ((), ())) if right_t else (((1,), (0,)), ((), ()))

    def one(a, b):
        return lax.dot_general(a, b, dims, preferred_element_type=jnp.float32)

    return one(left[0], right[0]) + one(left[0], right[1]) + one(left[1], right[0])


def local_kernel(side_ref, slot_ref, fine_ref, lead_ref, factor_ref, minus_ref,
                 xlo_ref, xhi_ref, ylo_ref, yhi_ref, cll_ref, clh_ref, chl_ref, chh_ref,
                 strong_ref, restrict_ref, pg, wg, gg, yg, zg):
    nx, ny = fine_ref.shape[0], fine_ref.shape[1]
    blk = fine_ref.shape[2:]
    zero = jnp.zeros(blk, jnp.float32)
    wide_x, wide_y = nx + 4, ny + 4
    pg_src, wg_src, gg_src = {}, {}, {}
    for i in range(nx):
        for j in range(ny):
            pg_src[(3 + i, 3 + j)] = (fine_ref, (i, j))
            gg_src[(1 + i, 1 + j)] = (factor_ref, (i, j))
            for e in range(2):
                wg_src[(2 + i, 2 + j, e)] = (lead_ref, (i, j, e))
    for c in range(ny):
        for r in range(3):
            pg_src[(r, 3 + c)] = (xlo_ref, (r * ny + c,))
            pg_src[(nx + 3 + r, 3 + c)] = (xhi_ref, (r * ny + c,))
        for r in range(2):
            for e in range(2):
                wg_src[(r, 2 + c, e)] = (xlo_ref, (3 * ny + (r * ny + c) * 2 + e,))
                wg_src[(nx + 2 + r, 2 + c, e)] = (xhi_ref, (3 * ny + (r * ny + c) * 2 + e,))
        gg_src[(0, 1 + c)] = (xlo_ref, (7 * ny + c,))
        gg_src[(nx + 1, 1 + c)] = (xhi_ref, (7 * ny + c,))
    for i in range(nx):
        for r in range(3):
            pg_src[(3 + i, r)] = (ylo_ref, (i * 3 + r,))
            pg_src[(3 + i, ny + 3 + r)] = (yhi_ref, (i * 3 + r,))
        for r in range(2):
            for e in range(2):
                wg_src[(2 + i, r, e)] = (ylo_ref, (3 * nx + (i * 2 + r) * 2 + e,))
                wg_src[(2 + i, ny + 2 + r, e)] = (yhi_ref, (3 * nx + (i * 2 + r) * 2 + e,))
        gg_src[(1 + i, 0)] = (ylo_ref, (7 * nx + i,))
        gg_src[(1 + i, ny + 1)] = (yhi_ref, (7 * nx + i,))
    for ref, px, py, wx, wy in ((cll_ref, 1, 1, 1, 1), (clh_ref, 1, ny + 3, 1, ny + 2),
                                (chl_ref, nx + 3, 1, nx + 2, 1),
                                (chh_ref, nx + 3, ny + 3, nx + 2, ny + 2)):
        for a in range(2):
            for b in range(2):
                pg_src[(px + a, py + b)] = (ref, (a * 2 + b,))
        for e in range(2):
            wg_src[(wx, wy, e)] = (ref, (4 + e,))
    for i in range(nx + 6):
        for j in range(ny + 6):
            ref, at = pg_src.get((i, j), (None, None))
            pg[i, j] = zero if ref is None else ref[at]
    for i in range(wide_x):
        for j in range(wide_y):
            for e in range(2):
                ref, at = wg_src.get((i, j, e), (None, None))
                wg[i, j, e] = zero if ref is None else ref[at]
    for i in range(nx + 2):
        for j in range(ny + 2):
            ref, at = gg_src.get((i, j), (None, None))
            gg[i, j] = zero if ref is None else ref[at]

    def side(i, j, d):
        return side_ref[(i * wide_y + j) * 2 + d]

    def near_step(p, carry):
        i = p // wide_y
        j = p % wide_y
        sx = side(i, j, 0)
        sy = side(i, j, 1)
        yg[i, j, 0] = dot3(split(wg[i, j, 0]), split(pg[i + 2 * sx, j + 1]))
        yg[i, j, 1] = dot3(split(wg[i, j, 1]), split(pg[i + 1, j + 2 * sy]))
        return carry

    lax.fori_loop(0, wide_x * wide_y, near_step, 0, unroll=8)

    def far_step(p, carry):
        i = p // (ny + 2)
        j = p % (ny + 2)
        zg[i, j, 0] = pg[i + 2, j + 2]
        for e in range(2):
            s = side(i + 1, j + 1, e)
            ui = i + 2 * s if e == 0 else i + 1
            uj = j + 1 if e == 0 else j + 2 * s
            lead = split(wg[i + 1, j + 1, e])
            zg[i, j, 1 + 3 * e] = dot3(lead, split(pg[ui + 1, uj + 1]))
            zg[i, j, 2 + 3 * e] = dot3(lead, split(yg[ui, uj, 0]))
            zg[i, j, 3 + 3 * e] = dot3(lead, split(yg[ui, uj, 1]))
        return carry

    lax.fori_loop(0, (nx + 2) * (ny + 2), far_step, 0, unroll=8)

    def strong_step(p, carry):
        i = p // ny
        j = p % ny
        factor = split(factor_ref[i, j])
        for d in range(2):
            s = side(i + 2, j + 2, d)
            up = gg[i + 2 * s, j + 1] if d == 0 else gg[i + 1, j + 2 * s]
            scaled = dot3(split(dot3(factor, split(minus_ref[i, j, d]))), split(up), True)
            total = jnp.sum(scaled * scaled, axis=(0, 1), keepdims=True)
            strong_ref[p * 2 + d] = jnp.broadcast_to(total * (1.0 / scaled.size), (1, 128))
        return carry

    lax.fori_loop(0, nx * ny, strong_step, 0, unroll=8)

    def slot_step(s, carry):
        cell = slot_ref[s * 4]
        weight = slot_ref[s * 4 + 3].astype(jnp.float32)
        ci = cell // ny
        cj = cell % ny
        for d in range(2):
            n = slot_ref[s * 4 + 1 + d]
            ni = n // (ny + 2)
            nj = n % (ny + 2)
            coupling = split(minus_ref[ci, cj, d])
            for w in range(7):
                row = dot3(coupling, split(zg[ni, nj, w]))
                restrict_ref[s, d * 7 + w] = (row * weight).astype(restrict_ref.dtype)
        return carry

    lax.fori_loop(0, restrict_ref.shape[0], slot_step, 0, unroll=8)


def local_compute(side_flat, slot_table, fine_own, lead_own, factor_own, minus_own, buffers):
    nx, ny = fine_own.shape[:2]
    blk = fine_own.shape[2:]
    vmem = pl.BlockSpec(memory_space=pltpu.VMEM)
    smem = pl.BlockSpec(memory_space=pltpu.SMEM)
    f32 = jnp.float32
    strong, restrict = pl.pallas_call(
        local_kernel,
        out_shape=(jax.ShapeDtypeStruct((nx * ny * 2, 1, 128), f32),
                   jax.ShapeDtypeStruct((CAP, 14) + blk, jnp.bfloat16)),
        in_specs=[smem, smem] + [vmem] * (4 + len(buffers)),
        out_specs=(vmem, vmem),
        scratch_shapes=[
            pltpu.VMEM((nx + 6, ny + 6) + blk, f32),
            pltpu.VMEM((nx + 4, ny + 4, 2) + blk, f32),
            pltpu.VMEM((nx + 2, ny + 2) + blk, f32),
            pltpu.VMEM((nx + 4, ny + 4, 2) + blk, f32),
            pltpu.VMEM((nx + 2, ny + 2, 7) + blk, f32),
        ],
        compiler_params=pltpu.CompilerParams(vmem_limit_bytes=60 * 1024 * 1024),
    )(side_flat, slot_table, fine_own, lead_own, factor_own, minus_own, *buffers)
    return strong[:, 0, 0].reshape(nx, ny, 2), restrict


def on_device(inv_factors, couplings, stencil, coarse):
    nx, ny, flat = inv_factors.shape
    order = math.isqrt(flat)
    blk = (order, order)
    n_gx = lax.axis_size("gx")
    n_gy = lax.axis_size("gy")
    total_x = nx * n_gx
    total_y = ny * n_gy
    coord_x = lax.axis_index("gx") * nx + jnp.arange(nx, dtype=jnp.int32)
    coord_y = lax.axis_index("gy") * ny + jnp.arange(ny, dtype=jnp.int32)
    target_x = coord_x[:, None] + 2 * stencil[:, :, 0] - 1
    target_y = coord_y[None, :] + 2 * stencil[:, :, 1] - 1
    reach = jnp.stack(
        [(target_x >= 0) & (target_x < total_x), (target_y >= 0) & (target_y < total_y)], axis=-1
    )
    minus_own = (couplings * (-reach.astype(jnp.float32))[:, :, :, None]).reshape(
        (nx, ny, 2) + blk
    )
    factor_own = inv_factors.reshape((nx, ny) + blk)
    fine_own = (1 - coarse).astype(jnp.float32)[:, :, None, None] * left_gram(
        factor_own, factor_own
    )
    lead_own = matmul(fine_own[:, :, None], minus_own)

    def face(rows, cols):
        return jnp.concatenate(
            [
                fine_own[rows[3], cols[3]].reshape((-1,) + blk),
                lead_own[rows[2], cols[2]].reshape((-1,) + blk),
                factor_own[rows[1], cols[1]].reshape((-1,) + blk),
                code_block(stencil[rows[2], cols[2]], order),
            ],
            axis=0,
        )

    every = {d: slice(None) for d in (1, 2, 3)}
    low = {d: slice(0, d) for d in (1, 2, 3)}
    high_x = {d: slice(nx - d, nx) for d in (1, 2, 3)}
    high_y = {d: slice(ny - d, ny) for d in (1, 2, 3)}
    sends = [
        (face(high_x, every), "gx", shift_pairs(n_gx, 1)),
        (face(low, every), "gx", shift_pairs(n_gx, -1)),
        (face(every, high_y), "gy", shift_pairs(n_gy, 1)),
        (face(every, low), "gy", shift_pairs(n_gy, -1)),
    ]
    steps = ((1, 1), (1, -1), (-1, 1), (-1, -1))
    for sx, sy in steps:
        rows2 = slice(nx - 2, nx) if sx == 1 else slice(0, 2)
        cols2 = slice(ny - 2, ny) if sy == 1 else slice(0, 2)
        row1 = nx - 1 if sx == 1 else 0
        col1 = ny - 1 if sy == 1 else 0
        buffer = jnp.concatenate(
            [
                fine_own[rows2, cols2].reshape((-1,) + blk),
                lead_own[row1, col1],
                code_block(stencil[row1, col1], order),
            ],
            axis=0,
        )
        sends.append((buffer, ("gx", "gy"), corner_pairs(n_gx, n_gy, sx, sy)))
    ready = lax.optimization_barrier(tuple(buffer for buffer, _, _ in sends))
    arrived = [lax.ppermute(buffer, axis, pairs)
               for buffer, (_, axis, pairs) in zip(ready, sends)]
    from_xlo, from_xhi, from_ylo, from_yhi = arrived[:4]
    corners = dict(zip(steps, arrived[4:]))

    def unpack_face(buffer, count, along_x):
        n_p, n_w = 3 * count, 2 * count * 2
        p_part = buffer[0:n_p]
        w_part = buffer[n_p : n_p + n_w]
        g_part = buffer[n_p + n_w : n_p + n_w + count]
        codes = buffer[n_p + n_w + count, 0, 0 : 2 * count * 2].astype(jnp.int32)
        if along_x:
            return (p_part.reshape((3, count) + blk), w_part.reshape((2, count, 2) + blk),
                    g_part.reshape((1, count) + blk), codes.reshape(2, count, 2))
        return (p_part.reshape((count, 3) + blk), w_part.reshape((count, 2, 2) + blk),
                g_part.reshape((count, 1) + blk), codes.reshape(count, 2, 2))

    pxl, wxl, gxl, cxl = unpack_face(from_xlo, ny, True)
    pxh, wxh, gxh, cxh = unpack_face(from_xhi, ny, True)
    pyl, wyl, gyl, cyl = unpack_face(from_ylo, nx, False)
    pyh, wyh, gyh, cyh = unpack_face(from_yhi, nx, False)

    def unpack_corner(buffer):
        return (buffer[0:4].reshape((2, 2) + blk), buffer[4:6].reshape((1, 1, 2) + blk),
                buffer[6, 0, 0:2].astype(jnp.int32).reshape(1, 1, 2))

    c_ll = unpack_corner(corners[(1, 1)])
    c_lh = unpack_corner(corners[(1, -1)])
    c_hl = unpack_corner(corners[(-1, 1)])
    c_hh = unpack_corner(corners[(-1, -1)])

    def cycle(k, lo_x, own, hi_x, lo_y, hi_y):
        return jnp.concatenate(
            [
                row_band([padded(c_ll[k], True, True), lo_x, padded(c_lh[k], True, False)]),
                row_band([lo_y, own, hi_y]),
                row_band([padded(c_hl[k], False, True), hi_x, padded(c_hh[k], False, False)]),
            ],
            axis=0,
        )

    side_cycle = cycle(2, cxl, stencil, cxh, cyl, cyh)

    cell_count = nx * ny
    flat_coarse = coarse.reshape(cell_count)
    slot_rank = jnp.cumsum(flat_coarse, dtype=jnp.int32) - flat_coarse
    chosen = (
        (slot_rank[None, :] == jnp.arange(CAP, dtype=jnp.int32)[:, None])
        & (flat_coarse[None, :] == 1)
    ).astype(jnp.int32)
    source = jnp.sum(
        chosen * jnp.arange(cell_count, dtype=jnp.int32)[None, :], axis=1, dtype=jnp.int32
    )
    filled = jnp.sum(chosen, axis=1, dtype=jnp.int32)
    span = ny + 2
    own_i = jnp.arange(nx, dtype=jnp.int32)[:, None] + 1
    own_j = jnp.arange(ny, dtype=jnp.int32)[None, :] + 1
    up_index = jnp.stack(
        [(own_i + 2 * stencil[:, :, 0] - 1) * span + own_j,
         own_i * span + own_j + 2 * stencil[:, :, 1] - 1],
        axis=-1,
    ).reshape(cell_count, 2)
    picked = jnp.take(up_index, source, axis=0, mode="clip")
    slot_table = jnp.concatenate([source[:, None], picked, filled[:, None]], axis=1).reshape(-1)
    buffers = (from_xlo, from_xhi, from_ylo, from_yhi, corners[(1, 1)], corners[(1, -1)],
               corners[(-1, 1)], corners[(-1, -1)])
    strong, restrict = local_compute(side_cycle.reshape(-1), slot_table, fine_own, lead_own,
                                     factor_own, minus_own, buffers)
    return (strong, restrict.reshape(CAP, 14, flat))


def solution(mesh):
    placed = (P("gx", "gy", None), P("gx", "gy", None, None), P("gx", "gy", None), P("gx", "gy"))
    return jax.shard_map(
        on_device,
        mesh=mesh,
        in_specs=placed,
        out_specs=(P("gx", "gy", None), P(("gx", "gy"), None, None)),
        check_vma=False,
    )
```

```python
import math

import jax
import jax.numpy as jnp
from jax import lax
from jax.experimental import pallas as pl
from jax.experimental.pallas import tpu as pltpu
from jax.sharding import PartitionSpec as P

CAP = 12
PREC = lax.Precision.HIGH


def matmul(left_block, right_block):
    return jnp.einsum("...ij,...jk->...ik", left_block, right_block, precision=PREC)


def left_gram(left_block, right_block):
    return jnp.einsum("...ji,...jk->...ik", left_block, right_block, precision=PREC)


def right_gram(left_block, right_block):
    return jnp.einsum("...ij,...kj->...ik", left_block, right_block, precision=PREC)


def crop_cycle(values, margin):
    return values[margin : values.shape[0] - margin, margin : values.shape[1] - margin]


def upwind_pick(values, upwind_side):
    trailing = (1,) * (values.ndim - 2)
    sign_x = upwind_side[:, :, 0].reshape(upwind_side.shape[:2] + trailing)
    sign_y = upwind_side[:, :, 1].reshape(upwind_side.shape[:2] + trailing)
    upwind_x = jnp.where(sign_x == 1, values[2:, 1:-1], values[:-2, 1:-1])
    upwind_y = jnp.where(sign_y == 1, values[1:-1, 2:], values[1:-1, :-2])
    return (upwind_x, upwind_y)


def shift_pairs(count, step):
    return [(i, i + step) for i in range(count) if 0 <= i + step < count]


def corner_pairs(n_x, n_y, step_x, step_y):
    pairs = []
    for a in range(n_x):
        for b in range(n_y):
            if 0 <= a + step_x < n_x and 0 <= b + step_y < n_y:
                pairs.append((a * n_y + b, (a + step_x) * n_y + (b + step_y)))
    return pairs


def code_block(codes, order):
    values = codes.reshape(1, -1).astype(jnp.float32)
    return jnp.pad(values, ((0, order - 1), (0, order - values.shape[1])))[None]


def row_band(pieces):
    return jnp.concatenate(pieces, axis=1)


def padded(values, before_x, before_y):
    widths = [(1, 0) if before_x else (0, 1), (1, 0) if before_y else (0, 1)]
    widths += [(0, 0)] * (values.ndim - 2)
    return jnp.pad(values, widths)


def split(value):
    high = value.astype(jnp.bfloat16)
    low = (value - high.astype(jnp.float32)).astype(jnp.bfloat16)
    return high, low


def dot3(left, right, right_t=False):
    dims = (((1,), (1,)), ((), ())) if right_t else (((1,), (0,)), ((), ()))

    def one(a, b):
        return lax.dot_general(a, b, dims, preferred_element_type=jnp.float32)

    return one(left[0], right[0]) + one(left[0], right[1]) + one(left[1], right[0])


def local_kernel(side_ref, slot_ref, fine_ref, lead_ref, factor_ref, minus_ref,
                 xlo_ref, xhi_ref, ylo_ref, yhi_ref, cll_ref, clh_ref, chl_ref, chh_ref,
                 strong_ref, restrict_ref, pg, wg, gg, yg, zg):
    nx, ny = fine_ref.shape[0], fine_ref.shape[1]
    blk = fine_ref.shape[2:]
    zero = jnp.zeros(blk, jnp.float32)
    wide_x, wide_y = nx + 4, ny + 4
    pg_src, wg_src, gg_src = {}, {}, {}
    for i in range(nx):
        for j in range(ny):
            pg_src[(3 + i, 3 + j)] = (fine_ref, (i, j))
            gg_src[(1 + i, 1 + j)] = (factor_ref, (i, j))
            for e in range(2):
                wg_src[(2 + i, 2 + j, e)] = (lead_ref, (i, j, e))
    for c in range(ny):
        for r in range(3):
            pg_src[(r, 3 + c)] = (xlo_ref, (r * ny + c,))
            pg_src[(nx + 3 + r, 3 + c)] = (xhi_ref, (r * ny + c,))
        for r in range(2):
            for e in range(2):
                wg_src[(r, 2 + c, e)] = (xlo_ref, (3 * ny + (r * ny + c) * 2 + e,))
                wg_src[(nx + 2 + r, 2 + c, e)] = (xhi_ref, (3 * ny + (r * ny + c) * 2 + e,))
        gg_src[(0, 1 + c)] = (xlo_ref, (7 * ny + c,))
        gg_src[(nx + 1, 1 + c)] = (xhi_ref, (7 * ny + c,))
    for i in range(nx):
        for r in range(3):
            pg_src[(3 + i, r)] = (ylo_ref, (i * 3 + r,))
            pg_src[(3 + i, ny + 3 + r)] = (yhi_ref, (i * 3 + r,))
        for r in range(2):
            for e in range(2):
                wg_src[(2 + i, r, e)] = (ylo_ref, (3 * nx + (i * 2 + r) * 2 + e,))
                wg_src[(2 + i, ny + 2 + r, e)] = (yhi_ref, (3 * nx + (i * 2 + r) * 2 + e,))
        gg_src[(1 + i, 0)] = (ylo_ref, (7 * nx + i,))
        gg_src[(1 + i, ny + 1)] = (yhi_ref, (7 * nx + i,))
    for ref, px, py, wx, wy in ((cll_ref, 1, 1, 1, 1), (clh_ref, 1, ny + 3, 1, ny + 2),
                                (chl_ref, nx + 3, 1, nx + 2, 1),
                                (chh_ref, nx + 3, ny + 3, nx + 2, ny + 2)):
        for a in range(2):
            for b in range(2):
                pg_src[(px + a, py + b)] = (ref, (a * 2 + b,))
        for e in range(2):
            wg_src[(wx, wy, e)] = (ref, (4 + e,))
    def block(ref, at):
        if ref is None:
            return zero
        if len(at) == 1 and ref.shape[-1] == 2 * blk[-1]:
            half = at[0] % 2
            return ref[at[0] // 2, :, half * blk[-1] : (half + 1) * blk[-1]]
        return ref[at]

    for i in range(nx + 6):
        for j in range(ny + 6):
            pg[i, j] = block(*pg_src.get((i, j), (None, None)))
    for i in range(wide_x):
        for j in range(wide_y):
            for e in range(2):
                wg[i, j, e] = block(*wg_src.get((i, j, e), (None, None)))
    for i in range(nx + 2):
        for j in range(ny + 2):
            gg[i, j] = block(*gg_src.get((i, j), (None, None)))

    def side(i, j, d):
        return side_ref[(i * wide_y + j) * 2 + d]

    def near_step(p, carry):
        i = p // wide_y
        j = p % wide_y
        sx = side(i, j, 0)
        sy = side(i, j, 1)
        yg[i, j, 0] = dot3(split(wg[i, j, 0]), split(pg[i + 2 * sx, j + 1]))
        yg[i, j, 1] = dot3(split(wg[i, j, 1]), split(pg[i + 1, j + 2 * sy]))
        return carry

    lax.fori_loop(0, wide_x * wide_y, near_step, 0, unroll=8)

    def far_step(p, carry):
        i = p // (ny + 2)
        j = p % (ny + 2)
        zg[i, j, 0] = pg[i + 2, j + 2]
        for e in range(2):
            s = side(i + 1, j + 1, e)
            ui = i + 2 * s if e == 0 else i + 1
            uj = j + 1 if e == 0 else j + 2 * s
            lead = split(wg[i + 1, j + 1, e])
            zg[i, j, 1 + 3 * e] = dot3(lead, split(pg[ui + 1, uj + 1]))
            zg[i, j, 2 + 3 * e] = dot3(lead, split(yg[ui, uj, 0]))
            zg[i, j, 3 + 3 * e] = dot3(lead, split(yg[ui, uj, 1]))
        return carry

    lax.fori_loop(0, (nx + 2) * (ny + 2), far_step, 0, unroll=8)

    def strong_step(p, carry):
        i = p // ny
        j = p % ny
        factor = split(factor_ref[i, j])
        for d in range(2):
            s = side(i + 2, j + 2, d)
            up = gg[i + 2 * s, j + 1] if d == 0 else gg[i + 1, j + 2 * s]
            scaled = dot3(split(dot3(factor, split(minus_ref[i, j, d]))), split(up), True)
            total = jnp.sum(scaled * scaled, axis=(0, 1), keepdims=True)
            strong_ref[p * 2 + d] = jnp.broadcast_to(total * (1.0 / scaled.size), (1, 128))
        return carry

    lax.fori_loop(0, nx * ny, strong_step, 0, unroll=8)

    def slot_step(s, carry):
        cell = slot_ref[s * 4]
        weight = slot_ref[s * 4 + 3].astype(jnp.float32)
        ci = cell // ny
        cj = cell % ny
        for d in range(2):
            n = slot_ref[s * 4 + 1 + d]
            ni = n // (ny + 2)
            nj = n % (ny + 2)
            coupling = split(minus_ref[ci, cj, d])
            for w in range(7):
                row = dot3(coupling, split(zg[ni, nj, w]))
                restrict_ref[s, d * 7 + w] = (row * weight).astype(restrict_ref.dtype)
        return carry

    lax.fori_loop(0, restrict_ref.shape[0], slot_step, 0, unroll=8)


def local_compute(side_flat, slot_table, fine_own, lead_own, factor_own, minus_own, buffers):
    nx, ny = fine_own.shape[:2]
    blk = fine_own.shape[2:]
    vmem = pl.BlockSpec(memory_space=pltpu.VMEM)
    smem = pl.BlockSpec(memory_space=pltpu.SMEM)
    f32 = jnp.float32
    strong, restrict = pl.pallas_call(
        local_kernel,
        out_shape=(jax.ShapeDtypeStruct((nx * ny * 2, 1, 128), f32),
                   jax.ShapeDtypeStruct((CAP, 14) + blk, jnp.bfloat16)),
        in_specs=[smem, smem] + [vmem] * (4 + len(buffers)),
        out_specs=(vmem, vmem),
        scratch_shapes=[
            pltpu.VMEM((nx + 6, ny + 6) + blk, f32),
            pltpu.VMEM((nx + 4, ny + 4, 2) + blk, f32),
            pltpu.VMEM((nx + 2, ny + 2) + blk, f32),
            pltpu.VMEM((nx + 4, ny + 4, 2) + blk, f32),
            pltpu.VMEM((nx + 2, ny + 2, 7) + blk, f32),
        ],
        compiler_params=pltpu.CompilerParams(vmem_limit_bytes=60 * 1024 * 1024),
    )(side_flat, slot_table, fine_own, lead_own, factor_own, minus_own, *buffers)
    return strong[:, 0, 0].reshape(nx, ny, 2), restrict


def on_device(inv_factors, couplings, stencil, coarse):
    nx, ny, flat = inv_factors.shape
    order = math.isqrt(flat)
    blk = (order, order)
    n_gx = lax.axis_size("gx")
    n_gy = lax.axis_size("gy")
    total_x = nx * n_gx
    total_y = ny * n_gy
    coord_x = lax.axis_index("gx") * nx + jnp.arange(nx, dtype=jnp.int32)
    coord_y = lax.axis_index("gy") * ny + jnp.arange(ny, dtype=jnp.int32)
    target_x = coord_x[:, None] + 2 * stencil[:, :, 0] - 1
    target_y = coord_y[None, :] + 2 * stencil[:, :, 1] - 1
    reach = jnp.stack(
        [(target_x >= 0) & (target_x < total_x), (target_y >= 0) & (target_y < total_y)], axis=-1
    )
    minus_own = (couplings * (-reach.astype(jnp.float32))[:, :, :, None]).reshape(
        (nx, ny, 2) + blk
    )
    factor_own = inv_factors.reshape((nx, ny) + blk)
    fine_own = (1 - coarse).astype(jnp.float32)[:, :, None, None] * left_gram(
        factor_own, factor_own
    )
    lead_own = matmul(fine_own[:, :, None], minus_own)

    def face(rows, cols):
        return jnp.concatenate(
            [
                fine_own[rows[3], cols[3]].reshape((-1,) + blk),
                lead_own[rows[2], cols[2]].reshape((-1,) + blk),
                factor_own[rows[1], cols[1]].reshape((-1,) + blk),
                code_block(stencil[rows[2], cols[2]], order),
            ],
            axis=0,
        )

    every = {d: slice(None) for d in (1, 2, 3)}
    low = {d: slice(0, d) for d in (1, 2, 3)}
    high_x = {d: slice(nx - d, nx) for d in (1, 2, 3)}
    high_y = {d: slice(ny - d, ny) for d in (1, 2, 3)}
    def paired(buffer):
        count = buffer.shape[0]
        if count % 2:
            buffer = jnp.concatenate([buffer, jnp.zeros((1,) + blk, buffer.dtype)], axis=0)
        halves = buffer.reshape((-1, 2) + blk)
        return jnp.concatenate([halves[:, 0], halves[:, 1]], axis=-1)

    from_xlo = lax.ppermute(paired(face(high_x, every)), "gx", shift_pairs(n_gx, 1))
    from_xhi = lax.ppermute(paired(face(low, every)), "gx", shift_pairs(n_gx, -1))
    from_ylo = lax.ppermute(paired(face(every, high_y)), "gy", shift_pairs(n_gy, 1))
    from_yhi = lax.ppermute(paired(face(every, low)), "gy", shift_pairs(n_gy, -1))

    corners = {}
    for sx in (1, -1):
        for sy in (1, -1):
            rows2 = slice(nx - 2, nx) if sx == 1 else slice(0, 2)
            cols2 = slice(ny - 2, ny) if sy == 1 else slice(0, 2)
            row1 = nx - 1 if sx == 1 else 0
            col1 = ny - 1 if sy == 1 else 0
            buffer = jnp.concatenate(
                [
                    fine_own[rows2, cols2].reshape((-1,) + blk),
                    lead_own[row1, col1],
                    code_block(stencil[row1, col1], order),
                ],
                axis=0,
            )
            corners[(sx, sy)] = lax.ppermute(
                buffer, ("gx", "gy"), corner_pairs(n_gx, n_gy, sx, sy)
            )

    def face_codes(buffer, count, along_x):
        at = 3 * count + 2 * count * 2 + count
        codes = buffer[at // 2, 0, (at % 2) * order : (at % 2) * order + 2 * count * 2]
        codes = codes.astype(jnp.int32)
        return codes.reshape((2, count, 2) if along_x else (count, 2, 2))

    cxl = face_codes(from_xlo, ny, True)
    cxh = face_codes(from_xhi, ny, True)
    cyl = face_codes(from_ylo, nx, False)
    cyh = face_codes(from_yhi, nx, False)

    def unpack_corner(buffer):
        return (buffer[0:4].reshape((2, 2) + blk), buffer[4:6].reshape((1, 1, 2) + blk),
                buffer[6, 0, 0:2].astype(jnp.int32).reshape(1, 1, 2))

    c_ll = unpack_corner(corners[(1, 1)])
    c_lh = unpack_corner(corners[(1, -1)])
    c_hl = unpack_corner(corners[(-1, 1)])
    c_hh = unpack_corner(corners[(-1, -1)])

    def cycle(k, lo_x, own, hi_x, lo_y, hi_y):
        return jnp.concatenate(
            [
                row_band([padded(c_ll[k], True, True), lo_x, padded(c_lh[k], True, False)]),
                row_band([lo_y, own, hi_y]),
                row_band([padded(c_hl[k], False, True), hi_x, padded(c_hh[k], False, False)]),
            ],
            axis=0,
        )

    side_cycle = cycle(2, cxl, stencil, cxh, cyl, cyh)

    cell_count = nx * ny
    flat_coarse = coarse.reshape(cell_count)
    slot_rank = jnp.cumsum(flat_coarse, dtype=jnp.int32) - flat_coarse
    chosen = (
        (slot_rank[None, :] == jnp.arange(CAP, dtype=jnp.int32)[:, None])
        & (flat_coarse[None, :] == 1)
    ).astype(jnp.int32)
    source = jnp.sum(
        chosen * jnp.arange(cell_count, dtype=jnp.int32)[None, :], axis=1, dtype=jnp.int32
    )
    filled = jnp.sum(chosen, axis=1, dtype=jnp.int32)
    span = ny + 2
    own_i = jnp.arange(nx, dtype=jnp.int32)[:, None] + 1
    own_j = jnp.arange(ny, dtype=jnp.int32)[None, :] + 1
    up_index = jnp.stack(
        [(own_i + 2 * stencil[:, :, 0] - 1) * span + own_j,
         own_i * span + own_j + 2 * stencil[:, :, 1] - 1],
        axis=-1,
    ).reshape(cell_count, 2)
    picked = jnp.take(up_index, source, axis=0, mode="clip")
    slot_table = jnp.concatenate([source[:, None], picked, filled[:, None]], axis=1).reshape(-1)
    buffers = (from_xlo, from_xhi, from_ylo, from_yhi, corners[(1, 1)], corners[(1, -1)],
               corners[(-1, 1)], corners[(-1, -1)])
    strong, restrict = local_compute(side_cycle.reshape(-1), slot_table, fine_own, lead_own,
                                     factor_own, minus_own, buffers)
    return (strong, restrict.reshape(CAP, 14, flat))


def solution(mesh):
    placed = (P("gx", "gy", None), P("gx", "gy", None, None), P("gx", "gy", None), P("gx", "gy"))
    return jax.shard_map(
        on_device,
        mesh=mesh,
        in_specs=placed,
        out_specs=(P("gx", "gy", None), P(("gx", "gy"), None, None)),
        check_vma=False,
    )
```

```python
import math

import jax
import jax.numpy as jnp
from jax import lax
from jax.experimental import pallas as pl
from jax.experimental.pallas import tpu as pltpu
from jax.sharding import PartitionSpec as P

CAP = 12
PREC = lax.Precision.HIGH


def matmul(left_block, right_block):
    return jnp.einsum("...ij,...jk->...ik", left_block, right_block, precision=PREC)


def left_gram(left_block, right_block):
    return jnp.einsum("...ji,...jk->...ik", left_block, right_block, precision=PREC)


def right_gram(left_block, right_block):
    return jnp.einsum("...ij,...kj->...ik", left_block, right_block, precision=PREC)


def crop_cycle(values, margin):
    return values[margin : values.shape[0] - margin, margin : values.shape[1] - margin]


def upwind_pick(values, upwind_side):
    trailing = (1,) * (values.ndim - 2)
    sign_x = upwind_side[:, :, 0].reshape(upwind_side.shape[:2] + trailing)
    sign_y = upwind_side[:, :, 1].reshape(upwind_side.shape[:2] + trailing)
    upwind_x = jnp.where(sign_x == 1, values[2:, 1:-1], values[:-2, 1:-1])
    upwind_y = jnp.where(sign_y == 1, values[1:-1, 2:], values[1:-1, :-2])
    return (upwind_x, upwind_y)


def shift_pairs(count, step):
    return [(i, i + step) for i in range(count) if 0 <= i + step < count]


def corner_pairs(n_x, n_y, step_x, step_y):
    pairs = []
    for a in range(n_x):
        for b in range(n_y):
            if 0 <= a + step_x < n_x and 0 <= b + step_y < n_y:
                pairs.append((a * n_y + b, (a + step_x) * n_y + (b + step_y)))
    return pairs


def code_block(codes, order):
    values = codes.reshape(1, -1).astype(jnp.float32)
    return jnp.pad(values, ((0, order - 1), (0, order - values.shape[1])))[None]


def row_band(pieces):
    return jnp.concatenate(pieces, axis=1)


def padded(values, before_x, before_y):
    widths = [(1, 0) if before_x else (0, 1), (1, 0) if before_y else (0, 1)]
    widths += [(0, 0)] * (values.ndim - 2)
    return jnp.pad(values, widths)


def split(value):
    high = value.astype(jnp.bfloat16)
    low = (value - high.astype(jnp.float32)).astype(jnp.bfloat16)
    return high, low


def dot3(left, right, right_t=False):
    dims = (((1,), (1,)), ((), ())) if right_t else (((1,), (0,)), ((), ()))

    def one(a, b):
        return lax.dot_general(a, b, dims, preferred_element_type=jnp.float32)

    return one(left[0], right[0]) + one(left[0], right[1]) + one(left[1], right[0])


def local_kernel(side_ref, slot_ref, fine_ref, lead_ref, factor_ref, minus_ref,
                 xlo_ref, xhi_ref, ylo_ref, yhi_ref, cll_ref, clh_ref, chl_ref, chh_ref,
                 strong_ref, restrict_ref, pg, wg, gg, yg, zg):
    nx, ny = fine_ref.shape[0], fine_ref.shape[1]
    blk = fine_ref.shape[2:]
    zero = jnp.zeros(blk, jnp.float32)
    wide_x, wide_y = nx + 4, ny + 4
    pg_src, wg_src, gg_src = {}, {}, {}
    for i in range(nx):
        for j in range(ny):
            pg_src[(3 + i, 3 + j)] = (fine_ref, (i, j))
            gg_src[(1 + i, 1 + j)] = (factor_ref, (i, j))
            for e in range(2):
                wg_src[(2 + i, 2 + j, e)] = (lead_ref, (i, j, e))
    for c in range(ny):
        for r in range(3):
            pg_src[(r, 3 + c)] = (xlo_ref, (r * ny + c,))
            pg_src[(nx + 3 + r, 3 + c)] = (xhi_ref, (r * ny + c,))
        for r in range(2):
            for e in range(2):
                wg_src[(r, 2 + c, e)] = (xlo_ref, (3 * ny + (r * ny + c) * 2 + e,))
                wg_src[(nx + 2 + r, 2 + c, e)] = (xhi_ref, (3 * ny + (r * ny + c) * 2 + e,))
        gg_src[(0, 1 + c)] = (xlo_ref, (7 * ny + c,))
        gg_src[(nx + 1, 1 + c)] = (xhi_ref, (7 * ny + c,))
    for i in range(nx):
        for r in range(3):
            pg_src[(3 + i, r)] = (ylo_ref, (i * 3 + r,))
            pg_src[(3 + i, ny + 3 + r)] = (yhi_ref, (i * 3 + r,))
        for r in range(2):
            for e in range(2):
                wg_src[(2 + i, r, e)] = (ylo_ref, (3 * nx + (i * 2 + r) * 2 + e,))
                wg_src[(2 + i, ny + 2 + r, e)] = (yhi_ref, (3 * nx + (i * 2 + r) * 2 + e,))
        gg_src[(1 + i, 0)] = (ylo_ref, (7 * nx + i,))
        gg_src[(1 + i, ny + 1)] = (yhi_ref, (7 * nx + i,))
    for ref, px, py, wx, wy in ((cll_ref, 1, 1, 1, 1), (clh_ref, 1, ny + 3, 1, ny + 2),
                                (chl_ref, nx + 3, 1, nx + 2, 1),
                                (chh_ref, nx + 3, ny + 3, nx + 2, ny + 2)):
        for a in range(2):
            for b in range(2):
                pg_src[(px + a, py + b)] = (ref, (a * 2 + b,))
        for e in range(2):
            wg_src[(wx, wy, e)] = (ref, (4 + e,))
    def block(ref, at):
        if ref is None:
            return zero
        if len(at) == 1 and ref.shape[-1] == 2 * blk[-1]:
            half = at[0] % 2
            return ref[at[0] // 2, :, half * blk[-1] : (half + 1) * blk[-1]]
        return ref[at]

    for i in range(nx + 6):
        for j in range(ny + 6):
            pg[i, j] = block(*pg_src.get((i, j), (None, None)))
    for i in range(wide_x):
        for j in range(wide_y):
            for e in range(2):
                wg[i, j, e] = block(*wg_src.get((i, j, e), (None, None)))
    for i in range(nx + 2):
        for j in range(ny + 2):
            gg[i, j] = block(*gg_src.get((i, j), (None, None)))

    def side(i, j, d):
        return side_ref[(i * wide_y + j) * 2 + d]

    def near_step(p, carry):
        i = p // wide_y
        j = p % wide_y
        sx = side(i, j, 0)
        sy = side(i, j, 1)
        yg[i, j, 0] = dot3(split(wg[i, j, 0]), split(pg[i + 2 * sx, j + 1]))
        yg[i, j, 1] = dot3(split(wg[i, j, 1]), split(pg[i + 1, j + 2 * sy]))
        return carry

    lax.fori_loop(0, wide_x * wide_y, near_step, 0, unroll=8)

    def far_step(p, carry):
        i = p // (ny + 2)
        j = p % (ny + 2)
        zg[i, j, 0] = pg[i + 2, j + 2]
        for e in range(2):
            s = side(i + 1, j + 1, e)
            ui = i + 2 * s if e == 0 else i + 1
            uj = j + 1 if e == 0 else j + 2 * s
            lead = split(wg[i + 1, j + 1, e])
            zg[i, j, 1 + 3 * e] = dot3(lead, split(pg[ui + 1, uj + 1]))
            zg[i, j, 2 + 3 * e] = dot3(lead, split(yg[ui, uj, 0]))
            zg[i, j, 3 + 3 * e] = dot3(lead, split(yg[ui, uj, 1]))
        return carry

    lax.fori_loop(0, (nx + 2) * (ny + 2), far_step, 0, unroll=8)

    def strong_step(p, carry):
        i = p // ny
        j = p % ny
        factor = split(factor_ref[i, j])
        for d in range(2):
            s = side(i + 2, j + 2, d)
            up = gg[i + 2 * s, j + 1] if d == 0 else gg[i + 1, j + 2 * s]
            scaled = dot3(split(dot3(factor, split(minus_ref[i, j, d]))), split(up), True)
            total = jnp.sum(scaled * scaled, axis=(0, 1), keepdims=True)
            strong_ref[p * 2 + d] = jnp.broadcast_to(total * (1.0 / scaled.size), (1, 128))
        return carry

    lax.fori_loop(0, nx * ny, strong_step, 0, unroll=8)

    def slot_step(s, carry):
        cell = slot_ref[s * 4]
        weight = slot_ref[s * 4 + 3].astype(jnp.float32)
        ci = cell // ny
        cj = cell % ny
        for d in range(2):
            n = slot_ref[s * 4 + 1 + d]
            ni = n // (ny + 2)
            nj = n % (ny + 2)
            coupling = split(minus_ref[ci, cj, d])
            for w in range(7):
                row = dot3(coupling, split(zg[ni, nj, w]))
                restrict_ref[s, d * 7 + w] = (row * weight).astype(restrict_ref.dtype)
        return carry

    lax.fori_loop(0, restrict_ref.shape[0], slot_step, 0, unroll=8)


def face_sources(nx, ny, side):
    sources = []
    if side in ("xhi", "xlo"):
        rows = {d: (range(nx - d, nx) if side == "xhi" else range(d)) for d in (1, 2, 3)}
        for r in rows[3]:
            for c in range(ny):
                sources.append(("fine", (r, c)))
        for r in rows[2]:
            for c in range(ny):
                for e in range(2):
                    sources.append(("lead", (r, c, e)))
        for r in rows[1]:
            for c in range(ny):
                sources.append(("factor", (r, c)))
        codes = [(r, c, e) for r in rows[2] for c in range(ny) for e in range(2)]
    else:
        cols = {d: (range(ny - d, ny) if side == "yhi" else range(d)) for d in (1, 2, 3)}
        for i in range(nx):
            for r in cols[3]:
                sources.append(("fine", (i, r)))
        for i in range(nx):
            for r in cols[2]:
                for e in range(2):
                    sources.append(("lead", (i, r, e)))
        for i in range(nx):
            for r in cols[1]:
                sources.append(("factor", (i, r)))
        codes = [(i, r, e) for i in range(nx) for r in cols[2] for e in range(2)]
    return sources, codes


def code_tile(side_ref, codes, ny, shape):
    rows = lax.broadcasted_iota(jnp.int32, shape, 0)
    lanes = lax.broadcasted_iota(jnp.int32, shape, 1)
    tile = jnp.zeros(shape, jnp.float32)
    for k, (i, j, e) in enumerate(codes):
        value = side_ref[(i * ny + j) * 2 + e].astype(jnp.float32)
        tile = jnp.where((rows == 0) & (lanes == k), value, tile)
    return tile


def pack_kernel(side_ref, fine_ref, lead_ref, factor_ref, *out_refs):
    nx, ny = fine_ref.shape[0], fine_ref.shape[1]
    width = fine_ref.shape[-1]
    named = {"fine": fine_ref, "lead": lead_ref, "factor": factor_ref}
    for out, side in zip(out_refs[:4], ("xhi", "xlo", "yhi", "ylo")):
        sources, codes = face_sources(nx, ny, side)
        for k, (name, at) in enumerate(sources):
            out[k // 2, :, (k % 2) * width : (k % 2 + 1) * width] = named[name][at]
        last = len(sources)
        out[last // 2] = code_tile(side_ref, codes, ny, out.shape[1:])
    for out, (sx, sy) in zip(out_refs[4:], ((1, 1), (1, -1), (-1, 1), (-1, -1))):
        rows2 = range(nx - 2, nx) if sx == 1 else range(2)
        cols2 = range(ny - 2, ny) if sy == 1 else range(2)
        row1 = nx - 1 if sx == 1 else 0
        col1 = ny - 1 if sy == 1 else 0
        k = 0
        for a in rows2:
            for b in cols2:
                out[k] = fine_ref[a, b]
                k += 1
        for e in range(2):
            out[4 + e] = lead_ref[row1, col1, e]
        out[6] = code_tile(side_ref, [(row1, col1, 0), (row1, col1, 1)], ny, out.shape[1:])


def pack_buffers(stencil, fine_own, lead_own, factor_own):
    nx, ny = fine_own.shape[:2]
    blk = fine_own.shape[2:]
    face_count = len(face_sources(nx, ny, "xhi")[0]) + 1
    face_y_count = len(face_sources(nx, ny, "yhi")[0]) + 1
    vmem = pl.BlockSpec(memory_space=pltpu.VMEM)
    smem = pl.BlockSpec(memory_space=pltpu.SMEM)
    paired = lambda count: jax.ShapeDtypeStruct(((count + 1) // 2, blk[0], 2 * blk[1]), jnp.float32)
    shapes = [paired(face_count)] * 2 + [paired(face_y_count)] * 2
    shapes += [jax.ShapeDtypeStruct((7,) + blk, jnp.float32)] * 4
    return pl.pallas_call(
        pack_kernel,
        out_shape=tuple(shapes),
        in_specs=[smem, vmem, vmem, vmem],
        out_specs=tuple([vmem] * 8),
    )(stencil.reshape(-1), fine_own, lead_own, factor_own)


def local_compute(side_flat, slot_table, fine_own, lead_own, factor_own, minus_own, buffers):
    nx, ny = fine_own.shape[:2]
    blk = fine_own.shape[2:]
    vmem = pl.BlockSpec(memory_space=pltpu.VMEM)
    smem = pl.BlockSpec(memory_space=pltpu.SMEM)
    f32 = jnp.float32
    strong, restrict = pl.pallas_call(
        local_kernel,
        out_shape=(jax.ShapeDtypeStruct((nx * ny * 2, 1, 128), f32),
                   jax.ShapeDtypeStruct((CAP, 14) + blk, jnp.bfloat16)),
        in_specs=[smem, smem] + [vmem] * (4 + len(buffers)),
        out_specs=(vmem, vmem),
        scratch_shapes=[
            pltpu.VMEM((nx + 6, ny + 6) + blk, f32),
            pltpu.VMEM((nx + 4, ny + 4, 2) + blk, f32),
            pltpu.VMEM((nx + 2, ny + 2) + blk, f32),
            pltpu.VMEM((nx + 4, ny + 4, 2) + blk, f32),
            pltpu.VMEM((nx + 2, ny + 2, 7) + blk, f32),
        ],
        compiler_params=pltpu.CompilerParams(vmem_limit_bytes=60 * 1024 * 1024),
    )(side_flat, slot_table, fine_own, lead_own, factor_own, minus_own, *buffers)
    return strong[:, 0, 0].reshape(nx, ny, 2), restrict


def on_device(inv_factors, couplings, stencil, coarse):
    nx, ny, flat = inv_factors.shape
    order = math.isqrt(flat)
    blk = (order, order)
    n_gx = lax.axis_size("gx")
    n_gy = lax.axis_size("gy")
    total_x = nx * n_gx
    total_y = ny * n_gy
    coord_x = lax.axis_index("gx") * nx + jnp.arange(nx, dtype=jnp.int32)
    coord_y = lax.axis_index("gy") * ny + jnp.arange(ny, dtype=jnp.int32)
    target_x = coord_x[:, None] + 2 * stencil[:, :, 0] - 1
    target_y = coord_y[None, :] + 2 * stencil[:, :, 1] - 1
    reach = jnp.stack(
        [(target_x >= 0) & (target_x < total_x), (target_y >= 0) & (target_y < total_y)], axis=-1
    )
    minus_own = (couplings * (-reach.astype(jnp.float32))[:, :, :, None]).reshape(
        (nx, ny, 2) + blk
    )
    factor_own = inv_factors.reshape((nx, ny) + blk)
    fine_own = (1 - coarse).astype(jnp.float32)[:, :, None, None] * left_gram(
        factor_own, factor_own
    )
    lead_own = matmul(fine_own[:, :, None], minus_own)

    def face(rows, cols):
        return jnp.concatenate(
            [
                fine_own[rows[3], cols[3]].reshape((-1,) + blk),
                lead_own[rows[2], cols[2]].reshape((-1,) + blk),
                factor_own[rows[1], cols[1]].reshape((-1,) + blk),
                code_block(stencil[rows[2], cols[2]], order),
            ],
            axis=0,
        )

    every = {d: slice(None) for d in (1, 2, 3)}
    low = {d: slice(0, d) for d in (1, 2, 3)}
    high_x = {d: slice(nx - d, nx) for d in (1, 2, 3)}
    high_y = {d: slice(ny - d, ny) for d in (1, 2, 3)}
    packed = pack_buffers(stencil, fine_own, lead_own, factor_own)
    from_xlo = lax.ppermute(packed[0], "gx", shift_pairs(n_gx, 1))
    from_xhi = lax.ppermute(packed[1], "gx", shift_pairs(n_gx, -1))
    from_ylo = lax.ppermute(packed[2], "gy", shift_pairs(n_gy, 1))
    from_yhi = lax.ppermute(packed[3], "gy", shift_pairs(n_gy, -1))
    corners = {}
    for step, buffer in zip(((1, 1), (1, -1), (-1, 1), (-1, -1)), packed[4:]):
        corners[step] = lax.ppermute(buffer, ("gx", "gy"), corner_pairs(n_gx, n_gy, *step))

    def face_codes(buffer, count, along_x):
        at = 3 * count + 2 * count * 2 + count
        codes = buffer[at // 2, 0, (at % 2) * order : (at % 2) * order + 2 * count * 2]
        codes = codes.astype(jnp.int32)
        return codes.reshape((2, count, 2) if along_x else (count, 2, 2))

    cxl = face_codes(from_xlo, ny, True)
    cxh = face_codes(from_xhi, ny, True)
    cyl = face_codes(from_ylo, nx, False)
    cyh = face_codes(from_yhi, nx, False)

    def unpack_corner(buffer):
        return (buffer[0:4].reshape((2, 2) + blk), buffer[4:6].reshape((1, 1, 2) + blk),
                buffer[6, 0, 0:2].astype(jnp.int32).reshape(1, 1, 2))

    c_ll = unpack_corner(corners[(1, 1)])
    c_lh = unpack_corner(corners[(1, -1)])
    c_hl = unpack_corner(corners[(-1, 1)])
    c_hh = unpack_corner(corners[(-1, -1)])

    def cycle(k, lo_x, own, hi_x, lo_y, hi_y):
        return jnp.concatenate(
            [
                row_band([padded(c_ll[k], True, True), lo_x, padded(c_lh[k], True, False)]),
                row_band([lo_y, own, hi_y]),
                row_band([padded(c_hl[k], False, True), hi_x, padded(c_hh[k], False, False)]),
            ],
            axis=0,
        )

    side_cycle = cycle(2, cxl, stencil, cxh, cyl, cyh)

    cell_count = nx * ny
    flat_coarse = coarse.reshape(cell_count)
    slot_rank = jnp.cumsum(flat_coarse, dtype=jnp.int32) - flat_coarse
    chosen = (
        (slot_rank[None, :] == jnp.arange(CAP, dtype=jnp.int32)[:, None])
        & (flat_coarse[None, :] == 1)
    ).astype(jnp.int32)
    source = jnp.sum(
        chosen * jnp.arange(cell_count, dtype=jnp.int32)[None, :], axis=1, dtype=jnp.int32
    )
    filled = jnp.sum(chosen, axis=1, dtype=jnp.int32)
    span = ny + 2
    own_i = jnp.arange(nx, dtype=jnp.int32)[:, None] + 1
    own_j = jnp.arange(ny, dtype=jnp.int32)[None, :] + 1
    up_index = jnp.stack(
        [(own_i + 2 * stencil[:, :, 0] - 1) * span + own_j,
         own_i * span + own_j + 2 * stencil[:, :, 1] - 1],
        axis=-1,
    ).reshape(cell_count, 2)
    picked = jnp.take(up_index, source, axis=0, mode="clip")
    slot_table = jnp.concatenate([source[:, None], picked, filled[:, None]], axis=1).reshape(-1)
    buffers = (from_xlo, from_xhi, from_ylo, from_yhi, corners[(1, 1)], corners[(1, -1)],
               corners[(-1, 1)], corners[(-1, -1)])
    strong, restrict = local_compute(side_cycle.reshape(-1), slot_table, fine_own, lead_own,
                                     factor_own, minus_own, buffers)
    return (strong, restrict.reshape(CAP, 14, flat))


def solution(mesh):
    placed = (P("gx", "gy", None), P("gx", "gy", None, None), P("gx", "gy", None), P("gx", "gy"))
    return jax.shard_map(
        on_device,
        mesh=mesh,
        in_specs=placed,
        out_specs=(P("gx", "gy", None), P(("gx", "gy"), None, None)),
        check_vma=False,
    )
```

```python
import math

import jax
import jax.numpy as jnp
from jax import lax
from jax.experimental import pallas as pl
from jax.experimental.pallas import tpu as pltpu
from jax.sharding import PartitionSpec as P

CAP = 12
PREC = lax.Precision.HIGH


def matmul(left_block, right_block):
    return jnp.einsum("...ij,...jk->...ik", left_block, right_block, precision=PREC)


def left_gram(left_block, right_block):
    return jnp.einsum("...ji,...jk->...ik", left_block, right_block, precision=PREC)


def right_gram(left_block, right_block):
    return jnp.einsum("...ij,...kj->...ik", left_block, right_block, precision=PREC)


def crop_cycle(values, margin):
    return values[margin : values.shape[0] - margin, margin : values.shape[1] - margin]


def upwind_pick(values, upwind_side):
    trailing = (1,) * (values.ndim - 2)
    sign_x = upwind_side[:, :, 0].reshape(upwind_side.shape[:2] + trailing)
    sign_y = upwind_side[:, :, 1].reshape(upwind_side.shape[:2] + trailing)
    upwind_x = jnp.where(sign_x == 1, values[2:, 1:-1], values[:-2, 1:-1])
    upwind_y = jnp.where(sign_y == 1, values[1:-1, 2:], values[1:-1, :-2])
    return (upwind_x, upwind_y)


def shift_pairs(count, step):
    return [(i, i + step) for i in range(count) if 0 <= i + step < count]


def corner_pairs(n_x, n_y, step_x, step_y):
    pairs = []
    for a in range(n_x):
        for b in range(n_y):
            if 0 <= a + step_x < n_x and 0 <= b + step_y < n_y:
                pairs.append((a * n_y + b, (a + step_x) * n_y + (b + step_y)))
    return pairs


def code_block(codes, order):
    values = codes.reshape(1, -1).astype(jnp.float32)
    return jnp.pad(values, ((0, order - 1), (0, order - values.shape[1])))[None]


def row_band(pieces):
    return jnp.concatenate(pieces, axis=1)


def padded(values, before_x, before_y):
    widths = [(1, 0) if before_x else (0, 1), (1, 0) if before_y else (0, 1)]
    widths += [(0, 0)] * (values.ndim - 2)
    return jnp.pad(values, widths)


def split(value):
    high = value.astype(jnp.bfloat16)
    low = (value - high.astype(jnp.float32)).astype(jnp.bfloat16)
    return high, low


def dot3(left, right, right_t=False):
    dims = (((1,), (1,)), ((), ())) if right_t else (((1,), (0,)), ((), ()))

    def one(a, b):
        return lax.dot_general(a, b, dims, preferred_element_type=jnp.float32)

    return one(left[0], right[0]) + one(left[0], right[1]) + one(left[1], right[0])


def local_kernel(side_ref, slot_ref, fine_ref, lead_ref, factor_ref, minus_ref,
                 xlo_ref, xhi_ref, ylo_ref, yhi_ref, cll_ref, clh_ref, chl_ref, chh_ref,
                 strong_ref, restrict_ref, pg, wg, gg, yg, zg):
    nx, ny = fine_ref.shape[0], fine_ref.shape[1]
    blk = fine_ref.shape[2:]
    zero = jnp.zeros(blk, jnp.float32)
    wide_x, wide_y = nx + 4, ny + 4
    pg_src, wg_src, gg_src = {}, {}, {}
    for i in range(nx):
        for j in range(ny):
            pg_src[(3 + i, 3 + j)] = (fine_ref, (i, j))
            gg_src[(1 + i, 1 + j)] = (factor_ref, (i, j))
            for e in range(2):
                wg_src[(2 + i, 2 + j, e)] = (lead_ref, (i, j, e))
    for c in range(ny):
        for r in range(3):
            pg_src[(r, 3 + c)] = (xlo_ref, (r * ny + c,))
            pg_src[(nx + 3 + r, 3 + c)] = (xhi_ref, (r * ny + c,))
        for r in range(2):
            for e in range(2):
                wg_src[(r, 2 + c, e)] = (xlo_ref, (3 * ny + (r * ny + c) * 2 + e,))
                wg_src[(nx + 2 + r, 2 + c, e)] = (xhi_ref, (3 * ny + (r * ny + c) * 2 + e,))
        gg_src[(0, 1 + c)] = (xlo_ref, (7 * ny + c,))
        gg_src[(nx + 1, 1 + c)] = (xhi_ref, (7 * ny + c,))
    for i in range(nx):
        for r in range(3):
            pg_src[(3 + i, r)] = (ylo_ref, (i * 3 + r,))
            pg_src[(3 + i, ny + 3 + r)] = (yhi_ref, (i * 3 + r,))
        for r in range(2):
            for e in range(2):
                wg_src[(2 + i, r, e)] = (ylo_ref, (3 * nx + (i * 2 + r) * 2 + e,))
                wg_src[(2 + i, ny + 2 + r, e)] = (yhi_ref, (3 * nx + (i * 2 + r) * 2 + e,))
        gg_src[(1 + i, 0)] = (ylo_ref, (7 * nx + i,))
        gg_src[(1 + i, ny + 1)] = (yhi_ref, (7 * nx + i,))
    for ref, px, py, wx, wy in ((cll_ref, 1, 1, 1, 1), (clh_ref, 1, ny + 3, 1, ny + 2),
                                (chl_ref, nx + 3, 1, nx + 2, 1),
                                (chh_ref, nx + 3, ny + 3, nx + 2, ny + 2)):
        for a in range(2):
            for b in range(2):
                pg_src[(px + a, py + b)] = (ref, (a * 2 + b,))
        for e in range(2):
            wg_src[(wx, wy, e)] = (ref, (4 + e,))
    def block(ref, at):
        if ref is None:
            return zero
        if len(at) == 1 and ref.shape[-1] == 2 * blk[-1]:
            half = at[0] % 2
            return ref[at[0] // 2, :, half * blk[-1] : (half + 1) * blk[-1]]
        return ref[at]

    for i in range(nx + 6):
        for j in range(ny + 6):
            pg[i, j] = block(*pg_src.get((i, j), (None, None)))
    for i in range(wide_x):
        for j in range(wide_y):
            for e in range(2):
                wg[i, j, e] = block(*wg_src.get((i, j, e), (None, None)))
    for i in range(nx + 2):
        for j in range(ny + 2):
            gg[i, j] = block(*gg_src.get((i, j), (None, None)))

    def side(i, j, d):
        return side_ref[(i * wide_y + j) * 2 + d]

    def near_step(p, carry):
        i = p // wide_y
        j = p % wide_y
        sx = side(i, j, 0)
        sy = side(i, j, 1)
        yg[i, j, 0] = dot3(split(wg[i, j, 0]), split(pg[i + 2 * sx, j + 1]))
        yg[i, j, 1] = dot3(split(wg[i, j, 1]), split(pg[i + 1, j + 2 * sy]))
        return carry

    lax.fori_loop(0, wide_x * wide_y, near_step, 0, unroll=True)

    def far_step(p, carry):
        i = p // (ny + 2)
        j = p % (ny + 2)
        zg[i, j, 0] = pg[i + 2, j + 2]
        for e in range(2):
            s = side(i + 1, j + 1, e)
            ui = i + 2 * s if e == 0 else i + 1
            uj = j + 1 if e == 0 else j + 2 * s
            lead = split(wg[i + 1, j + 1, e])
            zg[i, j, 1 + 3 * e] = dot3(lead, split(pg[ui + 1, uj + 1]))
            zg[i, j, 2 + 3 * e] = dot3(lead, split(yg[ui, uj, 0]))
            zg[i, j, 3 + 3 * e] = dot3(lead, split(yg[ui, uj, 1]))
        return carry

    lax.fori_loop(0, (nx + 2) * (ny + 2), far_step, 0, unroll=True)

    def strong_step(p, carry):
        i = p // ny
        j = p % ny
        factor = split(factor_ref[i, j])
        for d in range(2):
            s = side(i + 2, j + 2, d)
            up = gg[i + 2 * s, j + 1] if d == 0 else gg[i + 1, j + 2 * s]
            scaled = dot3(split(dot3(factor, split(minus_ref[i, j, d]))), split(up), True)
            total = jnp.sum(scaled * scaled, axis=(0, 1), keepdims=True)
            strong_ref[p * 2 + d] = jnp.broadcast_to(total * (1.0 / scaled.size), (1, 128))
        return carry

    lax.fori_loop(0, nx * ny, strong_step, 0, unroll=True)

    def slot_step(s, carry):
        cell = slot_ref[s * 4]
        weight = slot_ref[s * 4 + 3].astype(jnp.float32)
        ci = cell // ny
        cj = cell % ny
        for d in range(2):
            n = slot_ref[s * 4 + 1 + d]
            ni = n // (ny + 2)
            nj = n % (ny + 2)
            coupling = split(minus_ref[ci, cj, d])
            for w in range(7):
                row = dot3(coupling, split(zg[ni, nj, w]))
                restrict_ref[s, d * 7 + w] = (row * weight).astype(restrict_ref.dtype)
        return carry

    lax.fori_loop(0, restrict_ref.shape[0], slot_step, 0, unroll=True)


def face_sources(nx, ny, side):
    sources = []
    if side in ("xhi", "xlo"):
        rows = {d: (range(nx - d, nx) if side == "xhi" else range(d)) for d in (1, 2, 3)}
        for r in rows[3]:
            for c in range(ny):
                sources.append(("fine", (r, c)))
        for r in rows[2]:
            for c in range(ny):
                for e in range(2):
                    sources.append(("lead", (r, c, e)))
        for r in rows[1]:
            for c in range(ny):
                sources.append(("factor", (r, c)))
        codes = [(r, c, e) for r in rows[2] for c in range(ny) for e in range(2)]
    else:
        cols = {d: (range(ny - d, ny) if side == "yhi" else range(d)) for d in (1, 2, 3)}
        for i in range(nx):
            for r in cols[3]:
                sources.append(("fine", (i, r)))
        for i in range(nx):
            for r in cols[2]:
                for e in range(2):
                    sources.append(("lead", (i, r, e)))
        for i in range(nx):
            for r in cols[1]:
                sources.append(("factor", (i, r)))
        codes = [(i, r, e) for i in range(nx) for r in cols[2] for e in range(2)]
    return sources, codes


def code_tile(side_ref, codes, ny, shape):
    rows = lax.broadcasted_iota(jnp.int32, shape, 0)
    lanes = lax.broadcasted_iota(jnp.int32, shape, 1)
    tile = jnp.zeros(shape, jnp.float32)
    for k, (i, j, e) in enumerate(codes):
        value = side_ref[(i * ny + j) * 2 + e].astype(jnp.float32)
        tile = jnp.where((rows == 0) & (lanes == k), value, tile)
    return tile


def pack_kernel(side_ref, fine_ref, lead_ref, factor_ref, *out_refs):
    nx, ny = fine_ref.shape[0], fine_ref.shape[1]
    width = fine_ref.shape[-1]
    named = {"fine": fine_ref, "lead": lead_ref, "factor": factor_ref}
    for out, side in zip(out_refs[:4], ("xhi", "xlo", "yhi", "ylo")):
        sources, codes = face_sources(nx, ny, side)
        for k, (name, at) in enumerate(sources):
            out[k // 2, :, (k % 2) * width : (k % 2 + 1) * width] = named[name][at]
        last = len(sources)
        out[last // 2] = code_tile(side_ref, codes, ny, out.shape[1:])
    for out, (sx, sy) in zip(out_refs[4:], ((1, 1), (1, -1), (-1, 1), (-1, -1))):
        rows2 = range(nx - 2, nx) if sx == 1 else range(2)
        cols2 = range(ny - 2, ny) if sy == 1 else range(2)
        row1 = nx - 1 if sx == 1 else 0
        col1 = ny - 1 if sy == 1 else 0
        blocks = [fine_ref[a, b] for a in rows2 for b in cols2]
        blocks += [lead_ref[row1, col1, e] for e in range(2)]
        for k, value in enumerate(blocks):
            out[k // 2, :, (k % 2) * width : (k % 2 + 1) * width] = value
        out[len(blocks) // 2] = code_tile(side_ref, [(row1, col1, 0), (row1, col1, 1)], ny,
                                          out.shape[1:])


def pack_buffers(stencil, fine_own, lead_own, factor_own):
    nx, ny = fine_own.shape[:2]
    blk = fine_own.shape[2:]
    face_count = len(face_sources(nx, ny, "xhi")[0]) + 1
    face_y_count = len(face_sources(nx, ny, "yhi")[0]) + 1
    vmem = pl.BlockSpec(memory_space=pltpu.VMEM)
    smem = pl.BlockSpec(memory_space=pltpu.SMEM)
    paired = lambda count: jax.ShapeDtypeStruct(((count + 1) // 2, blk[0], 2 * blk[1]), jnp.float32)
    shapes = [paired(face_count)] * 2 + [paired(face_y_count)] * 2
    shapes += [paired(7)] * 4
    return pl.pallas_call(
        pack_kernel,
        out_shape=tuple(shapes),
        in_specs=[smem, vmem, vmem, vmem],
        out_specs=tuple([vmem] * 8),
    )(stencil.reshape(-1), fine_own, lead_own, factor_own)


def local_compute(side_flat, slot_table, fine_own, lead_own, factor_own, minus_own, buffers):
    nx, ny = fine_own.shape[:2]
    blk = fine_own.shape[2:]
    vmem = pl.BlockSpec(memory_space=pltpu.VMEM)
    smem = pl.BlockSpec(memory_space=pltpu.SMEM)
    f32 = jnp.float32
    strong, restrict = pl.pallas_call(
        local_kernel,
        out_shape=(jax.ShapeDtypeStruct((nx * ny * 2, 1, 128), f32),
                   jax.ShapeDtypeStruct((CAP, 14) + blk, jnp.bfloat16)),
        in_specs=[smem, smem] + [vmem] * (4 + len(buffers)),
        out_specs=(vmem, vmem),
        scratch_shapes=[
            pltpu.VMEM((nx + 6, ny + 6) + blk, f32),
            pltpu.VMEM((nx + 4, ny + 4, 2) + blk, f32),
            pltpu.VMEM((nx + 2, ny + 2) + blk, f32),
            pltpu.VMEM((nx + 4, ny + 4, 2) + blk, f32),
            pltpu.VMEM((nx + 2, ny + 2, 7) + blk, f32),
        ],
        compiler_params=pltpu.CompilerParams(vmem_limit_bytes=60 * 1024 * 1024),
    )(side_flat, slot_table, fine_own, lead_own, factor_own, minus_own, *buffers)
    return strong[:, 0, 0].reshape(nx, ny, 2), restrict


def on_device(inv_factors, couplings, stencil, coarse):
    nx, ny, flat = inv_factors.shape
    order = math.isqrt(flat)
    blk = (order, order)
    n_gx = lax.axis_size("gx")
    n_gy = lax.axis_size("gy")
    total_x = nx * n_gx
    total_y = ny * n_gy
    coord_x = lax.axis_index("gx") * nx + jnp.arange(nx, dtype=jnp.int32)
    coord_y = lax.axis_index("gy") * ny + jnp.arange(ny, dtype=jnp.int32)
    target_x = coord_x[:, None] + 2 * stencil[:, :, 0] - 1
    target_y = coord_y[None, :] + 2 * stencil[:, :, 1] - 1
    reach = jnp.stack(
        [(target_x >= 0) & (target_x < total_x), (target_y >= 0) & (target_y < total_y)], axis=-1
    )
    minus_own = (couplings * (-reach.astype(jnp.float32))[:, :, :, None]).reshape(
        (nx, ny, 2) + blk
    )
    factor_own = inv_factors.reshape((nx, ny) + blk)
    fine_own = (1 - coarse).astype(jnp.float32)[:, :, None, None] * left_gram(
        factor_own, factor_own
    )
    lead_own = matmul(fine_own[:, :, None], minus_own)

    def face(rows, cols):
        return jnp.concatenate(
            [
                fine_own[rows[3], cols[3]].reshape((-1,) + blk),
                lead_own[rows[2], cols[2]].reshape((-1,) + blk),
                factor_own[rows[1], cols[1]].reshape((-1,) + blk),
                code_block(stencil[rows[2], cols[2]], order),
            ],
            axis=0,
        )

    every = {d: slice(None) for d in (1, 2, 3)}
    low = {d: slice(0, d) for d in (1, 2, 3)}
    high_x = {d: slice(nx - d, nx) for d in (1, 2, 3)}
    high_y = {d: slice(ny - d, ny) for d in (1, 2, 3)}
    packed = pack_buffers(stencil, fine_own, lead_own, factor_own)
    from_xlo = lax.ppermute(packed[0], "gx", shift_pairs(n_gx, 1))
    from_xhi = lax.ppermute(packed[1], "gx", shift_pairs(n_gx, -1))
    from_ylo = lax.ppermute(packed[2], "gy", shift_pairs(n_gy, 1))
    from_yhi = lax.ppermute(packed[3], "gy", shift_pairs(n_gy, -1))
    corners = {}
    for step, buffer in zip(((1, 1), (1, -1), (-1, 1), (-1, -1)), packed[4:]):
        corners[step] = lax.ppermute(buffer, ("gx", "gy"), corner_pairs(n_gx, n_gy, *step))

    def face_codes(buffer, count, along_x):
        at = 3 * count + 2 * count * 2 + count
        codes = buffer[at // 2, 0, (at % 2) * order : (at % 2) * order + 2 * count * 2]
        codes = codes.astype(jnp.int32)
        return codes.reshape((2, count, 2) if along_x else (count, 2, 2))

    cxl = face_codes(from_xlo, ny, True)
    cxh = face_codes(from_xhi, ny, True)
    cyl = face_codes(from_ylo, nx, False)
    cyh = face_codes(from_yhi, nx, False)

    def unpack_corner(buffer):
        return (None, None, buffer[3, 0, 0:2].astype(jnp.int32).reshape(1, 1, 2))

    c_ll = unpack_corner(corners[(1, 1)])
    c_lh = unpack_corner(corners[(1, -1)])
    c_hl = unpack_corner(corners[(-1, 1)])
    c_hh = unpack_corner(corners[(-1, -1)])

    def cycle(k, lo_x, own, hi_x, lo_y, hi_y):
        return jnp.concatenate(
            [
                row_band([padded(c_ll[k], True, True), lo_x, padded(c_lh[k], True, False)]),
                row_band([lo_y, own, hi_y]),
                row_band([padded(c_hl[k], False, True), hi_x, padded(c_hh[k], False, False)]),
            ],
            axis=0,
        )

    side_cycle = cycle(2, cxl, stencil, cxh, cyl, cyh)

    cell_count = nx * ny
    flat_coarse = coarse.reshape(cell_count)
    slot_rank = jnp.cumsum(flat_coarse, dtype=jnp.int32) - flat_coarse
    chosen = (
        (slot_rank[None, :] == jnp.arange(CAP, dtype=jnp.int32)[:, None])
        & (flat_coarse[None, :] == 1)
    ).astype(jnp.int32)
    source = jnp.sum(
        chosen * jnp.arange(cell_count, dtype=jnp.int32)[None, :], axis=1, dtype=jnp.int32
    )
    filled = jnp.sum(chosen, axis=1, dtype=jnp.int32)
    span = ny + 2
    own_i = jnp.arange(nx, dtype=jnp.int32)[:, None] + 1
    own_j = jnp.arange(ny, dtype=jnp.int32)[None, :] + 1
    up_index = jnp.stack(
        [(own_i + 2 * stencil[:, :, 0] - 1) * span + own_j,
         own_i * span + own_j + 2 * stencil[:, :, 1] - 1],
        axis=-1,
    ).reshape(cell_count, 2)
    picked = jnp.take(up_index, source, axis=0, mode="clip")
    slot_table = jnp.concatenate([source[:, None], picked, filled[:, None]], axis=1).reshape(-1)
    buffers = (from_xlo, from_xhi, from_ylo, from_yhi, corners[(1, 1)], corners[(1, -1)],
               corners[(-1, 1)], corners[(-1, -1)])
    strong, restrict = local_compute(side_cycle.reshape(-1), slot_table, fine_own, lead_own,
                                     factor_own, minus_own, buffers)
    return (strong, restrict.reshape(CAP, 14, flat))


def solution(mesh):
    placed = (P("gx", "gy", None), P("gx", "gy", None, None), P("gx", "gy", None), P("gx", "gy"))
    return jax.shard_map(
        on_device,
        mesh=mesh,
        in_specs=placed,
        out_specs=(P("gx", "gy", None), P(("gx", "gy"), None, None)),
        check_vma=False,
    )
```

```python
import math

import jax
import jax.numpy as jnp
from jax import lax
from jax.experimental import pallas as pl
from jax.experimental.pallas import tpu as pltpu
from jax.sharding import PartitionSpec as P

CAP = 12
PREC = lax.Precision.HIGH


def matmul(left_block, right_block):
    return jnp.einsum("...ij,...jk->...ik", left_block, right_block, precision=PREC)


def left_gram(left_block, right_block):
    return jnp.einsum("...ji,...jk->...ik", left_block, right_block, precision=PREC)


def right_gram(left_block, right_block):
    return jnp.einsum("...ij,...kj->...ik", left_block, right_block, precision=PREC)


def crop_cycle(values, margin):
    return values[margin : values.shape[0] - margin, margin : values.shape[1] - margin]


def upwind_pick(values, upwind_side):
    trailing = (1,) * (values.ndim - 2)
    sign_x = upwind_side[:, :, 0].reshape(upwind_side.shape[:2] + trailing)
    sign_y = upwind_side[:, :, 1].reshape(upwind_side.shape[:2] + trailing)
    upwind_x = jnp.where(sign_x == 1, values[2:, 1:-1], values[:-2, 1:-1])
    upwind_y = jnp.where(sign_y == 1, values[1:-1, 2:], values[1:-1, :-2])
    return (upwind_x, upwind_y)


def shift_pairs(count, step):
    return [(i, i + step) for i in range(count) if 0 <= i + step < count]


def corner_pairs(n_x, n_y, step_x, step_y):
    pairs = []
    for a in range(n_x):
        for b in range(n_y):
            if 0 <= a + step_x < n_x and 0 <= b + step_y < n_y:
                pairs.append((a * n_y + b, (a + step_x) * n_y + (b + step_y)))
    return pairs


def code_block(codes, order):
    values = codes.reshape(1, -1).astype(jnp.float32)
    return jnp.pad(values, ((0, order - 1), (0, order - values.shape[1])))[None]


def row_band(pieces):
    return jnp.concatenate(pieces, axis=1)


def padded(values, before_x, before_y):
    widths = [(1, 0) if before_x else (0, 1), (1, 0) if before_y else (0, 1)]
    widths += [(0, 0)] * (values.ndim - 2)
    return jnp.pad(values, widths)


def split(value):
    high = value.astype(jnp.bfloat16)
    low = (value - high.astype(jnp.float32)).astype(jnp.bfloat16)
    return high, low


def dot3(left, right, right_t=False):
    dims = (((1,), (1,)), ((), ())) if right_t else (((1,), (0,)), ((), ()))

    def one(a, b):
        return lax.dot_general(a, b, dims, preferred_element_type=jnp.float32)

    return one(left[0], right[0]) + one(left[0], right[1]) + one(left[1], right[0])


def local_kernel(side_ref, slot_ref, fine_ref, lead_ref, factor_ref, minus_ref,
                 xlo_ref, xhi_ref, ylo_ref, yhi_ref, cll_ref, clh_ref, chl_ref, chh_ref,
                 strong_ref, restrict_ref, pg, wg, gg, yg, zg):
    nx, ny = fine_ref.shape[0], fine_ref.shape[1]
    blk = fine_ref.shape[2:]
    zero = jnp.zeros(blk, jnp.float32)
    wide_x, wide_y = nx + 4, ny + 4
    pg_src, wg_src, gg_src = {}, {}, {}
    for i in range(nx):
        for j in range(ny):
            pg_src[(3 + i, 3 + j)] = (fine_ref, (i, j))
            gg_src[(1 + i, 1 + j)] = (factor_ref, (i, j))
            for e in range(2):
                wg_src[(2 + i, 2 + j, e)] = (lead_ref, (i, j, e))
    for c in range(ny):
        for r in range(3):
            pg_src[(r, 3 + c)] = (xlo_ref, (r * ny + c,))
            pg_src[(nx + 3 + r, 3 + c)] = (xhi_ref, (r * ny + c,))
        for r in range(2):
            for e in range(2):
                wg_src[(r, 2 + c, e)] = (xlo_ref, (3 * ny + (r * ny + c) * 2 + e,))
                wg_src[(nx + 2 + r, 2 + c, e)] = (xhi_ref, (3 * ny + (r * ny + c) * 2 + e,))
        gg_src[(0, 1 + c)] = (xlo_ref, (7 * ny + c,))
        gg_src[(nx + 1, 1 + c)] = (xhi_ref, (7 * ny + c,))
    for i in range(nx):
        for r in range(3):
            pg_src[(3 + i, r)] = (ylo_ref, (i * 3 + r,))
            pg_src[(3 + i, ny + 3 + r)] = (yhi_ref, (i * 3 + r,))
        for r in range(2):
            for e in range(2):
                wg_src[(2 + i, r, e)] = (ylo_ref, (3 * nx + (i * 2 + r) * 2 + e,))
                wg_src[(2 + i, ny + 2 + r, e)] = (yhi_ref, (3 * nx + (i * 2 + r) * 2 + e,))
        gg_src[(1 + i, 0)] = (ylo_ref, (7 * nx + i,))
        gg_src[(1 + i, ny + 1)] = (yhi_ref, (7 * nx + i,))
    for ref, px, py, wx, wy in ((cll_ref, 1, 1, 1, 1), (clh_ref, 1, ny + 3, 1, ny + 2),
                                (chl_ref, nx + 3, 1, nx + 2, 1),
                                (chh_ref, nx + 3, ny + 3, nx + 2, ny + 2)):
        for a in range(2):
            for b in range(2):
                pg_src[(px + a, py + b)] = (ref, (a * 2 + b,))
        for e in range(2):
            wg_src[(wx, wy, e)] = (ref, (4 + e,))
    def block(ref, at):
        if ref is None:
            return zero
        if len(at) == 1 and ref.shape[-1] == 2 * blk[-1]:
            half = at[0] % 2
            return ref[at[0] // 2, :, half * blk[-1] : (half + 1) * blk[-1]]
        return ref[at]

    for i in range(nx + 6):
        for j in range(ny + 6):
            pg[i, j] = block(*pg_src.get((i, j), (None, None)))
    for i in range(wide_x):
        for j in range(wide_y):
            for e in range(2):
                wg[i, j, e] = block(*wg_src.get((i, j, e), (None, None)))
    for i in range(nx + 2):
        for j in range(ny + 2):
            gg[i, j] = block(*gg_src.get((i, j), (None, None)))

    def side(i, j, d):
        return side_ref[(i * wide_y + j) * 2 + d]

    def outside(k, low, size):
        return max(low - k, k - (low + size - 1), 0)

    for i in range(wide_x):
        for j in range(wide_y):
            if outside(i, 2, nx) + outside(j, 2, ny) > 2:
                continue
            sx = side(i, j, 0)
            sy = side(i, j, 1)
            yg[i, j, 0] = dot3(split(wg[i, j, 0]), split(pg[i + 2 * sx, j + 1]))
            yg[i, j, 1] = dot3(split(wg[i, j, 1]), split(pg[i + 1, j + 2 * sy]))

    for i in range(nx + 2):
        for j in range(ny + 2):
            if outside(i, 1, nx) + outside(j, 1, ny) > 1:
                continue
            zg[i, j, 0] = pg[i + 2, j + 2]
            for e in range(2):
                s = side(i + 1, j + 1, e)
                ui = i + 2 * s if e == 0 else i + 1
                uj = j + 1 if e == 0 else j + 2 * s
                lead = split(wg[i + 1, j + 1, e])
                zg[i, j, 1 + 3 * e] = dot3(lead, split(pg[ui + 1, uj + 1]))
                zg[i, j, 2 + 3 * e] = dot3(lead, split(yg[ui, uj, 0]))
                zg[i, j, 3 + 3 * e] = dot3(lead, split(yg[ui, uj, 1]))

    def strong_step(p, carry):
        i = p // ny
        j = p % ny
        factor = split(factor_ref[i, j])
        for d in range(2):
            s = side(i + 2, j + 2, d)
            up = gg[i + 2 * s, j + 1] if d == 0 else gg[i + 1, j + 2 * s]
            scaled = dot3(split(dot3(factor, split(minus_ref[i, j, d]))), split(up), True)
            total = jnp.sum(scaled * scaled, axis=(0, 1), keepdims=True)
            strong_ref[p * 2 + d] = jnp.broadcast_to(total * (1.0 / scaled.size), (1, 128))
        return carry

    lax.fori_loop(0, nx * ny, strong_step, 0, unroll=True)

    def slot_step(s, carry):
        cell = slot_ref[s * 4]
        weight = slot_ref[s * 4 + 3].astype(jnp.float32)
        ci = cell // ny
        cj = cell % ny
        for d in range(2):
            n = slot_ref[s * 4 + 1 + d]
            ni = n // (ny + 2)
            nj = n % (ny + 2)
            coupling = split(minus_ref[ci, cj, d])
            for w in range(7):
                row = dot3(coupling, split(zg[ni, nj, w]))
                restrict_ref[s, d * 7 + w] = (row * weight).astype(restrict_ref.dtype)
        return carry

    lax.fori_loop(0, restrict_ref.shape[0], slot_step, 0, unroll=True)


def face_sources(nx, ny, side):
    sources = []
    if side in ("xhi", "xlo"):
        rows = {d: (range(nx - d, nx) if side == "xhi" else range(d)) for d in (1, 2, 3)}
        for r in rows[3]:
            for c in range(ny):
                sources.append(("fine", (r, c)))
        for r in rows[2]:
            for c in range(ny):
                for e in range(2):
                    sources.append(("lead", (r, c, e)))
        for r in rows[1]:
            for c in range(ny):
                sources.append(("factor", (r, c)))
        codes = [(r, c, e) for r in rows[2] for c in range(ny) for e in range(2)]
    else:
        cols = {d: (range(ny - d, ny) if side == "yhi" else range(d)) for d in (1, 2, 3)}
        for i in range(nx):
            for r in cols[3]:
                sources.append(("fine", (i, r)))
        for i in range(nx):
            for r in cols[2]:
                for e in range(2):
                    sources.append(("lead", (i, r, e)))
        for i in range(nx):
            for r in cols[1]:
                sources.append(("factor", (i, r)))
        codes = [(i, r, e) for i in range(nx) for r in cols[2] for e in range(2)]
    return sources, codes


def code_tile(side_ref, codes, ny, shape):
    rows = lax.broadcasted_iota(jnp.int32, shape, 0)
    lanes = lax.broadcasted_iota(jnp.int32, shape, 1)
    tile = jnp.zeros(shape, jnp.float32)
    for k, (i, j, e) in enumerate(codes):
        value = side_ref[(i * ny + j) * 2 + e].astype(jnp.float32)
        tile = jnp.where((rows == 0) & (lanes == k), value, tile)
    return tile


def pack_kernel(side_ref, fine_ref, lead_ref, factor_ref, *out_refs):
    nx, ny = fine_ref.shape[0], fine_ref.shape[1]
    width = fine_ref.shape[-1]
    named = {"fine": fine_ref, "lead": lead_ref, "factor": factor_ref}
    for out, side in zip(out_refs[:4], ("xhi", "xlo", "yhi", "ylo")):
        sources, codes = face_sources(nx, ny, side)
        for k, (name, at) in enumerate(sources):
            out[k // 2, :, (k % 2) * width : (k % 2 + 1) * width] = named[name][at]
        last = len(sources)
        out[last // 2] = code_tile(side_ref, codes, ny, out.shape[1:])
    for out, (sx, sy) in zip(out_refs[4:], ((1, 1), (1, -1), (-1, 1), (-1, -1))):
        rows2 = range(nx - 2, nx) if sx == 1 else range(2)
        cols2 = range(ny - 2, ny) if sy == 1 else range(2)
        row1 = nx - 1 if sx == 1 else 0
        col1 = ny - 1 if sy == 1 else 0
        blocks = [fine_ref[a, b] for a in rows2 for b in cols2]
        blocks += [lead_ref[row1, col1, e] for e in range(2)]
        for k, value in enumerate(blocks):
            out[k // 2, :, (k % 2) * width : (k % 2 + 1) * width] = value
        out[len(blocks) // 2] = code_tile(side_ref, [(row1, col1, 0), (row1, col1, 1)], ny,
                                          out.shape[1:])


def pack_buffers(stencil, fine_own, lead_own, factor_own):
    nx, ny = fine_own.shape[:2]
    blk = fine_own.shape[2:]
    face_count = len(face_sources(nx, ny, "xhi")[0]) + 1
    face_y_count = len(face_sources(nx, ny, "yhi")[0]) + 1
    vmem = pl.BlockSpec(memory_space=pltpu.VMEM)
    smem = pl.BlockSpec(memory_space=pltpu.SMEM)
    paired = lambda count: jax.ShapeDtypeStruct(((count + 1) // 2, blk[0], 2 * blk[1]), jnp.float32)
    shapes = [paired(face_count)] * 2 + [paired(face_y_count)] * 2
    shapes += [paired(7)] * 4
    return pl.pallas_call(
        pack_kernel,
        out_shape=tuple(shapes),
        in_specs=[smem, vmem, vmem, vmem],
        out_specs=tuple([vmem] * 8),
    )(stencil.reshape(-1), fine_own, lead_own, factor_own)


def local_compute(side_flat, slot_table, fine_own, lead_own, factor_own, minus_own, buffers):
    nx, ny = fine_own.shape[:2]
    blk = fine_own.shape[2:]
    vmem = pl.BlockSpec(memory_space=pltpu.VMEM)
    smem = pl.BlockSpec(memory_space=pltpu.SMEM)
    f32 = jnp.float32
    strong, restrict = pl.pallas_call(
        local_kernel,
        out_shape=(jax.ShapeDtypeStruct((nx * ny * 2, 1, 128), f32),
                   jax.ShapeDtypeStruct((CAP, 14) + blk, jnp.bfloat16)),
        in_specs=[smem, smem] + [vmem] * (4 + len(buffers)),
        out_specs=(vmem, vmem),
        scratch_shapes=[
            pltpu.VMEM((nx + 6, ny + 6) + blk, f32),
            pltpu.VMEM((nx + 4, ny + 4, 2) + blk, f32),
            pltpu.VMEM((nx + 2, ny + 2) + blk, f32),
            pltpu.VMEM((nx + 4, ny + 4, 2) + blk, f32),
            pltpu.VMEM((nx + 2, ny + 2, 7) + blk, f32),
        ],
        compiler_params=pltpu.CompilerParams(vmem_limit_bytes=60 * 1024 * 1024),
    )(side_flat, slot_table, fine_own, lead_own, factor_own, minus_own, *buffers)
    return strong[:, 0, 0].reshape(nx, ny, 2), restrict


def on_device(inv_factors, couplings, stencil, coarse):
    nx, ny, flat = inv_factors.shape
    order = math.isqrt(flat)
    blk = (order, order)
    n_gx = lax.axis_size("gx")
    n_gy = lax.axis_size("gy")
    total_x = nx * n_gx
    total_y = ny * n_gy
    coord_x = lax.axis_index("gx") * nx + jnp.arange(nx, dtype=jnp.int32)
    coord_y = lax.axis_index("gy") * ny + jnp.arange(ny, dtype=jnp.int32)
    target_x = coord_x[:, None] + 2 * stencil[:, :, 0] - 1
    target_y = coord_y[None, :] + 2 * stencil[:, :, 1] - 1
    reach = jnp.stack(
        [(target_x >= 0) & (target_x < total_x), (target_y >= 0) & (target_y < total_y)], axis=-1
    )
    minus_own = (couplings * (-reach.astype(jnp.float32))[:, :, :, None]).reshape(
        (nx, ny, 2) + blk
    )
    factor_own = inv_factors.reshape((nx, ny) + blk)
    fine_own = (1 - coarse).astype(jnp.float32)[:, :, None, None] * left_gram(
        factor_own, factor_own
    )
    lead_own = matmul(fine_own[:, :, None], minus_own)

    def face(rows, cols):
        return jnp.concatenate(
            [
                fine_own[rows[3], cols[3]].reshape((-1,) + blk),
                lead_own[rows[2], cols[2]].reshape((-1,) + blk),
                factor_own[rows[1], cols[1]].reshape((-1,) + blk),
                code_block(stencil[rows[2], cols[2]], order),
            ],
            axis=0,
        )

    every = {d: slice(None) for d in (1, 2, 3)}
    low = {d: slice(0, d) for d in (1, 2, 3)}
    high_x = {d: slice(nx - d, nx) for d in (1, 2, 3)}
    high_y = {d: slice(ny - d, ny) for d in (1, 2, 3)}
    packed = pack_buffers(stencil, fine_own, lead_own, factor_own)
    from_xlo = lax.ppermute(packed[0], "gx", shift_pairs(n_gx, 1))
    from_xhi = lax.ppermute(packed[1], "gx", shift_pairs(n_gx, -1))
    from_ylo = lax.ppermute(packed[2], "gy", shift_pairs(n_gy, 1))
    from_yhi = lax.ppermute(packed[3], "gy", shift_pairs(n_gy, -1))
    corners = {}
    for step, buffer in zip(((1, 1), (1, -1), (-1, 1), (-1, -1)), packed[4:]):
        corners[step] = lax.ppermute(buffer, ("gx", "gy"), corner_pairs(n_gx, n_gy, *step))

    def face_codes(buffer, count, along_x):
        at = 3 * count + 2 * count * 2 + count
        codes = buffer[at // 2, 0, (at % 2) * order : (at % 2) * order + 2 * count * 2]
        codes = codes.astype(jnp.int32)
        return codes.reshape((2, count, 2) if along_x else (count, 2, 2))

    cxl = face_codes(from_xlo, ny, True)
    cxh = face_codes(from_xhi, ny, True)
    cyl = face_codes(from_ylo, nx, False)
    cyh = face_codes(from_yhi, nx, False)

    def unpack_corner(buffer):
        return (None, None, buffer[3, 0, 0:2].astype(jnp.int32).reshape(1, 1, 2))

    c_ll = unpack_corner(corners[(1, 1)])
    c_lh = unpack_corner(corners[(1, -1)])
    c_hl = unpack_corner(corners[(-1, 1)])
    c_hh = unpack_corner(corners[(-1, -1)])

    def cycle(k, lo_x, own, hi_x, lo_y, hi_y):
        return jnp.concatenate(
            [
                row_band([padded(c_ll[k], True, True), lo_x, padded(c_lh[k], True, False)]),
                row_band([lo_y, own, hi_y]),
                row_band([padded(c_hl[k], False, True), hi_x, padded(c_hh[k], False, False)]),
            ],
            axis=0,
        )

    side_cycle = cycle(2, cxl, stencil, cxh, cyl, cyh)

    cell_count = nx * ny
    flat_coarse = coarse.reshape(cell_count)
    slot_rank = jnp.cumsum(flat_coarse, dtype=jnp.int32) - flat_coarse
    chosen = (
        (slot_rank[None, :] == jnp.arange(CAP, dtype=jnp.int32)[:, None])
        & (flat_coarse[None, :] == 1)
    ).astype(jnp.int32)
    source = jnp.sum(
        chosen * jnp.arange(cell_count, dtype=jnp.int32)[None, :], axis=1, dtype=jnp.int32
    )
    filled = jnp.sum(chosen, axis=1, dtype=jnp.int32)
    span = ny + 2
    own_i = jnp.arange(nx, dtype=jnp.int32)[:, None] + 1
    own_j = jnp.arange(ny, dtype=jnp.int32)[None, :] + 1
    up_index = jnp.stack(
        [(own_i + 2 * stencil[:, :, 0] - 1) * span + own_j,
         own_i * span + own_j + 2 * stencil[:, :, 1] - 1],
        axis=-1,
    ).reshape(cell_count, 2)
    picked = jnp.take(up_index, source, axis=0, mode="clip")
    slot_table = jnp.concatenate([source[:, None], picked, filled[:, None]], axis=1).reshape(-1)
    buffers = (from_xlo, from_xhi, from_ylo, from_yhi, corners[(1, 1)], corners[(1, -1)],
               corners[(-1, 1)], corners[(-1, -1)])
    strong, restrict = local_compute(side_cycle.reshape(-1), slot_table, fine_own, lead_own,
                                     factor_own, minus_own, buffers)
    return (strong, restrict.reshape(CAP, 14, flat))


def solution(mesh):
    placed = (P("gx", "gy", None), P("gx", "gy", None, None), P("gx", "gy", None), P("gx", "gy"))
    return jax.shard_map(
        on_device,
        mesh=mesh,
        in_specs=placed,
        out_specs=(P("gx", "gy", None), P(("gx", "gy"), None, None)),
        check_vma=False,
    )
```

```python
import math

import jax
import jax.numpy as jnp
from jax import lax
from jax.experimental import pallas as pl
from jax.experimental.pallas import tpu as pltpu
from jax.sharding import PartitionSpec as P

CAP = 12
PREC = lax.Precision.HIGH


def matmul(left_block, right_block):
    return jnp.einsum("...ij,...jk->...ik", left_block, right_block, precision=PREC)


def left_gram(left_block, right_block):
    return jnp.einsum("...ji,...jk->...ik", left_block, right_block, precision=PREC)


def shift_pairs(count, step):
    return [(i, i + step) for i in range(count) if 0 <= i + step < count]


def corner_pairs(n_x, n_y, step_x, step_y):
    pairs = []
    for a in range(n_x):
        for b in range(n_y):
            if 0 <= a + step_x < n_x and 0 <= b + step_y < n_y:
                pairs.append((a * n_y + b, (a + step_x) * n_y + (b + step_y)))
    return pairs


def row_band(pieces):
    return jnp.concatenate(pieces, axis=1)


def padded(values, before_x, before_y):
    widths = [(1, 0) if before_x else (0, 1), (1, 0) if before_y else (0, 1)]
    widths += [(0, 0)] * (values.ndim - 2)
    return jnp.pad(values, widths)


def split(value):
    high = value.astype(jnp.bfloat16)
    low = (value - high.astype(jnp.float32)).astype(jnp.bfloat16)
    return high, low


def dot3(left, right, right_t=False):
    dims = (((1,), (1,)), ((), ())) if right_t else (((1,), (0,)), ((), ()))

    def one(a, b):
        return lax.dot_general(a, b, dims, preferred_element_type=jnp.float32)

    return one(left[0], right[0]) + one(left[0], right[1]) + one(left[1], right[0])


def local_kernel(side_ref, slot_ref, fine_ref, lead_ref, factor_ref, minus_ref,
                 xlo_ref, xhi_ref, ylo_ref, yhi_ref, cll_ref, clh_ref, chl_ref, chh_ref,
                 strong_ref, restrict_ref, pg, wg, gg, yg, zg):
    nx, ny = fine_ref.shape[0], fine_ref.shape[1]
    blk = fine_ref.shape[2:]
    zero = jnp.zeros(blk, jnp.float32)
    wide_x, wide_y = nx + 4, ny + 4
    pg_src, wg_src, gg_src = {}, {}, {}
    for i in range(nx):
        for j in range(ny):
            pg_src[(3 + i, 3 + j)] = (fine_ref, (i, j))
            gg_src[(1 + i, 1 + j)] = (factor_ref, (i, j))
            for e in range(2):
                wg_src[(2 + i, 2 + j, e)] = (lead_ref, (i, j, e))
    for c in range(ny):
        for r in range(3):
            pg_src[(r, 3 + c)] = (xlo_ref, (r * ny + c,))
            pg_src[(nx + 3 + r, 3 + c)] = (xhi_ref, (r * ny + c,))
        for r in range(2):
            for e in range(2):
                wg_src[(r, 2 + c, e)] = (xlo_ref, (3 * ny + (r * ny + c) * 2 + e,))
                wg_src[(nx + 2 + r, 2 + c, e)] = (xhi_ref, (3 * ny + (r * ny + c) * 2 + e,))
        gg_src[(0, 1 + c)] = (xlo_ref, (7 * ny + c,))
        gg_src[(nx + 1, 1 + c)] = (xhi_ref, (7 * ny + c,))
    for i in range(nx):
        for r in range(3):
            pg_src[(3 + i, r)] = (ylo_ref, (i * 3 + r,))
            pg_src[(3 + i, ny + 3 + r)] = (yhi_ref, (i * 3 + r,))
        for r in range(2):
            for e in range(2):
                wg_src[(2 + i, r, e)] = (ylo_ref, (3 * nx + (i * 2 + r) * 2 + e,))
                wg_src[(2 + i, ny + 2 + r, e)] = (yhi_ref, (3 * nx + (i * 2 + r) * 2 + e,))
        gg_src[(1 + i, 0)] = (ylo_ref, (7 * nx + i,))
        gg_src[(1 + i, ny + 1)] = (yhi_ref, (7 * nx + i,))
    for ref, px, py, wx, wy in ((cll_ref, 1, 1, 1, 1), (clh_ref, 1, ny + 3, 1, ny + 2),
                                (chl_ref, nx + 3, 1, nx + 2, 1),
                                (chh_ref, nx + 3, ny + 3, nx + 2, ny + 2)):
        for a in range(2):
            for b in range(2):
                pg_src[(px + a, py + b)] = (ref, (a * 2 + b,))
        for e in range(2):
            wg_src[(wx, wy, e)] = (ref, (4 + e,))

    def block(ref, at):
        if ref is None:
            return zero
        if len(at) == 1 and ref.shape[-1] == 2 * blk[-1]:
            half = at[0] % 2
            return ref[at[0] // 2, :, half * blk[-1] : (half + 1) * blk[-1]]
        return ref[at]

    for i in range(nx + 6):
        for j in range(ny + 6):
            pg[i, j] = block(*pg_src.get((i, j), (None, None)))
    for i in range(wide_x):
        for j in range(wide_y):
            for e in range(2):
                wg[i, j, e] = block(*wg_src.get((i, j, e), (None, None)))
    for i in range(nx + 2):
        for j in range(ny + 2):
            gg[i, j] = block(*gg_src.get((i, j), (None, None)))

    def side(i, j, d):
        return side_ref[(i * wide_y + j) * 2 + d]

    def outside(k, low, size):
        return max(low - k, k - (low + size - 1), 0)

    for i in range(wide_x):
        for j in range(wide_y):
            if outside(i, 2, nx) + outside(j, 2, ny) > 2:
                continue
            sx = side(i, j, 0)
            sy = side(i, j, 1)
            yg[i, j, 0] = dot3(split(wg[i, j, 0]), split(pg[i + 2 * sx, j + 1]))
            yg[i, j, 1] = dot3(split(wg[i, j, 1]), split(pg[i + 1, j + 2 * sy]))

    for i in range(nx + 2):
        for j in range(ny + 2):
            if outside(i, 1, nx) + outside(j, 1, ny) > 1:
                continue
            zg[i, j, 0] = pg[i + 2, j + 2]
            for e in range(2):
                s = side(i + 1, j + 1, e)
                ui = i + 2 * s if e == 0 else i + 1
                uj = j + 1 if e == 0 else j + 2 * s
                lead = split(wg[i + 1, j + 1, e])
                zg[i, j, 1 + 3 * e] = dot3(lead, split(pg[ui + 1, uj + 1]))
                zg[i, j, 2 + 3 * e] = dot3(lead, split(yg[ui, uj, 0]))
                zg[i, j, 3 + 3 * e] = dot3(lead, split(yg[ui, uj, 1]))

    def strong_step(p, carry):
        i = p // ny
        j = p % ny
        factor = split(factor_ref[i, j])
        for d in range(2):
            s = side(i + 2, j + 2, d)
            up = gg[i + 2 * s, j + 1] if d == 0 else gg[i + 1, j + 2 * s]
            scaled = dot3(split(dot3(factor, split(minus_ref[i, j, d]))), split(up), True)
            total = jnp.sum(scaled * scaled, axis=(0, 1), keepdims=True)
            strong_ref[p * 2 + d] = jnp.broadcast_to(total * (1.0 / scaled.size), (1, 128))
        return carry

    lax.fori_loop(0, nx * ny, strong_step, 0, unroll=True)

    def slot_step(s, carry):
        cell = slot_ref[s * 4]
        weight = slot_ref[s * 4 + 3].astype(jnp.float32)
        ci = cell // ny
        cj = cell % ny
        for d in range(2):
            n = slot_ref[s * 4 + 1 + d]
            ni = n // (ny + 2)
            nj = n % (ny + 2)
            coupling = split(minus_ref[ci, cj, d])
            for w in range(7):
                row = dot3(coupling, split(zg[ni, nj, w]))
                restrict_ref[s, d * 7 + w] = (row * weight).astype(restrict_ref.dtype)
        return carry

    lax.fori_loop(0, restrict_ref.shape[0], slot_step, 0, unroll=True)


def face_sources(nx, ny, side):
    sources = []
    if side in ("xhi", "xlo"):
        rows = {d: (range(nx - d, nx) if side == "xhi" else range(d)) for d in (1, 2, 3)}
        for r in rows[3]:
            for c in range(ny):
                sources.append(("fine", (r, c)))
        for r in rows[2]:
            for c in range(ny):
                for e in range(2):
                    sources.append(("lead", (r, c, e)))
        for r in rows[1]:
            for c in range(ny):
                sources.append(("factor", (r, c)))
        codes = [(r, c, e) for r in rows[2] for c in range(ny) for e in range(2)]
    else:
        cols = {d: (range(ny - d, ny) if side == "yhi" else range(d)) for d in (1, 2, 3)}
        for i in range(nx):
            for r in cols[3]:
                sources.append(("fine", (i, r)))
        for i in range(nx):
            for r in cols[2]:
                for e in range(2):
                    sources.append(("lead", (i, r, e)))
        for i in range(nx):
            for r in cols[1]:
                sources.append(("factor", (i, r)))
        codes = [(i, r, e) for i in range(nx) for r in cols[2] for e in range(2)]
    return sources, codes


def code_tile(side_ref, codes, ny, shape):
    rows = lax.broadcasted_iota(jnp.int32, shape, 0)
    lanes = lax.broadcasted_iota(jnp.int32, shape, 1)
    tile = jnp.zeros(shape, jnp.float32)
    for k, (i, j, e) in enumerate(codes):
        value = side_ref[(i * ny + j) * 2 + e].astype(jnp.float32)
        tile = jnp.where((rows == 0) & (lanes == k), value, tile)
    return tile


def pack_kernel(side_ref, fine_ref, lead_ref, factor_ref, *out_refs):
    nx, ny = fine_ref.shape[0], fine_ref.shape[1]
    width = fine_ref.shape[-1]
    named = {"fine": fine_ref, "lead": lead_ref, "factor": factor_ref}
    for out, side in zip(out_refs[:4], ("xhi", "xlo", "yhi", "ylo")):
        sources, codes = face_sources(nx, ny, side)
        for k, (name, at) in enumerate(sources):
            out[k // 2, :, (k % 2) * width : (k % 2 + 1) * width] = named[name][at]
        last = len(sources)
        out[last // 2] = code_tile(side_ref, codes, ny, out.shape[1:])
    for out, (sx, sy) in zip(out_refs[4:], ((1, 1), (1, -1), (-1, 1), (-1, -1))):
        rows2 = range(nx - 2, nx) if sx == 1 else range(2)
        cols2 = range(ny - 2, ny) if sy == 1 else range(2)
        row1 = nx - 1 if sx == 1 else 0
        col1 = ny - 1 if sy == 1 else 0
        blocks = [fine_ref[a, b] for a in rows2 for b in cols2]
        blocks += [lead_ref[row1, col1, e] for e in range(2)]
        for k, value in enumerate(blocks):
            out[k // 2, :, (k % 2) * width : (k % 2 + 1) * width] = value
        out[len(blocks) // 2] = code_tile(side_ref, [(row1, col1, 0), (row1, col1, 1)], ny,
                                          out.shape[1:])


def pack_buffers(stencil, fine_own, lead_own, factor_own):
    nx, ny = fine_own.shape[:2]
    blk = fine_own.shape[2:]
    face_count = len(face_sources(nx, ny, "xhi")[0]) + 1
    face_y_count = len(face_sources(nx, ny, "yhi")[0]) + 1
    vmem = pl.BlockSpec(memory_space=pltpu.VMEM)
    smem = pl.BlockSpec(memory_space=pltpu.SMEM)
    paired = lambda count: jax.ShapeDtypeStruct(((count + 1) // 2, blk[0], 2 * blk[1]), jnp.float32)
    shapes = [paired(face_count)] * 2 + [paired(face_y_count)] * 2
    shapes += [paired(7)] * 4
    return pl.pallas_call(
        pack_kernel,
        out_shape=tuple(shapes),
        in_specs=[smem, vmem, vmem, vmem],
        out_specs=tuple([vmem] * 8),
    )(stencil.reshape(-1), fine_own, lead_own, factor_own)


def local_compute(side_flat, slot_table, fine_own, lead_own, factor_own, minus_own, buffers):
    nx, ny = fine_own.shape[:2]
    blk = fine_own.shape[2:]
    vmem = pl.BlockSpec(memory_space=pltpu.VMEM)
    smem = pl.BlockSpec(memory_space=pltpu.SMEM)
    f32 = jnp.float32
    strong, restrict = pl.pallas_call(
        local_kernel,
        out_shape=(jax.ShapeDtypeStruct((nx * ny * 2, 1, 128), f32),
                   jax.ShapeDtypeStruct((CAP, 14) + blk, jnp.bfloat16)),
        in_specs=[smem, smem] + [vmem] * (4 + len(buffers)),
        out_specs=(vmem, vmem),
        scratch_shapes=[
            pltpu.VMEM((nx + 6, ny + 6) + blk, f32),
            pltpu.VMEM((nx + 4, ny + 4, 2) + blk, f32),
            pltpu.VMEM((nx + 2, ny + 2) + blk, f32),
            pltpu.VMEM((nx + 4, ny + 4, 2) + blk, f32),
            pltpu.VMEM((nx + 2, ny + 2, 7) + blk, f32),
        ],
        compiler_params=pltpu.CompilerParams(vmem_limit_bytes=60 * 1024 * 1024),
    )(side_flat, slot_table, fine_own, lead_own, factor_own, minus_own, *buffers)
    return strong[:, 0, 0].reshape(nx, ny, 2), restrict


def on_device(inv_factors, couplings, stencil, coarse):
    nx, ny, flat = inv_factors.shape
    order = math.isqrt(flat)
    blk = (order, order)
    n_gx = lax.axis_size("gx")
    n_gy = lax.axis_size("gy")
    total_x = nx * n_gx
    total_y = ny * n_gy
    coord_x = lax.axis_index("gx") * nx + jnp.arange(nx, dtype=jnp.int32)
    coord_y = lax.axis_index("gy") * ny + jnp.arange(ny, dtype=jnp.int32)
    target_x = coord_x[:, None] + 2 * stencil[:, :, 0] - 1
    target_y = coord_y[None, :] + 2 * stencil[:, :, 1] - 1
    reach = jnp.stack(
        [(target_x >= 0) & (target_x < total_x), (target_y >= 0) & (target_y < total_y)], axis=-1
    )
    minus_own = (couplings * (-reach.astype(jnp.float32))[:, :, :, None]).reshape(
        (nx, ny, 2) + blk
    )
    factor_own = inv_factors.reshape((nx, ny) + blk)
    fine_own = (1 - coarse).astype(jnp.float32)[:, :, None, None] * left_gram(
        factor_own, factor_own
    )
    lead_own = matmul(fine_own[:, :, None], minus_own)

    packed = pack_buffers(stencil, fine_own, lead_own, factor_own)
    from_xlo = lax.ppermute(packed[0], "gx", shift_pairs(n_gx, 1))
    from_xhi = lax.ppermute(packed[1], "gx", shift_pairs(n_gx, -1))
    from_ylo = lax.ppermute(packed[2], "gy", shift_pairs(n_gy, 1))
    from_yhi = lax.ppermute(packed[3], "gy", shift_pairs(n_gy, -1))
    corners = {}
    for step, buffer in zip(((1, 1), (1, -1), (-1, 1), (-1, -1)), packed[4:]):
        corners[step] = lax.ppermute(buffer, ("gx", "gy"),
                                     corner_pairs(n_gx, n_gy, *step))

    def face_codes(buffer, count, along_x):
        at = 3 * count + 2 * count * 2 + count
        codes = buffer[at // 2, 0, (at % 2) * order : (at % 2) * order + 2 * count * 2]
        codes = codes.astype(jnp.int32)
        return codes.reshape((2, count, 2) if along_x else (count, 2, 2))

    cxl = face_codes(from_xlo, ny, True)
    cxh = face_codes(from_xhi, ny, True)
    cyl = face_codes(from_ylo, nx, False)
    cyh = face_codes(from_yhi, nx, False)

    def unpack_corner(buffer):
        return (None, None, buffer[3, 0, 0:2].astype(jnp.int32).reshape(1, 1, 2))

    c_ll = unpack_corner(corners[(1, 1)])
    c_lh = unpack_corner(corners[(1, -1)])
    c_hl = unpack_corner(corners[(-1, 1)])
    c_hh = unpack_corner(corners[(-1, -1)])

    def cycle(k, lo_x, own, hi_x, lo_y, hi_y):
        return jnp.concatenate(
            [
                row_band([padded(c_ll[k], True, True), lo_x, padded(c_lh[k], True, False)]),
                row_band([lo_y, own, hi_y]),
                row_band([padded(c_hl[k], False, True), hi_x, padded(c_hh[k], False, False)]),
            ],
            axis=0,
        )

    side_cycle = cycle(2, cxl, stencil, cxh, cyl, cyh)

    cell_count = nx * ny
    flat_coarse = coarse.reshape(cell_count)
    slot_rank = jnp.cumsum(flat_coarse, dtype=jnp.int32) - flat_coarse
    chosen = (
        (slot_rank[None, :] == jnp.arange(CAP, dtype=jnp.int32)[:, None])
        & (flat_coarse[None, :] == 1)
    ).astype(jnp.int32)
    source = jnp.sum(
        chosen * jnp.arange(cell_count, dtype=jnp.int32)[None, :], axis=1, dtype=jnp.int32
    )
    filled = jnp.sum(chosen, axis=1, dtype=jnp.int32)
    span = ny + 2
    own_i = jnp.arange(nx, dtype=jnp.int32)[:, None] + 1
    own_j = jnp.arange(ny, dtype=jnp.int32)[None, :] + 1
    up_index = jnp.stack(
        [(own_i + 2 * stencil[:, :, 0] - 1) * span + own_j,
         own_i * span + own_j + 2 * stencil[:, :, 1] - 1],
        axis=-1,
    ).reshape(cell_count, 2)
    picked = jnp.take(up_index, source, axis=0, mode="clip")
    slot_table = jnp.concatenate([source[:, None], picked, filled[:, None]], axis=1).reshape(-1)
    buffers = (from_xlo, from_xhi, from_ylo, from_yhi, corners[(1, 1)], corners[(1, -1)],
               corners[(-1, 1)], corners[(-1, -1)])
    strong, restrict = local_compute(side_cycle.reshape(-1), slot_table, fine_own, lead_own,
                                     factor_own, minus_own, buffers)
    return (strong, restrict.reshape(CAP, 14, flat))


def solution(mesh):
    placed = (P("gx", "gy", None), P("gx", "gy", None, None), P("gx", "gy", None), P("gx", "gy"))
    return jax.shard_map(
        on_device,
        mesh=mesh,
        in_specs=placed,
        out_specs=(P("gx", "gy", None), P(("gx", "gy"), None, None)),
        check_vma=False,
    )
```

```python
import math

import jax
import jax.numpy as jnp
from jax import lax
from jax.experimental import pallas as pl
from jax.experimental.pallas import tpu as pltpu
from jax.sharding import PartitionSpec as P

CAP = 12
PREC = lax.Precision.HIGH


def left_gram(left_block, right_block):
    return jnp.einsum("...ji,...jk->...ik", left_block, right_block, precision=PREC)


def shift_pairs(count, step):
    return [(i, i + step) for i in range(count) if 0 <= i + step < count]


def corner_pairs(n_x, n_y, step_x, step_y):
    pairs = []
    for a in range(n_x):
        for b in range(n_y):
            if 0 <= a + step_x < n_x and 0 <= b + step_y < n_y:
                pairs.append((a * n_y + b, (a + step_x) * n_y + (b + step_y)))
    return pairs


def row_band(pieces):
    return jnp.concatenate(pieces, axis=1)


def padded(values, before_x, before_y):
    widths = [(1, 0) if before_x else (0, 1), (1, 0) if before_y else (0, 1)]
    widths += [(0, 0)] * (values.ndim - 2)
    return jnp.pad(values, widths)


def split(value):
    high = value.astype(jnp.bfloat16)
    low = (value - high.astype(jnp.float32)).astype(jnp.bfloat16)
    return high, low


def dot3(left, right, right_t=False):
    dims = (((1,), (1,)), ((), ())) if right_t else (((1,), (0,)), ((), ()))

    def one(a, b):
        return lax.dot_general(a, b, dims, preferred_element_type=jnp.float32)

    return one(left[0], right[0]) + one(left[0], right[1]) + one(left[1], right[0])


def local_kernel(side_ref, slot_ref, fine_ref, lead_ref, factor_ref, minus_ref,
                 xlo_ref, xhi_ref, ylo_ref, yhi_ref, cll_ref, clh_ref, chl_ref, chh_ref,
                 strong_ref, restrict_ref, pg, wg, gg, yg, zg):
    nx, ny = fine_ref.shape[0], fine_ref.shape[1]
    blk = fine_ref.shape[2:]
    zero = jnp.zeros(blk, jnp.float32)
    wide_x, wide_y = nx + 4, ny + 4
    pg_src, wg_src, gg_src = {}, {}, {}
    for i in range(nx):
        for j in range(ny):
            pg_src[(3 + i, 3 + j)] = (fine_ref, (i, j))
            gg_src[(1 + i, 1 + j)] = (factor_ref, (i, j))
            for e in range(2):
                wg_src[(2 + i, 2 + j, e)] = (lead_ref, (i, j, e))
    for c in range(ny):
        for r in range(3):
            pg_src[(r, 3 + c)] = (xlo_ref, (r * ny + c,))
            pg_src[(nx + 3 + r, 3 + c)] = (xhi_ref, (r * ny + c,))
        for r in range(2):
            for e in range(2):
                wg_src[(r, 2 + c, e)] = (xlo_ref, (3 * ny + (r * ny + c) * 2 + e,))
                wg_src[(nx + 2 + r, 2 + c, e)] = (xhi_ref, (3 * ny + (r * ny + c) * 2 + e,))
        gg_src[(0, 1 + c)] = (xlo_ref, (7 * ny + c,))
        gg_src[(nx + 1, 1 + c)] = (xhi_ref, (7 * ny + c,))
    for i in range(nx):
        for r in range(3):
            pg_src[(3 + i, r)] = (ylo_ref, (i * 3 + r,))
            pg_src[(3 + i, ny + 3 + r)] = (yhi_ref, (i * 3 + r,))
        for r in range(2):
            for e in range(2):
                wg_src[(2 + i, r, e)] = (ylo_ref, (3 * nx + (i * 2 + r) * 2 + e,))
                wg_src[(2 + i, ny + 2 + r, e)] = (yhi_ref, (3 * nx + (i * 2 + r) * 2 + e,))
        gg_src[(1 + i, 0)] = (ylo_ref, (7 * nx + i,))
        gg_src[(1 + i, ny + 1)] = (yhi_ref, (7 * nx + i,))
    for ref, px, py, wx, wy in ((cll_ref, 1, 1, 1, 1), (clh_ref, 1, ny + 3, 1, ny + 2),
                                (chl_ref, nx + 3, 1, nx + 2, 1),
                                (chh_ref, nx + 3, ny + 3, nx + 2, ny + 2)):
        for a in range(2):
            for b in range(2):
                pg_src[(px + a, py + b)] = (ref, (a * 2 + b,))
        for e in range(2):
            wg_src[(wx, wy, e)] = (ref, (4 + e,))

    def block(ref, at):
        if ref is None:
            return zero
        if len(at) == 1 and ref.shape[-1] == 2 * blk[-1]:
            half = at[0] % 2
            return ref[at[0] // 2, :, half * blk[-1] : (half + 1) * blk[-1]]
        return ref[at]

    for i in range(nx + 6):
        for j in range(ny + 6):
            pg[i, j] = block(*pg_src.get((i, j), (None, None)))
    for i in range(wide_x):
        for j in range(wide_y):
            for e in range(2):
                wg[i, j, e] = block(*wg_src.get((i, j, e), (None, None)))
    for i in range(nx + 2):
        for j in range(ny + 2):
            gg[i, j] = block(*gg_src.get((i, j), (None, None)))

    def side(i, j, d):
        return side_ref[(i * wide_y + j) * 2 + d]

    def outside(k, low, size):
        return max(low - k, k - (low + size - 1), 0)

    for i in range(wide_x):
        for j in range(wide_y):
            if outside(i, 2, nx) + outside(j, 2, ny) > 2:
                continue
            sx = side(i, j, 0)
            sy = side(i, j, 1)
            yg[i, j, 0] = dot3(split(wg[i, j, 0]), split(pg[i + 2 * sx, j + 1]))
            yg[i, j, 1] = dot3(split(wg[i, j, 1]), split(pg[i + 1, j + 2 * sy]))

    for i in range(nx + 2):
        for j in range(ny + 2):
            if outside(i, 1, nx) + outside(j, 1, ny) > 1:
                continue
            zg[i, j, 0] = pg[i + 2, j + 2]
            for e in range(2):
                s = side(i + 1, j + 1, e)
                ui = i + 2 * s if e == 0 else i + 1
                uj = j + 1 if e == 0 else j + 2 * s
                lead = split(wg[i + 1, j + 1, e])
                zg[i, j, 1 + 3 * e] = dot3(lead, split(pg[ui + 1, uj + 1]))
                zg[i, j, 2 + 3 * e] = dot3(lead, split(yg[ui, uj, 0]))
                zg[i, j, 3 + 3 * e] = dot3(lead, split(yg[ui, uj, 1]))

    def strong_step(p, carry):
        i = p // ny
        j = p % ny
        factor = split(factor_ref[i, j])
        for d in range(2):
            s = side(i + 2, j + 2, d)
            up = gg[i + 2 * s, j + 1] if d == 0 else gg[i + 1, j + 2 * s]
            scaled = dot3(split(dot3(factor, split(minus_ref[i, j, d]))), split(up), True)
            total = jnp.sum(scaled * scaled, axis=(0, 1), keepdims=True)
            strong_ref[pl.ds(p * 2 + d, 1), :] = jnp.broadcast_to(total * (1.0 / scaled.size),
                                                                 (1, 128))
        return carry

    lax.fori_loop(0, nx * ny, strong_step, 0, unroll=True)

    def slot_step(s, carry):
        cell = slot_ref[s * 4]
        weight = slot_ref[s * 4 + 3].astype(jnp.float32)
        ci = cell // ny
        cj = cell % ny
        for d in range(2):
            n = slot_ref[s * 4 + 1 + d]
            ni = n // (ny + 2)
            nj = n % (ny + 2)
            coupling = split(minus_ref[ci, cj, d])
            for w in range(7):
                row = dot3(coupling, split(zg[ni, nj, w]))
                restrict_ref[s, d * 7 + w] = (row * weight).astype(restrict_ref.dtype)
        return carry

    lax.fori_loop(0, restrict_ref.shape[0], slot_step, 0, unroll=True)


def face_sources(nx, ny, side):
    sources = []
    if side in ("xhi", "xlo"):
        rows = {d: (range(nx - d, nx) if side == "xhi" else range(d)) for d in (1, 2, 3)}
        for r in rows[3]:
            for c in range(ny):
                sources.append(("fine", (r, c)))
        for r in rows[2]:
            for c in range(ny):
                for e in range(2):
                    sources.append(("lead", (r, c, e)))
        for r in rows[1]:
            for c in range(ny):
                sources.append(("factor", (r, c)))
        codes = [(r, c, e) for r in rows[2] for c in range(ny) for e in range(2)]
    else:
        cols = {d: (range(ny - d, ny) if side == "yhi" else range(d)) for d in (1, 2, 3)}
        for i in range(nx):
            for r in cols[3]:
                sources.append(("fine", (i, r)))
        for i in range(nx):
            for r in cols[2]:
                for e in range(2):
                    sources.append(("lead", (i, r, e)))
        for i in range(nx):
            for r in cols[1]:
                sources.append(("factor", (i, r)))
        codes = [(i, r, e) for i in range(nx) for r in cols[2] for e in range(2)]
    return sources, codes


def code_tile(side_ref, codes, ny, shape):
    rows = lax.broadcasted_iota(jnp.int32, shape, 0)
    lanes = lax.broadcasted_iota(jnp.int32, shape, 1)
    tile = jnp.zeros(shape, jnp.float32)
    for k, (i, j, e) in enumerate(codes):
        value = side_ref[(i * ny + j) * 2 + e].astype(jnp.float32)
        tile = jnp.where((rows == 0) & (lanes == k), value, tile)
    return tile


def pack_kernel(side_ref, fine_ref, minus_ref, factor_ref, lead_ref, *out_refs):
    nx, ny = fine_ref.shape[0], fine_ref.shape[1]
    width = fine_ref.shape[-1]
    for i in range(nx):
        for j in range(ny):
            fine = split(fine_ref[i, j])
            for e in range(2):
                lead_ref[i, j, e] = dot3(fine, split(minus_ref[i, j, e]))
    named = {"fine": fine_ref, "lead": lead_ref, "factor": factor_ref}
    for out, side in zip(out_refs[:4], ("xhi", "xlo", "yhi", "ylo")):
        sources, codes = face_sources(nx, ny, side)
        for k, (name, at) in enumerate(sources):
            out[k // 2, :, (k % 2) * width : (k % 2 + 1) * width] = named[name][at]
        last = len(sources)
        out[last // 2] = code_tile(side_ref, codes, ny, out.shape[1:])
    for out, (sx, sy) in zip(out_refs[4:], ((1, 1), (1, -1), (-1, 1), (-1, -1))):
        rows2 = range(nx - 2, nx) if sx == 1 else range(2)
        cols2 = range(ny - 2, ny) if sy == 1 else range(2)
        row1 = nx - 1 if sx == 1 else 0
        col1 = ny - 1 if sy == 1 else 0
        blocks = [fine_ref[a, b] for a in rows2 for b in cols2]
        blocks += [lead_ref[row1, col1, e] for e in range(2)]
        for k, value in enumerate(blocks):
            out[k // 2, :, (k % 2) * width : (k % 2 + 1) * width] = value
        out[len(blocks) // 2] = code_tile(side_ref, [(row1, col1, 0), (row1, col1, 1)], ny,
                                          out.shape[1:])


def pack_buffers(stencil, fine_own, minus_own, factor_own):
    nx, ny = fine_own.shape[:2]
    blk = fine_own.shape[2:]
    face_count = len(face_sources(nx, ny, "xhi")[0]) + 1
    face_y_count = len(face_sources(nx, ny, "yhi")[0]) + 1
    vmem = pl.BlockSpec(memory_space=pltpu.VMEM)
    smem = pl.BlockSpec(memory_space=pltpu.SMEM)
    paired = lambda count: jax.ShapeDtypeStruct(((count + 1) // 2, blk[0], 2 * blk[1]), jnp.float32)
    shapes = [paired(face_count)] * 2 + [paired(face_y_count)] * 2
    shapes += [paired(7)] * 4
    shapes = [jax.ShapeDtypeStruct(minus_own.shape, jnp.float32)] + shapes
    return pl.pallas_call(
        pack_kernel,
        out_shape=tuple(shapes),
        in_specs=[smem, vmem, vmem, vmem],
        out_specs=tuple([vmem] * 9),
    )(stencil.reshape(-1), fine_own, minus_own, factor_own)


def local_compute(side_flat, slot_table, fine_own, lead_own, factor_own, minus_own, buffers):
    nx, ny = fine_own.shape[:2]
    blk = fine_own.shape[2:]
    vmem = pl.BlockSpec(memory_space=pltpu.VMEM)
    smem = pl.BlockSpec(memory_space=pltpu.SMEM)
    f32 = jnp.float32
    strong, restrict = pl.pallas_call(
        local_kernel,
        out_shape=(jax.ShapeDtypeStruct((nx * ny * 2, 128), f32),
                   jax.ShapeDtypeStruct((CAP, 14) + blk, jnp.bfloat16)),
        in_specs=[smem, smem] + [vmem] * (4 + len(buffers)),
        out_specs=(vmem, vmem),
        scratch_shapes=[
            pltpu.VMEM((nx + 6, ny + 6) + blk, f32),
            pltpu.VMEM((nx + 4, ny + 4, 2) + blk, f32),
            pltpu.VMEM((nx + 2, ny + 2) + blk, f32),
            pltpu.VMEM((nx + 4, ny + 4, 2) + blk, f32),
            pltpu.VMEM((nx + 2, ny + 2, 7) + blk, f32),
        ],
        compiler_params=pltpu.CompilerParams(vmem_limit_bytes=60 * 1024 * 1024),
    )(side_flat, slot_table, fine_own, lead_own, factor_own, minus_own, *buffers)
    return strong[:, 0].reshape(nx, ny, 2), restrict


def on_device(inv_factors, couplings, stencil, coarse):
    nx, ny, flat = inv_factors.shape
    order = math.isqrt(flat)
    blk = (order, order)
    n_gx = lax.axis_size("gx")
    n_gy = lax.axis_size("gy")
    total_x = nx * n_gx
    total_y = ny * n_gy
    coord_x = lax.axis_index("gx") * nx + jnp.arange(nx, dtype=jnp.int32)
    coord_y = lax.axis_index("gy") * ny + jnp.arange(ny, dtype=jnp.int32)
    target_x = coord_x[:, None] + 2 * stencil[:, :, 0] - 1
    target_y = coord_y[None, :] + 2 * stencil[:, :, 1] - 1
    reach = jnp.stack(
        [(target_x >= 0) & (target_x < total_x), (target_y >= 0) & (target_y < total_y)], axis=-1
    )
    minus_own = (couplings * (-reach.astype(jnp.float32))[:, :, :, None]).reshape(
        (nx, ny, 2) + blk
    )
    factor_own = inv_factors.reshape((nx, ny) + blk)
    fine_own = (1 - coarse).astype(jnp.float32)[:, :, None, None] * left_gram(
        factor_own, factor_own
    )

    lead_own, *packed = pack_buffers(stencil, fine_own, minus_own, factor_own)
    from_xlo = lax.ppermute(packed[0], "gx", shift_pairs(n_gx, 1))
    from_xhi = lax.ppermute(packed[1], "gx", shift_pairs(n_gx, -1))
    from_ylo = lax.ppermute(packed[2], "gy", shift_pairs(n_gy, 1))
    from_yhi = lax.ppermute(packed[3], "gy", shift_pairs(n_gy, -1))
    corners = {}
    for step, buffer in zip(((1, 1), (1, -1), (-1, 1), (-1, -1)), packed[4:]):
        corners[step] = lax.ppermute(buffer, ("gx", "gy"),
                                     corner_pairs(n_gx, n_gy, *step))

    def face_codes(buffer, count, along_x):
        at = 3 * count + 2 * count * 2 + count
        codes = buffer[at // 2, 0, (at % 2) * order : (at % 2) * order + 2 * count * 2]
        codes = codes.astype(jnp.int32)
        return codes.reshape((2, count, 2) if along_x else (count, 2, 2))

    cxl = face_codes(from_xlo, ny, True)
    cxh = face_codes(from_xhi, ny, True)
    cyl = face_codes(from_ylo, nx, False)
    cyh = face_codes(from_yhi, nx, False)

    def unpack_corner(buffer):
        return (None, None, buffer[3, 0, 0:2].astype(jnp.int32).reshape(1, 1, 2))

    c_ll = unpack_corner(corners[(1, 1)])
    c_lh = unpack_corner(corners[(1, -1)])
    c_hl = unpack_corner(corners[(-1, 1)])
    c_hh = unpack_corner(corners[(-1, -1)])

    def cycle(k, lo_x, own, hi_x, lo_y, hi_y):
        return jnp.concatenate(
            [
                row_band([padded(c_ll[k], True, True), lo_x, padded(c_lh[k], True, False)]),
                row_band([lo_y, own, hi_y]),
                row_band([padded(c_hl[k], False, True), hi_x, padded(c_hh[k], False, False)]),
            ],
            axis=0,
        )

    side_cycle = cycle(2, cxl, stencil, cxh, cyl, cyh)

    cell_count = nx * ny
    flat_coarse = coarse.reshape(cell_count)
    slot_rank = jnp.cumsum(flat_coarse, dtype=jnp.int32) - flat_coarse
    chosen = (
        (slot_rank[None, :] == jnp.arange(CAP, dtype=jnp.int32)[:, None])
        & (flat_coarse[None, :] == 1)
    ).astype(jnp.int32)
    source = jnp.sum(
        chosen * jnp.arange(cell_count, dtype=jnp.int32)[None, :], axis=1, dtype=jnp.int32
    )
    filled = jnp.sum(chosen, axis=1, dtype=jnp.int32)
    span = ny + 2
    own_i = jnp.arange(nx, dtype=jnp.int32)[:, None] + 1
    own_j = jnp.arange(ny, dtype=jnp.int32)[None, :] + 1
    up_index = jnp.stack(
        [(own_i + 2 * stencil[:, :, 0] - 1) * span + own_j,
         own_i * span + own_j + 2 * stencil[:, :, 1] - 1],
        axis=-1,
    ).reshape(cell_count, 2)
    picked = jnp.take(up_index, source, axis=0, mode="clip")
    slot_table = jnp.concatenate([source[:, None], picked, filled[:, None]], axis=1).reshape(-1)
    buffers = (from_xlo, from_xhi, from_ylo, from_yhi, corners[(1, 1)], corners[(1, -1)],
               corners[(-1, 1)], corners[(-1, -1)])
    strong, restrict = local_compute(side_cycle.reshape(-1), slot_table, fine_own, lead_own,
                                     factor_own, minus_own, buffers)
    return (strong, restrict.reshape(CAP, 14, flat))


def solution(mesh):
    placed = (P("gx", "gy", None), P("gx", "gy", None, None), P("gx", "gy", None), P("gx", "gy"))
    return jax.shard_map(
        on_device,
        mesh=mesh,
        in_specs=placed,
        out_specs=(P("gx", "gy", None), P(("gx", "gy"), None, None)),
        check_vma=False,
    )
```

```python
import math

import jax
import jax.numpy as jnp
from jax import lax
from jax.experimental import pallas as pl
from jax.experimental.pallas import tpu as pltpu
from jax.sharding import PartitionSpec as P

CAP = 12
PREC = lax.Precision.HIGH


def left_gram(left_block, right_block):
    return jnp.einsum("...ji,...jk->...ik", left_block, right_block, precision=PREC)


def shift_pairs(count, step):
    return [(i, i + step) for i in range(count) if 0 <= i + step < count]


def corner_pairs(n_x, n_y, step_x, step_y):
    pairs = []
    for a in range(n_x):
        for b in range(n_y):
            if 0 <= a + step_x < n_x and 0 <= b + step_y < n_y:
                pairs.append((a * n_y + b, (a + step_x) * n_y + (b + step_y)))
    return pairs


def row_band(pieces):
    return jnp.concatenate(pieces, axis=1)


def padded(values, before_x, before_y):
    widths = [(1, 0) if before_x else (0, 1), (1, 0) if before_y else (0, 1)]
    widths += [(0, 0)] * (values.ndim - 2)
    return jnp.pad(values, widths)


def split(value):
    high = value.astype(jnp.bfloat16)
    low = (value - high.astype(jnp.float32)).astype(jnp.bfloat16)
    return high, low


def dot3(left, right, right_t=False):
    dims = (((1,), (1,)), ((), ())) if right_t else (((1,), (0,)), ((), ()))

    def one(a, b):
        return lax.dot_general(a, b, dims, preferred_element_type=jnp.float32)

    return one(left[0], right[0]) + one(left[0], right[1]) + one(left[1], right[0])


def local_kernel(side_ref, slot_ref, fine_ref, lead_ref, factor_ref, minus_ref,
                 xlo_ref, xhi_ref, ylo_ref, yhi_ref, cll_ref, clh_ref, chl_ref, chh_ref,
                 strong_ref, restrict_ref, pg, wg, gg, yg, zg):
    nx, ny = fine_ref.shape[0], fine_ref.shape[1]
    blk = fine_ref.shape[2:]
    zero = jnp.zeros(blk, jnp.float32)
    wide_x, wide_y = nx + 4, ny + 4
    pg_src, wg_src, gg_src = {}, {}, {}
    for i in range(nx):
        for j in range(ny):
            pg_src[(3 + i, 3 + j)] = (fine_ref, (i, j))
            gg_src[(1 + i, 1 + j)] = (factor_ref, (i, j))
            for e in range(2):
                wg_src[(2 + i, 2 + j, e)] = (lead_ref, (i, j, e))
    for c in range(ny):
        for r in range(3):
            pg_src[(r, 3 + c)] = (xlo_ref, (r * ny + c,))
            pg_src[(nx + 3 + r, 3 + c)] = (xhi_ref, (r * ny + c,))
        for r in range(2):
            for e in range(2):
                wg_src[(r, 2 + c, e)] = (xlo_ref, (3 * ny + (r * ny + c) * 2 + e,))
                wg_src[(nx + 2 + r, 2 + c, e)] = (xhi_ref, (3 * ny + (r * ny + c) * 2 + e,))
        gg_src[(0, 1 + c)] = (xlo_ref, (7 * ny + c,))
        gg_src[(nx + 1, 1 + c)] = (xhi_ref, (7 * ny + c,))
    for i in range(nx):
        for r in range(3):
            pg_src[(3 + i, r)] = (ylo_ref, (i * 3 + r,))
            pg_src[(3 + i, ny + 3 + r)] = (yhi_ref, (i * 3 + r,))
        for r in range(2):
            for e in range(2):
                wg_src[(2 + i, r, e)] = (ylo_ref, (3 * nx + (i * 2 + r) * 2 + e,))
                wg_src[(2 + i, ny + 2 + r, e)] = (yhi_ref, (3 * nx + (i * 2 + r) * 2 + e,))
        gg_src[(1 + i, 0)] = (ylo_ref, (7 * nx + i,))
        gg_src[(1 + i, ny + 1)] = (yhi_ref, (7 * nx + i,))
    for ref, px, py, wx, wy in ((cll_ref, 1, 1, 1, 1), (clh_ref, 1, ny + 3, 1, ny + 2),
                                (chl_ref, nx + 3, 1, nx + 2, 1),
                                (chh_ref, nx + 3, ny + 3, nx + 2, ny + 2)):
        for a in range(2):
            for b in range(2):
                pg_src[(px + a, py + b)] = (ref, (a * 2 + b,))
        for e in range(2):
            wg_src[(wx, wy, e)] = (ref, (4 + e,))

    def block(ref, at):
        if ref is None:
            return zero
        if len(at) == 1 and ref.shape[-1] == 2 * blk[-1]:
            half = at[0] % 2
            return ref[at[0] // 2, :, half * blk[-1] : (half + 1) * blk[-1]]
        return ref[at]

    for i in range(nx + 6):
        for j in range(ny + 6):
            pg[i, j] = block(*pg_src.get((i, j), (None, None)))
    for i in range(wide_x):
        for j in range(wide_y):
            for e in range(2):
                wg[i, j, e] = block(*wg_src.get((i, j, e), (None, None)))
    for i in range(nx + 2):
        for j in range(ny + 2):
            gg[i, j] = block(*gg_src.get((i, j), (None, None)))

    def side(i, j, d):
        return side_ref[(i * wide_y + j) * 2 + d]

    def outside(k, low, size):
        return max(low - k, k - (low + size - 1), 0)

    for i in range(wide_x):
        for j in range(wide_y):
            if outside(i, 2, nx) + outside(j, 2, ny) > 2:
                continue
            sx = side(i, j, 0)
            sy = side(i, j, 1)
            yg[i, j, 0] = dot3(split(wg[i, j, 0]), split(pg[i + 2 * sx, j + 1]))
            yg[i, j, 1] = dot3(split(wg[i, j, 1]), split(pg[i + 1, j + 2 * sy]))

    for i in range(nx + 2):
        for j in range(ny + 2):
            if outside(i, 1, nx) + outside(j, 1, ny) > 1:
                continue
            zg[i, j, 0] = pg[i + 2, j + 2]
            for e in range(2):
                s = side(i + 1, j + 1, e)
                ui = i + 2 * s if e == 0 else i + 1
                uj = j + 1 if e == 0 else j + 2 * s
                lead = split(wg[i + 1, j + 1, e])
                zg[i, j, 1 + 3 * e] = dot3(lead, split(pg[ui + 1, uj + 1]))
                zg[i, j, 2 + 3 * e] = dot3(lead, split(yg[ui, uj, 0]))
                zg[i, j, 3 + 3 * e] = dot3(lead, split(yg[ui, uj, 1]))

    for p in range(nx * ny):
        i = p // ny
        j = p % ny
        factor = split(factor_ref[i, j])
        for d in range(2):
            s = side(i + 2, j + 2, d)
            up = gg[i + 2 * s, j + 1] if d == 0 else gg[i + 1, j + 2 * s]
            scaled = dot3(split(dot3(factor, split(minus_ref[i, j, d]))), split(up), True)
            total = jnp.sum(scaled * scaled, axis=(0, 1), keepdims=True)
            strong_ref[pl.ds(p * 2 + d, 1), :] = jnp.broadcast_to(total * (1.0 / scaled.size),
                                                                 (1, 128))


    def slot_step(s, carry):
        cell = slot_ref[s * 4]
        weight = slot_ref[s * 4 + 3].astype(jnp.float32)
        ci = cell // ny
        cj = cell % ny
        for d in range(2):
            n = slot_ref[s * 4 + 1 + d]
            ni = n // (ny + 2)
            nj = n % (ny + 2)
            coupling = split(minus_ref[ci, cj, d])
            for w in range(7):
                row = dot3(coupling, split(zg[ni, nj, w]))
                restrict_ref[s, d * 7 + w] = (row * weight).astype(restrict_ref.dtype)
        return carry

    lax.fori_loop(0, restrict_ref.shape[0], slot_step, 0, unroll=True)


def face_sources(nx, ny, side):
    sources = []
    if side in ("xhi", "xlo"):
        rows = {d: (range(nx - d, nx) if side == "xhi" else range(d)) for d in (1, 2, 3)}
        for r in rows[3]:
            for c in range(ny):
                sources.append(("fine", (r, c)))
        for r in rows[2]:
            for c in range(ny):
                for e in range(2):
                    sources.append(("lead", (r, c, e)))
        for r in rows[1]:
            for c in range(ny):
                sources.append(("factor", (r, c)))
        codes = [(r, c, e) for r in rows[2] for c in range(ny) for e in range(2)]
    else:
        cols = {d: (range(ny - d, ny) if side == "yhi" else range(d)) for d in (1, 2, 3)}
        for i in range(nx):
            for r in cols[3]:
                sources.append(("fine", (i, r)))
        for i in range(nx):
            for r in cols[2]:
                for e in range(2):
                    sources.append(("lead", (i, r, e)))
        for i in range(nx):
            for r in cols[1]:
                sources.append(("factor", (i, r)))
        codes = [(i, r, e) for i in range(nx) for r in cols[2] for e in range(2)]
    return sources, codes


def code_tile(side_ref, codes, ny, shape):
    rows = lax.broadcasted_iota(jnp.int32, shape, 0)
    lanes = lax.broadcasted_iota(jnp.int32, shape, 1)
    tile = jnp.zeros(shape, jnp.float32)
    for k, (i, j, e) in enumerate(codes):
        value = side_ref[(i * ny + j) * 2 + e].astype(jnp.float32)
        tile = jnp.where((rows == 0) & (lanes == k), value, tile)
    return tile


def pack_kernel(side_ref, fine_ref, minus_ref, factor_ref, lead_ref, *out_refs):
    nx, ny = fine_ref.shape[0], fine_ref.shape[1]
    width = fine_ref.shape[-1]
    for i in range(nx):
        for j in range(ny):
            fine = split(fine_ref[i, j])
            for e in range(2):
                lead_ref[i, j, e] = dot3(fine, split(minus_ref[i, j, e]))
    named = {"fine": fine_ref, "lead": lead_ref, "factor": factor_ref}
    for out, side in zip(out_refs[:4], ("xhi", "xlo", "yhi", "ylo")):
        sources, codes = face_sources(nx, ny, side)
        for k, (name, at) in enumerate(sources):
            out[k // 2, :, (k % 2) * width : (k % 2 + 1) * width] = named[name][at]
        last = len(sources)
        out[last // 2] = code_tile(side_ref, codes, ny, out.shape[1:])
    for out, (sx, sy) in zip(out_refs[4:], ((1, 1), (1, -1), (-1, 1), (-1, -1))):
        rows2 = range(nx - 2, nx) if sx == 1 else range(2)
        cols2 = range(ny - 2, ny) if sy == 1 else range(2)
        row1 = nx - 1 if sx == 1 else 0
        col1 = ny - 1 if sy == 1 else 0
        blocks = [fine_ref[a, b] for a in rows2 for b in cols2]
        blocks += [lead_ref[row1, col1, e] for e in range(2)]
        for k, value in enumerate(blocks):
            out[k // 2, :, (k % 2) * width : (k % 2 + 1) * width] = value
        out[len(blocks) // 2] = code_tile(side_ref, [(row1, col1, 0), (row1, col1, 1)], ny,
                                          out.shape[1:])


def pack_buffers(stencil, fine_own, minus_own, factor_own):
    nx, ny = fine_own.shape[:2]
    blk = fine_own.shape[2:]
    face_count = len(face_sources(nx, ny, "xhi")[0]) + 1
    face_y_count = len(face_sources(nx, ny, "yhi")[0]) + 1
    vmem = pl.BlockSpec(memory_space=pltpu.VMEM)
    smem = pl.BlockSpec(memory_space=pltpu.SMEM)
    paired = lambda count: jax.ShapeDtypeStruct(((count + 1) // 2, blk[0], 2 * blk[1]), jnp.float32)
    shapes = [paired(face_count)] * 2 + [paired(face_y_count)] * 2
    shapes += [paired(7)] * 4
    shapes = [jax.ShapeDtypeStruct(minus_own.shape, jnp.float32)] + shapes
    return pl.pallas_call(
        pack_kernel,
        out_shape=tuple(shapes),
        in_specs=[smem, vmem, vmem, vmem],
        out_specs=tuple([vmem] * 9),
    )(stencil.reshape(-1), fine_own, minus_own, factor_own)


def local_compute(side_flat, slot_table, fine_own, lead_own, factor_own, minus_own, buffers):
    nx, ny = fine_own.shape[:2]
    blk = fine_own.shape[2:]
    vmem = pl.BlockSpec(memory_space=pltpu.VMEM)
    smem = pl.BlockSpec(memory_space=pltpu.SMEM)
    f32 = jnp.float32
    strong, restrict = pl.pallas_call(
        local_kernel,
        out_shape=(jax.ShapeDtypeStruct((nx * ny * 2, 128), f32),
                   jax.ShapeDtypeStruct((CAP, 14) + blk, jnp.bfloat16)),
        in_specs=[smem, smem] + [vmem] * (4 + len(buffers)),
        out_specs=(vmem, vmem),
        scratch_shapes=[
            pltpu.VMEM((nx + 6, ny + 6) + blk, f32),
            pltpu.VMEM((nx + 4, ny + 4, 2) + blk, f32),
            pltpu.VMEM((nx + 2, ny + 2) + blk, f32),
            pltpu.VMEM((nx + 4, ny + 4, 2) + blk, f32),
            pltpu.VMEM((nx + 2, ny + 2, 7) + blk, f32),
        ],
        compiler_params=pltpu.CompilerParams(vmem_limit_bytes=60 * 1024 * 1024),
    )(side_flat, slot_table, fine_own, lead_own, factor_own, minus_own, *buffers)
    return strong[:, 0].reshape(nx, ny, 2), restrict


def on_device(inv_factors, couplings, stencil, coarse):
    nx, ny, flat = inv_factors.shape
    order = math.isqrt(flat)
    blk = (order, order)
    n_gx = lax.axis_size("gx")
    n_gy = lax.axis_size("gy")
    total_x = nx * n_gx
    total_y = ny * n_gy
    coord_x = lax.axis_index("gx") * nx + jnp.arange(nx, dtype=jnp.int32)
    coord_y = lax.axis_index("gy") * ny + jnp.arange(ny, dtype=jnp.int32)
    target_x = coord_x[:, None] + 2 * stencil[:, :, 0] - 1
    target_y = coord_y[None, :] + 2 * stencil[:, :, 1] - 1
    reach = jnp.stack(
        [(target_x >= 0) & (target_x < total_x), (target_y >= 0) & (target_y < total_y)], axis=-1
    )
    minus_own = couplings.reshape((nx, ny, 2) + blk) * (-reach.astype(jnp.float32))[
        :, :, :, None, None
    ]
    factor_own = inv_factors.reshape((nx, ny) + blk)
    fine_own = (1 - coarse).astype(jnp.float32)[:, :, None, None] * left_gram(
        factor_own, factor_own
    )

    lead_own, *packed = pack_buffers(stencil, fine_own, minus_own, factor_own)
    from_xlo = lax.ppermute(packed[0], "gx", shift_pairs(n_gx, 1))
    from_xhi = lax.ppermute(packed[1], "gx", shift_pairs(n_gx, -1))
    from_ylo = lax.ppermute(packed[2], "gy", shift_pairs(n_gy, 1))
    from_yhi = lax.ppermute(packed[3], "gy", shift_pairs(n_gy, -1))
    corners = {}
    for step, buffer in zip(((1, 1), (1, -1), (-1, 1), (-1, -1)), packed[4:]):
        corners[step] = lax.ppermute(buffer, ("gx", "gy"),
                                     corner_pairs(n_gx, n_gy, *step))

    def face_codes(buffer, count, along_x):
        at = 3 * count + 2 * count * 2 + count
        codes = buffer[at // 2, 0, (at % 2) * order : (at % 2) * order + 2 * count * 2]
        codes = codes.astype(jnp.int32)
        return codes.reshape((2, count, 2) if along_x else (count, 2, 2))

    cxl = face_codes(from_xlo, ny, True)
    cxh = face_codes(from_xhi, ny, True)
    cyl = face_codes(from_ylo, nx, False)
    cyh = face_codes(from_yhi, nx, False)

    def unpack_corner(buffer):
        return (None, None, buffer[3, 0, 0:2].astype(jnp.int32).reshape(1, 1, 2))

    c_ll = unpack_corner(corners[(1, 1)])
    c_lh = unpack_corner(corners[(1, -1)])
    c_hl = unpack_corner(corners[(-1, 1)])
    c_hh = unpack_corner(corners[(-1, -1)])

    def cycle(k, lo_x, own, hi_x, lo_y, hi_y):
        return jnp.concatenate(
            [
                row_band([padded(c_ll[k], True, True), lo_x, padded(c_lh[k], True, False)]),
                row_band([lo_y, own, hi_y]),
                row_band([padded(c_hl[k], False, True), hi_x, padded(c_hh[k], False, False)]),
            ],
            axis=0,
        )

    side_cycle = cycle(2, cxl, stencil, cxh, cyl, cyh)

    cell_count = nx * ny
    flat_coarse = coarse.reshape(cell_count)
    slot_rank = jnp.cumsum(flat_coarse, dtype=jnp.int32) - flat_coarse
    chosen = (
        (slot_rank[None, :] == jnp.arange(CAP, dtype=jnp.int32)[:, None])
        & (flat_coarse[None, :] == 1)
    ).astype(jnp.int32)
    source = jnp.sum(
        chosen * jnp.arange(cell_count, dtype=jnp.int32)[None, :], axis=1, dtype=jnp.int32
    )
    filled = jnp.sum(chosen, axis=1, dtype=jnp.int32)
    span = ny + 2
    own_i = jnp.arange(nx, dtype=jnp.int32)[:, None] + 1
    own_j = jnp.arange(ny, dtype=jnp.int32)[None, :] + 1
    up_index = jnp.stack(
        [(own_i + 2 * stencil[:, :, 0] - 1) * span + own_j,
         own_i * span + own_j + 2 * stencil[:, :, 1] - 1],
        axis=-1,
    ).reshape(cell_count, 2)
    picked = jnp.take(up_index, source, axis=0, mode="clip")
    slot_table = jnp.concatenate([source[:, None], picked, filled[:, None]], axis=1).reshape(-1)
    buffers = (from_xlo, from_xhi, from_ylo, from_yhi, corners[(1, 1)], corners[(1, -1)],
               corners[(-1, 1)], corners[(-1, -1)])
    strong, restrict = local_compute(side_cycle.reshape(-1), slot_table, fine_own, lead_own,
                                     factor_own, minus_own, buffers)
    return (strong, restrict.reshape(CAP, 14, flat))


def solution(mesh):
    placed = (P("gx", "gy", None), P("gx", "gy", None, None), P("gx", "gy", None), P("gx", "gy"))
    return jax.shard_map(
        on_device,
        mesh=mesh,
        in_specs=placed,
        out_specs=(P("gx", "gy", None), P(("gx", "gy"), None, None)),
        check_vma=False,
    )
```
